32 devices in a mesh: groups: 1, wide: 32 (over z, y, x, core).
Axes of the slice: x: 2, y: 2, z: 4, core: 2. Of those that a mesh axis runs over, the one named last changes fastest.
Arguments:
- trial_bands: bfloat16 [1, 2, 3, 192, 192, 192], P('groups', None, None, 'wide'), may hold values from -160 to 160, as said below
- locked_bands: bfloat16 [4, 2, 3, 192, 192, 192], P('groups', None, None, 'wide'), may hold values from -240 to 240, as said below
- inv_diag: float32 [3, 192, 192, 192], P('groups', None, 'wide'), may hold values from 0.1 to 1
- inv_corr: float32 [3, 192, 192, 192], P('groups', None, 'wide'), may hold values from -0.3 to 0.3
Outputs:
- applied: bfloat16 [1, 2, 3, 192, 192, 192], P('groups', None, None, 'wide')
- rayleigh: float32 [2, 1, 1], P('groups')
The draws below stay inside these ranges and needn't reach their ends.
Inputs may be any that keep to these rules, and one draw needn't show every extreme that they name: `trial_bands`: sums of locked and independent fields, bounded. `locked_bands`: the locked bands are linearly independent.
All inputs are finite; a program needn't handle non-finite values.
Results may differ from the reference program's by a relative error of at most 0.0013.
Values sent between devices are 32-bit elements; how exact they have to be, the bound alone decides.
No kernel may reach another device: no remote copies, remote signals or barrier semaphores. Data moves between devices by JAX's collectives and lax.ppermute only.
A program may use at most 128 MiB of HBM per device.

```python
import math
import jax
import jax.numpy as jnp
from jax import lax

NG = 192
B = 1
K = 4


def signed_axis(length):
    indices = jnp.arange(length, dtype=jnp.int32)
    shifted = jnp.where(indices < length // 2, indices, indices - length)
    return shifted.astype(jnp.float32) / (length / 2.0)


def plane_fraction():
    indices = jnp.arange(NG, dtype=jnp.int32).astype(jnp.float32)
    return (indices / float(NG))[:, None, None]


def rise_profile():
    frac = plane_fraction()
    return 0.6 + 0.9 * frac


def fall_profile():
    frac = plane_fraction()
    return 2.0 - 1.6 * frac


def envelope_field():
    wave_axis = signed_axis(NG)
    radius = wave_axis[:, None, None] ** 2 + wave_axis[None, :, None] ** 2 + wave_axis[None, None, :] ** 2
    return 1.5 / (1.0 + radius)


def rough_field(key, length):
    return jnp.clip(jax.random.normal(key, (length, 2, 3, NG, NG, NG), jnp.float32), -6.0, 6.0)


def locked_base(key):
    noise_field = rough_field(jax.random.fold_in(key, 101), K)
    offdiag = jax.random.uniform(jax.random.fold_in(key, 102), (K, K), jnp.float32, -1.0, 1.0) * (0.75 / max(K - 1, 1))
    identity = jnp.eye(K, dtype=jnp.float32)
    mixing = identity + offdiag * (1.0 - identity)
    mixed = jnp.einsum('kj,jpcxyz->kpcxyz', mixing, noise_field, precision=lax.Precision.HIGHEST)
    return mixed * (envelope_field() * rise_profile())


def draw_locked_bands(key, part):
    base_field = locked_base(key)
    scales = jnp.exp(jax.random.uniform(jax.random.fold_in(key, 103), (K,), jnp.float32, 0.0, math.log(10.0)))
    return (base_field * scales[:, None, None, None, None, None]).astype(jnp.bfloat16)


def draw_trial_bands(key, part):
    base_field = locked_base(key)
    coeffs = jax.random.uniform(jax.random.fold_in(key, 104), (B, K), jnp.float32, -0.6, 0.6)
    own_part = rough_field(jax.random.fold_in(key, 105), B) * (envelope_field() * rise_profile())
    mixed = jnp.einsum('bk,kpcxyz->bpcxyz', coeffs, base_field, precision=lax.Precision.HIGHEST)
    return (mixed * fall_profile() + own_part).astype(jnp.bfloat16)


def block_levels(own_key, extent, split, smallest, high):
    factor_of, own = 1.0, jax.random.fold_in(own_key, 6)
    for axis_at, shards_of in split:
        draws = jnp.exp(jax.random.uniform(jax.random.fold_in(own, axis_at), (shards_of,), jnp.float32, smallest / len(split), high / len(split)))
        factor_of = factor_of * jnp.repeat(draws, extent[axis_at] // shards_of).reshape([-1 if axis == axis_at else 1 for axis in range(len(extent))])
    return factor_of


def setup_inputs(seed: int = 0, part: int = 0) -> dict:
    streams_of = jax.random.split(jax.random.key(seed), 5)
    part_splits = jax.random.split(jax.random.fold_in(streams_of[4], part), 5)
    return {
        "trial_bands": draw_trial_bands(jax.random.fold_in(jax.random.fold_in(streams_of[4], part), 71), part),
        "locked_bands": draw_locked_bands(jax.random.fold_in(jax.random.fold_in(streams_of[4], part), 71), part),
        "inv_diag": jnp.clip(jnp.exp(math.log(1.0) - 2.3025851 * jax.random.uniform(part_splits[2], (3, NG, NG, NG), jnp.float32) ** block_levels(part_splits[2], (3, NG, NG, NG), ((2, 32),), -0.2, 0.2)), 0.1, 1.0),
        "inv_corr": jnp.clip(jax.random.uniform(part_splits[3], (3, NG, NG, NG), jnp.float32, -0.3, 0.3) * block_levels(part_splits[3], (3, NG, NG, NG), ((2, 32),), -0.4, 0.0), -0.3, 0.3),
    }


highest = lax.Precision.HIGHEST

def signed_wave(length):
    indices = jnp.arange(length, dtype=jnp.int32)
    shifted = jnp.where(indices < length // 2, indices, indices - length)
    return shifted.astype(jnp.float32) / (length / 2.0)

def cross_wave(wave_x, wave_y, wave_z, vectors):
    comp_x = vectors[..., 0, :, :, :]
    comp_y = vectors[..., 1, :, :, :]
    comp_z = vectors[..., 2, :, :, :]
    along_x = wave_x[:, None, None]
    along_y = wave_y[None, :, None]
    along_z = wave_z[None, None, :]
    return jnp.stack([along_y * comp_z - along_z * comp_y, along_z * comp_x - along_x * comp_z, along_x * comp_y - along_y * comp_x], axis=-4)

def apply_tensor(vectors, inv_diag, inv_corr):
    coupling_xy = inv_corr[0] * jnp.sqrt(inv_diag[0] * inv_diag[1])
    coupling_xz = inv_corr[1] * jnp.sqrt(inv_diag[0] * inv_diag[2])
    coupling_yz = inv_corr[2] * jnp.sqrt(inv_diag[1] * inv_diag[2])
    comp_x = vectors[..., 0, :, :, :]
    comp_y = vectors[..., 1, :, :, :]
    comp_z = vectors[..., 2, :, :, :]
    out_x = inv_diag[0] * comp_x + coupling_xy * comp_y + coupling_xz * comp_z
    out_y = coupling_xy * comp_x + inv_diag[1] * comp_y + coupling_yz * comp_z
    out_z = coupling_xz * comp_x + coupling_yz * comp_y + inv_diag[2] * comp_z
    return jnp.stack([out_x, out_y, out_z], axis=-4)

def inner_sum(left_rows, right_rows):
    return jnp.einsum('an,bn->ab', left_rows.astype(jnp.float32), right_rows.astype(jnp.float32), preferred_element_type=jnp.float32)

def remove_locked(gram_sums, trial_re, trial_im, locked_re, locked_im):
    gram_a, gram_q, proj_re, proj_im = gram_sums
    kept_count = gram_a.shape[0]
    gram = jnp.concatenate([jnp.concatenate([gram_a, gram_q], axis=1), jnp.concatenate([gram_q.T, gram_a], axis=1)], axis=0)
    rhs_both = jnp.concatenate([proj_re, proj_im], axis=0)
    lower = jnp.linalg.cholesky(gram)
    middle = lax.linalg.triangular_solve(lower, rhs_both, left_side=True, lower=True)
    coef = lax.linalg.triangular_solve(lower, middle, left_side=True, lower=True, transpose_a=True)
    coef_one = coef[:kept_count]
    coef_two = coef[kept_count:]
    locked_re32 = locked_re.astype(jnp.float32)
    locked_im32 = locked_im.astype(jnp.float32)
    out_re = trial_re.astype(jnp.float32) - jnp.einsum('ab,an->bn', coef_one, locked_re32, precision=highest) + jnp.einsum('ab,an->bn', coef_two, locked_im32, precision=highest)
    out_im = trial_im.astype(jnp.float32) - jnp.einsum('ab,an->bn', coef_one, locked_im32, precision=highest) - jnp.einsum('ab,an->bn', coef_two, locked_re32, precision=highest)
    return (out_re, out_im)

def reference(trial_bands, locked_bands, inv_diag, inv_corr):
    band_count = trial_bands.shape[0]
    kept_count = locked_bands.shape[0]
    trial_re = trial_bands[:, 0].reshape(band_count, -1)
    trial_im = trial_bands[:, 1].reshape(band_count, -1)
    locked_re = locked_bands[:, 0].reshape(kept_count, -1)
    locked_im = locked_bands[:, 1].reshape(kept_count, -1)
    gram_a = inner_sum(locked_re, locked_re) + inner_sum(locked_im, locked_im)
    gram_q = inner_sum(locked_im, locked_re) - inner_sum(locked_re, locked_im)
    proj_re = inner_sum(locked_re, trial_re) + inner_sum(locked_im, trial_im)
    proj_im = inner_sum(locked_re, trial_im) - inner_sum(locked_im, trial_re)
    flat_re, flat_im = remove_locked((gram_a, gram_q, proj_re, proj_im), trial_re, trial_im, locked_re, locked_im)
    shape_one = (band_count, 3, NG, NG, NG)
    wave_axis = signed_wave(NG)

    def apply_band(inputs):
        part_re, part_im = inputs
        curled_re = -cross_wave(wave_axis, wave_axis, wave_axis, part_im)
        curled_im = cross_wave(wave_axis, wave_axis, wave_axis, part_re)
        spatial = jnp.fft.ifftn(lax.complex(curled_re, curled_im), axes=(1, 2, 3), norm='ortho')
        weighted_re = apply_tensor(jnp.real(spatial), inv_diag, inv_corr)
        weighted_im = apply_tensor(jnp.imag(spatial), inv_diag, inv_corr)
        spectral = jnp.fft.fftn(lax.complex(weighted_re, weighted_im), axes=(1, 2, 3), norm='ortho')
        spec_re = jnp.real(spectral)
        spec_im = jnp.imag(spectral)
        return (-cross_wave(wave_axis, wave_axis, wave_axis, spec_im), cross_wave(wave_axis, wave_axis, wave_axis, spec_re))
    applied_re, applied_im = lax.map(apply_band, (flat_re.reshape(shape_one), flat_im.reshape(shape_one)))
    applied = jnp.stack([applied_re, applied_im], axis=1).astype(jnp.bfloat16)
    rows_re = applied_re.reshape(band_count, -1)
    rows_im = applied_im.reshape(band_count, -1)
    scale_all = 1.0 / float(NG * NG * NG)
    rayleigh_re = (jnp.einsum('an,bn->ab', flat_re, rows_re, precision=highest) + jnp.einsum('an,bn->ab', flat_im, rows_im, precision=highest)) * scale_all
    rayleigh_im = (jnp.einsum('an,bn->ab', flat_re, rows_im, precision=highest) - jnp.einsum('an,bn->ab', flat_im, rows_re, precision=highest)) * scale_all
    return (applied, jnp.stack([rayleigh_re, rayleigh_im], axis=0))
```

```python
import math

import jax
import jax.numpy as jnp
from jax import lax
from jax.sharding import PartitionSpec as P

highest = lax.Precision.HIGHEST
three_pass = lax.Precision.HIGH


def signed_wave(indices, length):
    shifted = jnp.where(indices < length // 2, indices, indices - length)
    return shifted.astype(jnp.float32) / (length / 2.0)


def cross_wave(wave_x, wave_y, wave_z, vectors):
    comp_x = vectors[..., 0, :, :, :]
    comp_y = vectors[..., 1, :, :, :]
    comp_z = vectors[..., 2, :, :, :]
    along_x = wave_x[:, None, None]
    along_y = wave_y[None, :, None]
    along_z = wave_z[None, None, :]
    return jnp.stack(
        [
            along_y * comp_z - along_z * comp_y,
            along_z * comp_x - along_x * comp_z,
            along_x * comp_y - along_y * comp_x,
        ],
        axis=-4,
    )


def curl_times_i(waves, stacked):
    wave_x, wave_y, wave_z = waves
    return jnp.stack(
        [
            -cross_wave(wave_x, wave_y, wave_z, stacked[1]),
            cross_wave(wave_x, wave_y, wave_z, stacked[0]),
        ],
        axis=0,
    )


def apply_tensor(vectors, inv_diag, inv_corr):
    coupling_xy = inv_corr[0] * jnp.sqrt(inv_diag[0] * inv_diag[1])
    coupling_xz = inv_corr[1] * jnp.sqrt(inv_diag[0] * inv_diag[2])
    coupling_yz = inv_corr[2] * jnp.sqrt(inv_diag[1] * inv_diag[2])
    comp_x = vectors[..., 0, :, :, :]
    comp_y = vectors[..., 1, :, :, :]
    comp_z = vectors[..., 2, :, :, :]
    out_x = inv_diag[0] * comp_x + coupling_xy * comp_y + coupling_xz * comp_z
    out_y = coupling_xy * comp_x + inv_diag[1] * comp_y + coupling_yz * comp_z
    out_z = coupling_xz * comp_x + coupling_yz * comp_y + inv_diag[2] * comp_z
    return jnp.stack([out_x, out_y, out_z], axis=-4)


def complex_table(length, orient):
    indices = jnp.arange(length, dtype=jnp.int32)
    phases = indices[:, None] * indices[None, :] % length
    angles = phases.astype(jnp.float32) * (2.0 * math.pi / length)
    norm_factor = 1.0 / math.sqrt(length)
    cos_table = jnp.cos(angles) * norm_factor
    sin_table = jnp.sin(angles) * norm_factor * orient
    return jnp.stack(
        [jnp.stack([cos_table, sin_table], axis=0), jnp.stack([-sin_table, cos_table], axis=0)],
        axis=0,
    )


def transform(stacked, axis_dim, orient):
    table = complex_table(stacked.shape[axis_dim + 1], orient)
    if axis_dim == 2:
        return jnp.einsum("pbckyz,pqkn->qbcnyz", stacked, table, precision=three_pass)
    if axis_dim == 3:
        return jnp.einsum("pbcxkz,pqkn->qbcxnz", stacked, table, precision=three_pass)
    return jnp.einsum("pbcxyk,pqkn->qbcxyn", stacked, table, precision=three_pass)


def inner_sum(left_rows, right_rows):
    return jnp.einsum("an,bn->ab", left_rows, right_rows, preferred_element_type=jnp.float32)


def remove_locked(gram_sums, trial_re, trial_im, locked_re, locked_im):
    gram_a, gram_q, proj_re, proj_im = gram_sums
    kept_count = gram_a.shape[0]
    gram = jnp.concatenate(
        [jnp.concatenate([gram_a, gram_q], axis=1), jnp.concatenate([gram_q.T, gram_a], axis=1)],
        axis=0,
    )
    rhs_both = jnp.concatenate([proj_re, proj_im], axis=0)
    lower = jnp.linalg.cholesky(gram)
    middle = lax.linalg.triangular_solve(lower, rhs_both, left_side=True, lower=True)
    coef = lax.linalg.triangular_solve(lower, middle, left_side=True, lower=True, transpose_a=True)
    coef_one = coef[:kept_count]
    coef_two = coef[kept_count:]
    locked_re32 = locked_re.astype(jnp.float32)
    locked_im32 = locked_im.astype(jnp.float32)
    out_re = (
        trial_re.astype(jnp.float32)
        - jnp.einsum("ab,an->bn", coef_one, locked_re32, precision=highest)
        + jnp.einsum("ab,an->bn", coef_two, locked_im32, precision=highest)
    )
    out_im = (
        trial_im.astype(jnp.float32)
        - jnp.einsum("ab,an->bn", coef_one, locked_im32, precision=highest)
        - jnp.einsum("ab,an->bn", coef_two, locked_re32, precision=highest)
    )
    return (out_re, out_im)


def maxwell_pass(spectrum, waves, inv_diag, inv_corr, to_space_fn, to_spectrum_fn):
    curled = curl_times_i(waves, spectrum)
    curled = transform(curled, 4, 1.0)
    curled = transform(curled, 3, 1.0)
    moved = to_space_fn(curled)
    space = transform(moved, 2, 1.0)
    weighted = apply_tensor(space, inv_diag, inv_corr)
    front = transform(weighted, 2, -1.0)
    home = to_spectrum_fn(front)
    home = transform(home, 3, -1.0)
    home = transform(home, 4, -1.0)
    return (curl_times_i(waves, home), space, weighted)


def per_device(trial_bands, locked_bands, inv_diag, inv_corr):
    band_count = trial_bands.shape[0]
    kept_count = locked_bands.shape[0]
    local_x = trial_bands.shape[3]
    grid_len = trial_bands.shape[4]
    trial_re = trial_bands[:, 0].reshape(band_count, -1)
    trial_im = trial_bands[:, 1].reshape(band_count, -1)
    locked_re = locked_bands[:, 0].reshape(kept_count, -1)
    locked_im = locked_bands[:, 1].reshape(kept_count, -1)
    rows = jnp.concatenate(
        [locked_bands.reshape((2 * kept_count,) + locked_bands.shape[2:]),
         trial_bands.reshape((2 * band_count,) + trial_bands.shape[2:])],
        axis=0,
    )
    pairs = jnp.einsum("icxyz,jcxyz->ij", rows, rows, preferred_element_type=jnp.float32)
    pairs = lax.psum(pairs, "wide")
    lk = pairs[: 2 * kept_count, : 2 * kept_count].reshape(kept_count, 2, kept_count, 2)
    lt = pairs[: 2 * kept_count, 2 * kept_count :].reshape(kept_count, 2, band_count, 2)
    gram_a = lk[:, 0, :, 0] + lk[:, 1, :, 1]
    gram_q = lk[:, 1, :, 0] - lk[:, 0, :, 1]
    proj_re = lt[:, 0, :, 0] + lt[:, 1, :, 1]
    proj_im = lt[:, 0, :, 1] - lt[:, 1, :, 0]
    gram_sums = (gram_a, gram_q, proj_re, proj_im)
    flat_re, flat_im = remove_locked(gram_sums, trial_re, trial_im, locked_re, locked_im)
    shape_local = (band_count, 3, local_x, grid_len, grid_len)
    spectrum = jnp.stack([flat_re.reshape(shape_local), flat_im.reshape(shape_local)], axis=0)
    start_x = lax.axis_index("wide") * local_x
    full_axis = jnp.arange(grid_len, dtype=jnp.int32)
    wave_x = signed_wave(start_x + jnp.arange(local_x, dtype=jnp.int32), grid_len)
    wave_full = signed_wave(full_axis, grid_len)
    waves = (wave_x, wave_full, wave_full)

    def send_out_one(field):
        return lax.all_to_all(field, "wide", split_axis=4, concat_axis=3, tiled=True)

    def send_home_one(field):
        return lax.all_to_all(field, "wide", split_axis=3, concat_axis=4, tiled=True)

    results = [maxwell_pass(spectrum, waves, inv_diag, inv_corr, send_out_one, send_home_one)]
    applied_st, space, weighted = [
        jnp.concatenate([entry[slot] for entry in results], axis=1) for slot in range(3)
    ]
    applied = jnp.stack([applied_st[0], applied_st[1]], axis=1).astype(jnp.bfloat16)
    scale_all = 1.0 / float(grid_len * grid_len * grid_len)
    left_re = space[0].reshape(band_count, -1)
    left_im = space[1].reshape(band_count, -1)
    right_re = weighted[0].reshape(band_count, -1)
    right_im = weighted[1].reshape(band_count, -1)
    part_re = jnp.einsum("an,bn->ab", left_re, right_re, precision=highest) + jnp.einsum(
        "an,bn->ab", left_im, right_im, precision=highest
    )
    part_im = jnp.einsum("an,bn->ab", left_re, right_im, precision=highest) - jnp.einsum(
        "an,bn->ab", left_im, right_re, precision=highest
    )
    total_re, total_im = lax.psum((part_re, part_im), "wide")
    rayleigh = jnp.stack([total_re * scale_all, total_im * scale_all], axis=0)
    return (applied, rayleigh)


def solution(mesh):
    in_specs = (
        P("groups", None, None, "wide", None, None),
        P("groups", None, None, "wide", None, None),
        P("groups", None, "wide", None),
        P("groups", None, "wide", None),
    )
    out_specs = (P("groups", None, None, "wide", None, None), P("groups", None, None))
    return jax.shard_map(
        per_device, mesh=mesh, in_specs=in_specs, out_specs=out_specs, check_vma=False
    )
```

```python
import math

import ml_dtypes
import numpy as np

import jax
import jax.numpy as jnp
from jax import lax
from jax.sharding import PartitionSpec as P
from jax.experimental import pallas as pl
from jax.experimental.pallas import tpu as pltpu

highest = lax.Precision.HIGHEST
three_pass = lax.Precision.HIGH


def signed_wave(indices, length):
    shifted = jnp.where(indices < length // 2, indices, indices - length)
    return shifted.astype(jnp.float32) / (length / 2.0)


def cross_wave(wave_x, wave_y, wave_z, vectors):
    comp_x = vectors[..., 0, :, :, :]
    comp_y = vectors[..., 1, :, :, :]
    comp_z = vectors[..., 2, :, :, :]
    along_x = wave_x[:, None, None]
    along_y = wave_y[None, :, None]
    along_z = wave_z[None, None, :]
    return jnp.stack(
        [
            along_y * comp_z - along_z * comp_y,
            along_z * comp_x - along_x * comp_z,
            along_x * comp_y - along_y * comp_x,
        ],
        axis=-4,
    )


def curl_times_i(waves, stacked):
    wave_x, wave_y, wave_z = waves
    return jnp.stack(
        [
            -cross_wave(wave_x, wave_y, wave_z, stacked[1]),
            cross_wave(wave_x, wave_y, wave_z, stacked[0]),
        ],
        axis=0,
    )


def apply_tensor(vectors, inv_diag, inv_corr):
    coupling_xy = inv_corr[0] * jnp.sqrt(inv_diag[0] * inv_diag[1])
    coupling_xz = inv_corr[1] * jnp.sqrt(inv_diag[0] * inv_diag[2])
    coupling_yz = inv_corr[2] * jnp.sqrt(inv_diag[1] * inv_diag[2])
    comp_x = vectors[..., 0, :, :, :]
    comp_y = vectors[..., 1, :, :, :]
    comp_z = vectors[..., 2, :, :, :]
    out_x = inv_diag[0] * comp_x + coupling_xy * comp_y + coupling_xz * comp_z
    out_y = coupling_xy * comp_x + inv_diag[1] * comp_y + coupling_yz * comp_z
    out_z = coupling_xz * comp_x + coupling_yz * comp_y + inv_diag[2] * comp_z
    return jnp.stack([out_x, out_y, out_z], axis=-4)


def complex_table(length, orient):
    indices = jnp.arange(length, dtype=jnp.int32)
    phases = indices[:, None] * indices[None, :] % length
    angles = phases.astype(jnp.float32) * (2.0 * math.pi / length)
    norm_factor = 1.0 / math.sqrt(length)
    cos_table = jnp.cos(angles) * norm_factor
    sin_table = jnp.sin(angles) * norm_factor * orient
    return jnp.stack(
        [jnp.stack([cos_table, sin_table], axis=0), jnp.stack([-sin_table, cos_table], axis=0)],
        axis=0,
    )


def transform(stacked, axis_dim, orient):
    table = complex_table(stacked.shape[axis_dim + 1], orient)
    if axis_dim == 2:
        return jnp.einsum("pbckyz,pqkn->qbcnyz", stacked, table, precision=three_pass)
    if axis_dim == 3:
        return jnp.einsum("pbcxkz,pqkn->qbcxnz", stacked, table, precision=three_pass)
    return jnp.einsum("pbcxyk,pqkn->qbcxyn", stacked, table, precision=three_pass)


def split_hi_lo(values):
    scaled = values * 65537.0
    top = scaled - (scaled - values)
    return top.astype(jnp.bfloat16), (values - top).astype(jnp.bfloat16)


def dot_right(values, table_hi, table_lo):
    high, low = split_hi_lo(values)
    f32 = jnp.float32
    return (
        jnp.dot(high, table_hi, preferred_element_type=f32)
        + jnp.dot(low, table_hi, preferred_element_type=f32)
        + jnp.dot(high, table_lo, preferred_element_type=f32)
    )


def dot_left(table_hi, table_lo, values):
    high, low = split_hi_lo(values)
    f32 = jnp.float32
    return (
        jnp.dot(table_hi, high, preferred_element_type=f32)
        + jnp.dot(table_hi, low, preferred_element_type=f32)
        + jnp.dot(table_lo, high, preferred_element_type=f32)
    )


def front_kernel(coef_ref, qx_ref, trial_ref, locked_ref, chi_ref, clo_ref, shi_ref, slo_ref, out_ref):
    band = pl.program_id(0)
    plane = pl.program_id(1)
    kept = locked_ref.shape[0]
    size = trial_ref.shape[-1]
    f32 = jnp.float32
    first = [coef_ref[band, k] for k in range(kept)]
    second = [coef_ref[band, kept + k] for k in range(kept)]
    part_re = []
    part_im = []
    for comp in range(3):
        acc_re = trial_ref[0, 0, comp, 0].astype(f32)
        acc_im = trial_ref[0, 1, comp, 0].astype(f32)
        for k in range(kept):
            l_re = locked_ref[k, 0, comp, 0].astype(f32)
            l_im = locked_ref[k, 1, comp, 0].astype(f32)
            acc_re = acc_re - first[k] * l_re + second[k] * l_im
            acc_im = acc_im - first[k] * l_im - second[k] * l_re
        part_re.append(acc_re)
        part_im.append(acc_im)
    rows = lax.broadcasted_iota(jnp.int32, (size, 1), 0)
    cols = lax.broadcasted_iota(jnp.int32, (1, size), 1)
    half = size // 2
    wave_y = jnp.where(rows < half, rows, rows - size).astype(f32) / (size / 2.0)
    wave_z = jnp.where(cols < half, cols, cols - size).astype(f32) / (size / 2.0)
    waves = (qx_ref[plane], wave_y, wave_z)
    c_hi = chi_ref[...]
    c_lo = clo_ref[...]
    s_hi = shi_ref[...]
    s_lo = slo_ref[...]
    for comp in range(3):
        a = (comp + 1) % 3
        b = (comp + 2) % 3
        cur_re = -(waves[a] * part_im[b] - waves[b] * part_im[a])
        cur_im = waves[a] * part_re[b] - waves[b] * part_re[a]
        z_re = dot_right(cur_re, c_hi, c_lo) - dot_right(cur_im, s_hi, s_lo)
        z_im = dot_right(cur_re, s_hi, s_lo) + dot_right(cur_im, c_hi, c_lo)
        y_re = dot_left(c_hi, c_lo, z_re) - dot_left(s_hi, s_lo, z_im)
        y_im = dot_left(s_hi, s_lo, z_re) + dot_left(c_hi, c_lo, z_im)
        out_ref[0, 0, comp, 0] = y_re
        out_ref[1, 0, comp, 0] = y_im


def numpy_split(table):
    full = table.astype(np.float32)
    high = full.astype(ml_dtypes.bfloat16)
    low = (full - high.astype(np.float32)).astype(ml_dtypes.bfloat16)
    return jnp.asarray(high), jnp.asarray(low)


def dft_tables(length, orient):
    indices = np.arange(length, dtype=np.int64)
    phases = indices[:, None] * indices[None, :] % length
    angles = phases.astype(np.float64) * (2.0 * math.pi / length)
    norm_factor = 1.0 / math.sqrt(length)
    c_hi, c_lo = numpy_split(np.cos(angles) * norm_factor)
    s_hi, s_lo = numpy_split(np.sin(angles) * norm_factor * orient)
    return c_hi, c_lo, s_hi, s_lo


def front_pass(coef_rows, wave_x, trial_bands, locked_bands):
    band_count, _, _, local_x, size, _ = trial_bands.shape
    kept = locked_bands.shape[0]
    tables = dft_tables(size, 1.0)
    smem = pl.BlockSpec(memory_space=pltpu.SMEM)
    table_spec = pl.BlockSpec((size, size), lambda b, x: (0, 0))
    return pl.pallas_call(
        front_kernel,
        grid=(band_count, local_x),
        in_specs=[
            smem,
            smem,
            pl.BlockSpec((1, 2, 3, 1, size, size), lambda b, x: (b, 0, 0, x, 0, 0)),
            pl.BlockSpec((kept, 2, 3, 1, size, size), lambda b, x: (0, 0, 0, x, 0, 0)),
            table_spec,
            table_spec,
            table_spec,
            table_spec,
        ],
        out_specs=pl.BlockSpec((2, 1, 3, 1, size, size), lambda b, x: (0, b, 0, x, 0, 0)),
        out_shape=jax.ShapeDtypeStruct((2, band_count, 3, local_x, size, size), jnp.float32),
    )(coef_rows, wave_x, trial_bands, locked_bands, *tables)


def inner_sum(left_rows, right_rows):
    return jnp.einsum("an,bn->ab", left_rows, right_rows, preferred_element_type=jnp.float32)


def remove_locked(gram_sums, trial_re, trial_im, locked_re, locked_im):
    gram_a, gram_q, proj_re, proj_im = gram_sums
    kept_count = gram_a.shape[0]
    gram = jnp.concatenate(
        [jnp.concatenate([gram_a, gram_q], axis=1), jnp.concatenate([gram_q.T, gram_a], axis=1)],
        axis=0,
    )
    rhs_both = jnp.concatenate([proj_re, proj_im], axis=0)
    lower = jnp.linalg.cholesky(gram)
    middle = lax.linalg.triangular_solve(lower, rhs_both, left_side=True, lower=True)
    coef = lax.linalg.triangular_solve(lower, middle, left_side=True, lower=True, transpose_a=True)
    coef_one = coef[:kept_count]
    coef_two = coef[kept_count:]
    locked_re32 = locked_re.astype(jnp.float32)
    locked_im32 = locked_im.astype(jnp.float32)
    out_re = (
        trial_re.astype(jnp.float32)
        - jnp.einsum("ab,an->bn", coef_one, locked_re32, precision=highest)
        + jnp.einsum("ab,an->bn", coef_two, locked_im32, precision=highest)
    )
    out_im = (
        trial_im.astype(jnp.float32)
        - jnp.einsum("ab,an->bn", coef_one, locked_im32, precision=highest)
        - jnp.einsum("ab,an->bn", coef_two, locked_re32, precision=highest)
    )
    return (out_re, out_im)


def solve_coef(gram_sums):
    gram_a, gram_q, proj_re, proj_im = gram_sums
    gram = jnp.concatenate(
        [jnp.concatenate([gram_a, gram_q], axis=1), jnp.concatenate([gram_q.T, gram_a], axis=1)],
        axis=0,
    )
    rhs_both = jnp.concatenate([proj_re, proj_im], axis=0)
    lower = jnp.linalg.cholesky(gram)
    middle = lax.linalg.triangular_solve(lower, rhs_both, left_side=True, lower=True)
    return lax.linalg.triangular_solve(lower, middle, left_side=True, lower=True, transpose_a=True)


def maxwell_pass(curled, waves, inv_diag, inv_corr, to_space_fn, to_spectrum_fn):
    moved = to_space_fn(curled)
    space = transform(moved, 2, 1.0)
    weighted = apply_tensor(space, inv_diag, inv_corr)
    front = transform(weighted, 2, -1.0)
    home = to_spectrum_fn(front)
    home = transform(home, 3, -1.0)
    home = transform(home, 4, -1.0)
    return (curl_times_i(waves, home), space, weighted)


def per_device(trial_bands, locked_bands, inv_diag, inv_corr):
    band_count = trial_bands.shape[0]
    kept_count = locked_bands.shape[0]
    local_x = trial_bands.shape[3]
    grid_len = trial_bands.shape[4]
    rows = jnp.concatenate(
        [locked_bands.reshape((2 * kept_count,) + locked_bands.shape[2:]),
         trial_bands.reshape((2 * band_count,) + trial_bands.shape[2:])],
        axis=0,
    )
    pairs = jnp.einsum("icxyz,jcxyz->ij", rows, rows, preferred_element_type=jnp.float32)
    pairs = lax.psum(pairs, "wide")
    lk = pairs[: 2 * kept_count, : 2 * kept_count].reshape(kept_count, 2, kept_count, 2)
    lt = pairs[: 2 * kept_count, 2 * kept_count :].reshape(kept_count, 2, band_count, 2)
    gram_a = lk[:, 0, :, 0] + lk[:, 1, :, 1]
    gram_q = lk[:, 1, :, 0] - lk[:, 0, :, 1]
    proj_re = lt[:, 0, :, 0] + lt[:, 1, :, 1]
    proj_im = lt[:, 0, :, 1] - lt[:, 1, :, 0]
    gram_sums = (gram_a, gram_q, proj_re, proj_im)
    coef = solve_coef(gram_sums)
    start_x = lax.axis_index("wide") * local_x
    full_axis = jnp.arange(grid_len, dtype=jnp.int32)
    wave_x = signed_wave(start_x + jnp.arange(local_x, dtype=jnp.int32), grid_len)
    wave_full = signed_wave(full_axis, grid_len)
    waves = (wave_x, wave_full, wave_full)

    def send_out_one(field):
        return lax.all_to_all(field, "wide", split_axis=4, concat_axis=3, tiled=True)

    def send_home_one(field):
        return lax.all_to_all(field, "wide", split_axis=3, concat_axis=4, tiled=True)

    curled = front_pass(coef.T, wave_x, trial_bands, locked_bands)
    results = [maxwell_pass(curled, waves, inv_diag, inv_corr, send_out_one, send_home_one)]
    applied_st, space, weighted = [
        jnp.concatenate([entry[slot] for entry in results], axis=1) for slot in range(3)
    ]
    applied = jnp.stack([applied_st[0], applied_st[1]], axis=1).astype(jnp.bfloat16)
    scale_all = 1.0 / float(grid_len * grid_len * grid_len)
    left_re = space[0].reshape(band_count, -1)
    left_im = space[1].reshape(band_count, -1)
    right_re = weighted[0].reshape(band_count, -1)
    right_im = weighted[1].reshape(band_count, -1)
    part_re = jnp.einsum("an,bn->ab", left_re, right_re, precision=highest) + jnp.einsum(
        "an,bn->ab", left_im, right_im, precision=highest
    )
    part_im = jnp.einsum("an,bn->ab", left_re, right_im, precision=highest) - jnp.einsum(
        "an,bn->ab", left_im, right_re, precision=highest
    )
    total_re, total_im = lax.psum((part_re, part_im), "wide")
    rayleigh = jnp.stack([total_re * scale_all, total_im * scale_all], axis=0)
    return (applied, rayleigh)


def solution(mesh):
    in_specs = (
        P("groups", None, None, "wide", None, None),
        P("groups", None, None, "wide", None, None),
        P("groups", None, "wide", None),
        P("groups", None, "wide", None),
    )
    out_specs = (P("groups", None, None, "wide", None, None), P("groups", None, None))
    return jax.shard_map(
        per_device, mesh=mesh, in_specs=in_specs, out_specs=out_specs, check_vma=False
    )
```

```python
import functools
import math

import ml_dtypes
import numpy as np

import jax
import jax.numpy as jnp
from jax import lax
from jax.sharding import PartitionSpec as P
from jax.experimental import pallas as pl
from jax.experimental.pallas import tpu as pltpu

highest = lax.Precision.HIGHEST
three_pass = lax.Precision.HIGH


def signed_wave(indices, length):
    shifted = jnp.where(indices < length // 2, indices, indices - length)
    return shifted.astype(jnp.float32) / (length / 2.0)


def cross_wave(wave_x, wave_y, wave_z, vectors):
    comp_x = vectors[..., 0, :, :, :]
    comp_y = vectors[..., 1, :, :, :]
    comp_z = vectors[..., 2, :, :, :]
    along_x = wave_x[:, None, None]
    along_y = wave_y[None, :, None]
    along_z = wave_z[None, None, :]
    return jnp.stack(
        [
            along_y * comp_z - along_z * comp_y,
            along_z * comp_x - along_x * comp_z,
            along_x * comp_y - along_y * comp_x,
        ],
        axis=-4,
    )


def curl_times_i(waves, stacked):
    wave_x, wave_y, wave_z = waves
    return jnp.stack(
        [
            -cross_wave(wave_x, wave_y, wave_z, stacked[1]),
            cross_wave(wave_x, wave_y, wave_z, stacked[0]),
        ],
        axis=0,
    )


def apply_tensor(vectors, inv_diag, inv_corr):
    coupling_xy = inv_corr[0] * jnp.sqrt(inv_diag[0] * inv_diag[1])
    coupling_xz = inv_corr[1] * jnp.sqrt(inv_diag[0] * inv_diag[2])
    coupling_yz = inv_corr[2] * jnp.sqrt(inv_diag[1] * inv_diag[2])
    comp_x = vectors[..., 0, :, :, :]
    comp_y = vectors[..., 1, :, :, :]
    comp_z = vectors[..., 2, :, :, :]
    out_x = inv_diag[0] * comp_x + coupling_xy * comp_y + coupling_xz * comp_z
    out_y = coupling_xy * comp_x + inv_diag[1] * comp_y + coupling_yz * comp_z
    out_z = coupling_xz * comp_x + coupling_yz * comp_y + inv_diag[2] * comp_z
    return jnp.stack([out_x, out_y, out_z], axis=-4)


def complex_table(length, orient):
    indices = jnp.arange(length, dtype=jnp.int32)
    phases = indices[:, None] * indices[None, :] % length
    angles = phases.astype(jnp.float32) * (2.0 * math.pi / length)
    norm_factor = 1.0 / math.sqrt(length)
    cos_table = jnp.cos(angles) * norm_factor
    sin_table = jnp.sin(angles) * norm_factor * orient
    return jnp.stack(
        [jnp.stack([cos_table, sin_table], axis=0), jnp.stack([-sin_table, cos_table], axis=0)],
        axis=0,
    )


def transform(stacked, axis_dim, orient):
    table = complex_table(stacked.shape[axis_dim + 1], orient)
    if axis_dim == 2:
        return jnp.einsum("pbckyz,pqkn->qbcnyz", stacked, table, precision=three_pass)
    if axis_dim == 3:
        return jnp.einsum("pbcxkz,pqkn->qbcxnz", stacked, table, precision=three_pass)
    return jnp.einsum("pbcxyk,pqkn->qbcxyn", stacked, table, precision=three_pass)


def split_hi_lo(values):
    scaled = values * 65537.0
    top = scaled - (scaled - values)
    return top.astype(jnp.bfloat16), (values - top).astype(jnp.bfloat16)


def dot_right(values, table_hi, table_lo):
    high, low = split_hi_lo(values)
    f32 = jnp.float32
    return (
        jnp.dot(high, table_hi, preferred_element_type=f32)
        + jnp.dot(low, table_hi, preferred_element_type=f32)
        + jnp.dot(high, table_lo, preferred_element_type=f32)
    )


def dot_left(table_hi, table_lo, values):
    high, low = split_hi_lo(values)
    f32 = jnp.float32
    return (
        jnp.dot(table_hi, high, preferred_element_type=f32)
        + jnp.dot(table_hi, low, preferred_element_type=f32)
        + jnp.dot(table_lo, high, preferred_element_type=f32)
    )


def front_kernel(coef_ref, qx_ref, trial_ref, locked_ref, chi_ref, clo_ref, shi_ref, slo_ref, out_ref):
    band = pl.program_id(0)
    plane = pl.program_id(1)
    kept = locked_ref.shape[0]
    size = trial_ref.shape[-1]
    f32 = jnp.float32
    first = [coef_ref[band, k] for k in range(kept)]
    second = [coef_ref[band, kept + k] for k in range(kept)]
    part_re = []
    part_im = []
    for comp in range(3):
        acc_re = trial_ref[0, 0, comp, 0].astype(f32)
        acc_im = trial_ref[0, 1, comp, 0].astype(f32)
        for k in range(kept):
            l_re = locked_ref[k, 0, comp, 0].astype(f32)
            l_im = locked_ref[k, 1, comp, 0].astype(f32)
            acc_re = acc_re - first[k] * l_re + second[k] * l_im
            acc_im = acc_im - first[k] * l_im - second[k] * l_re
        part_re.append(acc_re)
        part_im.append(acc_im)
    rows = lax.broadcasted_iota(jnp.int32, (size, 1), 0)
    cols = lax.broadcasted_iota(jnp.int32, (1, size), 1)
    half = size // 2
    wave_y = jnp.where(rows < half, rows, rows - size).astype(f32) / (size / 2.0)
    wave_z = jnp.where(cols < half, cols, cols - size).astype(f32) / (size / 2.0)
    waves = (qx_ref[plane], wave_y, wave_z)
    c_hi = chi_ref[...]
    c_lo = clo_ref[...]
    s_hi = shi_ref[...]
    s_lo = slo_ref[...]
    for comp in range(3):
        a = (comp + 1) % 3
        b = (comp + 2) % 3
        cur_re = -(waves[a] * part_im[b] - waves[b] * part_im[a])
        cur_im = waves[a] * part_re[b] - waves[b] * part_re[a]
        z_re = dot_right(cur_re, c_hi, c_lo) - dot_right(cur_im, s_hi, s_lo)
        z_im = dot_right(cur_re, s_hi, s_lo) + dot_right(cur_im, c_hi, c_lo)
        y_re = dot_left(c_hi, c_lo, z_re) - dot_left(s_hi, s_lo, z_im)
        y_im = dot_left(s_hi, s_lo, z_re) + dot_left(c_hi, c_lo, z_im)
        out_ref[0, 0, comp, 0] = y_re
        out_ref[1, 0, comp, 0] = y_im


def numpy_split(table):
    full = table.astype(np.float32)
    high = full.astype(ml_dtypes.bfloat16)
    low = (full - high.astype(np.float32)).astype(ml_dtypes.bfloat16)
    return jnp.asarray(high), jnp.asarray(low)


def dft_tables(length, orient):
    indices = np.arange(length, dtype=np.int64)
    phases = indices[:, None] * indices[None, :] % length
    angles = phases.astype(np.float64) * (2.0 * math.pi / length)
    norm_factor = 1.0 / math.sqrt(length)
    c_hi, c_lo = numpy_split(np.cos(angles) * norm_factor)
    s_hi, s_lo = numpy_split(np.sin(angles) * norm_factor * orient)
    return c_hi, c_lo, s_hi, s_lo


def front_pass(coef_rows, wave_x, trial_bands, locked_bands):
    band_count, _, _, local_x, size, _ = trial_bands.shape
    kept = locked_bands.shape[0]
    tables = dft_tables(size, 1.0)
    smem = pl.BlockSpec(memory_space=pltpu.SMEM)
    table_spec = pl.BlockSpec((size, size), lambda b, x: (0, 0))
    return pl.pallas_call(
        front_kernel,
        grid=(band_count, local_x),
        in_specs=[
            smem,
            smem,
            pl.BlockSpec((1, 2, 3, 1, size, size), lambda b, x: (b, 0, 0, x, 0, 0)),
            pl.BlockSpec((kept, 2, 3, 1, size, size), lambda b, x: (0, 0, 0, x, 0, 0)),
            table_spec,
            table_spec,
            table_spec,
            table_spec,
        ],
        out_specs=pl.BlockSpec((2, 1, 3, 1, size, size), lambda b, x: (0, b, 0, x, 0, 0)),
        out_shape=jax.ShapeDtypeStruct((2, band_count, 3, local_x, size, size), jnp.float32),
    )(coef_rows, wave_x, trial_bands, locked_bands, *tables)


def butterfly_sum(values, axis, count):
    if count & (count - 1):
        return lax.psum(values, axis)
    step = 1
    while step < count:
        pairs = [(index, index ^ step) for index in range(count)]
        values = values + lax.ppermute(values, axis, pairs)
        step *= 2
    return values


def inner_sum(left_rows, right_rows):
    return jnp.einsum("an,bn->ab", left_rows, right_rows, preferred_element_type=jnp.float32)


def remove_locked(gram_sums, trial_re, trial_im, locked_re, locked_im):
    gram_a, gram_q, proj_re, proj_im = gram_sums
    kept_count = gram_a.shape[0]
    gram = jnp.concatenate(
        [jnp.concatenate([gram_a, gram_q], axis=1), jnp.concatenate([gram_q.T, gram_a], axis=1)],
        axis=0,
    )
    rhs_both = jnp.concatenate([proj_re, proj_im], axis=0)
    lower = jnp.linalg.cholesky(gram)
    middle = lax.linalg.triangular_solve(lower, rhs_both, left_side=True, lower=True)
    coef = lax.linalg.triangular_solve(lower, middle, left_side=True, lower=True, transpose_a=True)
    coef_one = coef[:kept_count]
    coef_two = coef[kept_count:]
    locked_re32 = locked_re.astype(jnp.float32)
    locked_im32 = locked_im.astype(jnp.float32)
    out_re = (
        trial_re.astype(jnp.float32)
        - jnp.einsum("ab,an->bn", coef_one, locked_re32, precision=highest)
        + jnp.einsum("ab,an->bn", coef_two, locked_im32, precision=highest)
    )
    out_im = (
        trial_im.astype(jnp.float32)
        - jnp.einsum("ab,an->bn", coef_one, locked_im32, precision=highest)
        - jnp.einsum("ab,an->bn", coef_two, locked_re32, precision=highest)
    )
    return (out_re, out_im)


def solve_coef(gram_sums):
    gram_a, gram_q, proj_re, proj_im = gram_sums
    gram = jnp.concatenate(
        [jnp.concatenate([gram_a, gram_q], axis=1), jnp.concatenate([gram_q.T, gram_a], axis=1)],
        axis=0,
    )
    rhs_both = jnp.concatenate([proj_re, proj_im], axis=0)
    lower = jnp.linalg.cholesky(gram)
    middle = lax.linalg.triangular_solve(lower, rhs_both, left_side=True, lower=True)
    return lax.linalg.triangular_solve(lower, middle, left_side=True, lower=True, transpose_a=True)


def maxwell_pass(curled, waves, inv_diag, inv_corr, to_space_fn, to_spectrum_fn):
    moved = to_space_fn(curled)
    space = transform(moved, 2, 1.0)
    weighted = apply_tensor(space, inv_diag, inv_corr)
    front = transform(weighted, 2, -1.0)
    home = to_spectrum_fn(front)
    home = transform(home, 3, -1.0)
    home = transform(home, 4, -1.0)
    return (curl_times_i(waves, home), space, weighted)


def per_device(wide_count, trial_bands, locked_bands, inv_diag, inv_corr):
    band_count = trial_bands.shape[0]
    kept_count = locked_bands.shape[0]
    local_x = trial_bands.shape[3]
    grid_len = trial_bands.shape[4]
    rows = jnp.concatenate(
        [locked_bands.reshape((2 * kept_count,) + locked_bands.shape[2:]),
         trial_bands.reshape((2 * band_count,) + trial_bands.shape[2:])],
        axis=0,
    )
    pairs = jnp.einsum("icxyz,jcxyz->ij", rows, rows, preferred_element_type=jnp.float32)
    pairs = butterfly_sum(pairs, "wide", wide_count)
    lk = pairs[: 2 * kept_count, : 2 * kept_count].reshape(kept_count, 2, kept_count, 2)
    lt = pairs[: 2 * kept_count, 2 * kept_count :].reshape(kept_count, 2, band_count, 2)
    gram_a = lk[:, 0, :, 0] + lk[:, 1, :, 1]
    gram_q = lk[:, 1, :, 0] - lk[:, 0, :, 1]
    proj_re = lt[:, 0, :, 0] + lt[:, 1, :, 1]
    proj_im = lt[:, 0, :, 1] - lt[:, 1, :, 0]
    gram_sums = (gram_a, gram_q, proj_re, proj_im)
    coef = solve_coef(gram_sums)
    start_x = lax.axis_index("wide") * local_x
    full_axis = jnp.arange(grid_len, dtype=jnp.int32)
    wave_x = signed_wave(start_x + jnp.arange(local_x, dtype=jnp.int32), grid_len)
    wave_full = signed_wave(full_axis, grid_len)
    waves = (wave_x, wave_full, wave_full)

    def send_out_one(field):
        return lax.all_to_all(field, "wide", split_axis=4, concat_axis=3, tiled=True)

    def send_home_one(field):
        return lax.all_to_all(field, "wide", split_axis=3, concat_axis=4, tiled=True)

    curled = front_pass(coef.T, wave_x, trial_bands, locked_bands)
    results = [maxwell_pass(curled, waves, inv_diag, inv_corr, send_out_one, send_home_one)]
    applied_st, space, weighted = [
        jnp.concatenate([entry[slot] for entry in results], axis=1) for slot in range(3)
    ]
    applied = jnp.stack([applied_st[0], applied_st[1]], axis=1).astype(jnp.bfloat16)
    scale_all = 1.0 / float(grid_len * grid_len * grid_len)
    left_re = space[0].reshape(band_count, -1)
    left_im = space[1].reshape(band_count, -1)
    right_re = weighted[0].reshape(band_count, -1)
    right_im = weighted[1].reshape(band_count, -1)
    part_re = jnp.einsum("an,bn->ab", left_re, right_re, precision=highest) + jnp.einsum(
        "an,bn->ab", left_im, right_im, precision=highest
    )
    part_im = jnp.einsum("an,bn->ab", left_re, right_im, precision=highest) - jnp.einsum(
        "an,bn->ab", left_im, right_re, precision=highest
    )
    total_re, total_im = lax.psum((part_re, part_im), "wide")
    rayleigh = jnp.stack([total_re * scale_all, total_im * scale_all], axis=0)
    return (applied, rayleigh)


def solution(mesh):
    in_specs = (
        P("groups", None, None, "wide", None, None),
        P("groups", None, None, "wide", None, None),
        P("groups", None, "wide", None),
        P("groups", None, "wide", None),
    )
    out_specs = (P("groups", None, None, "wide", None, None), P("groups", None, None))
    wide_count = mesh.shape["wide"]
    return jax.shard_map(
        functools.partial(per_device, wide_count), mesh=mesh, in_specs=in_specs, out_specs=out_specs, check_vma=False
    )
```

```python
import functools
import math

import ml_dtypes
import numpy as np

import jax
import jax.numpy as jnp
from jax import lax
from jax.sharding import PartitionSpec as P
from jax.experimental import pallas as pl
from jax.experimental.pallas import tpu as pltpu

highest = lax.Precision.HIGHEST
three_pass = lax.Precision.HIGH


def signed_wave(indices, length):
    shifted = jnp.where(indices < length // 2, indices, indices - length)
    return shifted.astype(jnp.float32) / (length / 2.0)


def cross_wave(wave_x, wave_y, wave_z, vectors):
    comp_x = vectors[..., 0, :, :, :]
    comp_y = vectors[..., 1, :, :, :]
    comp_z = vectors[..., 2, :, :, :]
    along_x = wave_x[:, None, None]
    along_y = wave_y[None, :, None]
    along_z = wave_z[None, None, :]
    return jnp.stack(
        [
            along_y * comp_z - along_z * comp_y,
            along_z * comp_x - along_x * comp_z,
            along_x * comp_y - along_y * comp_x,
        ],
        axis=-4,
    )


def curl_times_i(waves, stacked):
    wave_x, wave_y, wave_z = waves
    return jnp.stack(
        [
            -cross_wave(wave_x, wave_y, wave_z, stacked[1]),
            cross_wave(wave_x, wave_y, wave_z, stacked[0]),
        ],
        axis=0,
    )


def apply_tensor(vectors, inv_diag, inv_corr):
    coupling_xy = inv_corr[0] * jnp.sqrt(inv_diag[0] * inv_diag[1])
    coupling_xz = inv_corr[1] * jnp.sqrt(inv_diag[0] * inv_diag[2])
    coupling_yz = inv_corr[2] * jnp.sqrt(inv_diag[1] * inv_diag[2])
    comp_x = vectors[..., 0, :, :, :]
    comp_y = vectors[..., 1, :, :, :]
    comp_z = vectors[..., 2, :, :, :]
    out_x = inv_diag[0] * comp_x + coupling_xy * comp_y + coupling_xz * comp_z
    out_y = coupling_xy * comp_x + inv_diag[1] * comp_y + coupling_yz * comp_z
    out_z = coupling_xz * comp_x + coupling_yz * comp_y + inv_diag[2] * comp_z
    return jnp.stack([out_x, out_y, out_z], axis=-4)


def complex_table(length, orient):
    indices = jnp.arange(length, dtype=jnp.int32)
    phases = indices[:, None] * indices[None, :] % length
    angles = phases.astype(jnp.float32) * (2.0 * math.pi / length)
    norm_factor = 1.0 / math.sqrt(length)
    cos_table = jnp.cos(angles) * norm_factor
    sin_table = jnp.sin(angles) * norm_factor * orient
    return jnp.stack(
        [jnp.stack([cos_table, sin_table], axis=0), jnp.stack([-sin_table, cos_table], axis=0)],
        axis=0,
    )


def transform(stacked, axis_dim, orient):
    table = complex_table(stacked.shape[axis_dim + 1], orient)
    if axis_dim == 2:
        return jnp.einsum("pbckyz,pqkn->qbcnyz", stacked, table, precision=three_pass)
    if axis_dim == 3:
        return jnp.einsum("pbcxkz,pqkn->qbcxnz", stacked, table, precision=three_pass)
    return jnp.einsum("pbcxyk,pqkn->qbcxyn", stacked, table, precision=three_pass)


def split_hi_lo(values):
    scaled = values * 65537.0
    top = scaled - (scaled - values)
    return top.astype(jnp.bfloat16), (values - top).astype(jnp.bfloat16)


def dot_right(values, table_hi, table_lo):
    high, low = split_hi_lo(values)
    f32 = jnp.float32
    return (
        jnp.dot(high, table_hi, preferred_element_type=f32)
        + jnp.dot(low, table_hi, preferred_element_type=f32)
        + jnp.dot(high, table_lo, preferred_element_type=f32)
    )


def dot_left(table_hi, table_lo, values):
    high, low = split_hi_lo(values)
    f32 = jnp.float32
    return (
        jnp.dot(table_hi, high, preferred_element_type=f32)
        + jnp.dot(table_hi, low, preferred_element_type=f32)
        + jnp.dot(table_lo, high, preferred_element_type=f32)
    )


def front_kernel(comps, coef_ref, qx_ref, trial_ref, locked_ref, chi_ref, clo_ref, shi_ref, slo_ref, out_ref):
    band = pl.program_id(0)
    plane = pl.program_id(1)
    kept = locked_ref.shape[0]
    size = trial_ref.shape[-1]
    f32 = jnp.float32
    first = [coef_ref[band, k] for k in range(kept)]
    second = [coef_ref[band, kept + k] for k in range(kept)]
    needed = sorted({(c + 1) % 3 for c in comps} | {(c + 2) % 3 for c in comps})
    part_re = {}
    part_im = {}
    for comp in needed:
        acc_re = trial_ref[0, 0, comp, 0].astype(f32)
        acc_im = trial_ref[0, 1, comp, 0].astype(f32)
        for k in range(kept):
            l_re = locked_ref[k, 0, comp, 0].astype(f32)
            l_im = locked_ref[k, 1, comp, 0].astype(f32)
            acc_re = acc_re - first[k] * l_re + second[k] * l_im
            acc_im = acc_im - first[k] * l_im - second[k] * l_re
        part_re[comp] = acc_re
        part_im[comp] = acc_im
    rows = lax.broadcasted_iota(jnp.int32, (size, 1), 0)
    cols = lax.broadcasted_iota(jnp.int32, (1, size), 1)
    half = size // 2
    wave_y = jnp.where(rows < half, rows, rows - size).astype(f32) / (size / 2.0)
    wave_z = jnp.where(cols < half, cols, cols - size).astype(f32) / (size / 2.0)
    waves = (qx_ref[plane], wave_y, wave_z)
    c_hi = chi_ref[...]
    c_lo = clo_ref[...]
    s_hi = shi_ref[...]
    s_lo = slo_ref[...]
    for slot, comp in enumerate(comps):
        a = (comp + 1) % 3
        b = (comp + 2) % 3
        cur_re = -(waves[a] * part_im[b] - waves[b] * part_im[a])
        cur_im = waves[a] * part_re[b] - waves[b] * part_re[a]
        z_re = dot_right(cur_re, c_hi, c_lo) - dot_right(cur_im, s_hi, s_lo)
        z_im = dot_right(cur_re, s_hi, s_lo) + dot_right(cur_im, c_hi, c_lo)
        y_re = dot_left(c_hi, c_lo, z_re) - dot_left(s_hi, s_lo, z_im)
        y_im = dot_left(s_hi, s_lo, z_re) + dot_left(c_hi, c_lo, z_im)
        out_ref[0, 0, slot, 0] = y_re
        out_ref[1, 0, slot, 0] = y_im


def numpy_split(table):
    full = table.astype(np.float32)
    high = full.astype(ml_dtypes.bfloat16)
    low = (full - high.astype(np.float32)).astype(ml_dtypes.bfloat16)
    return jnp.asarray(high), jnp.asarray(low)


def dft_tables(length, orient):
    indices = np.arange(length, dtype=np.int64)
    phases = indices[:, None] * indices[None, :] % length
    angles = phases.astype(np.float64) * (2.0 * math.pi / length)
    norm_factor = 1.0 / math.sqrt(length)
    c_hi, c_lo = numpy_split(np.cos(angles) * norm_factor)
    s_hi, s_lo = numpy_split(np.sin(angles) * norm_factor * orient)
    return c_hi, c_lo, s_hi, s_lo


def front_pass(comps, coef_rows, wave_x, trial_bands, locked_bands):
    band_count, _, _, local_x, size, _ = trial_bands.shape
    kept = locked_bands.shape[0]
    tables = dft_tables(size, 1.0)
    smem = pl.BlockSpec(memory_space=pltpu.SMEM)
    table_spec = pl.BlockSpec((size, size), lambda b, x: (0, 0))
    width = len(comps)
    return pl.pallas_call(
        functools.partial(front_kernel, comps),
        grid=(band_count, local_x),
        in_specs=[
            smem,
            smem,
            pl.BlockSpec((1, 2, 3, 1, size, size), lambda b, x: (b, 0, 0, x, 0, 0)),
            pl.BlockSpec((kept, 2, 3, 1, size, size), lambda b, x: (0, 0, 0, x, 0, 0)),
            table_spec,
            table_spec,
            table_spec,
            table_spec,
        ],
        out_specs=pl.BlockSpec((2, 1, width, 1, size, size), lambda b, x: (0, b, 0, x, 0, 0)),
        out_shape=jax.ShapeDtypeStruct((2, band_count, width, local_x, size, size), jnp.float32),
    )(coef_rows, wave_x, trial_bands, locked_bands, *tables)


def butterfly_sum(values, axis, count):
    if count & (count - 1):
        return lax.psum(values, axis)
    step = 1
    while step < count:
        pairs = [(index, index ^ step) for index in range(count)]
        values = values + lax.ppermute(values, axis, pairs)
        step *= 2
    return values


def inner_sum(left_rows, right_rows):
    return jnp.einsum("an,bn->ab", left_rows, right_rows, preferred_element_type=jnp.float32)


def remove_locked(gram_sums, trial_re, trial_im, locked_re, locked_im):
    gram_a, gram_q, proj_re, proj_im = gram_sums
    kept_count = gram_a.shape[0]
    gram = jnp.concatenate(
        [jnp.concatenate([gram_a, gram_q], axis=1), jnp.concatenate([gram_q.T, gram_a], axis=1)],
        axis=0,
    )
    rhs_both = jnp.concatenate([proj_re, proj_im], axis=0)
    lower = jnp.linalg.cholesky(gram)
    middle = lax.linalg.triangular_solve(lower, rhs_both, left_side=True, lower=True)
    coef = lax.linalg.triangular_solve(lower, middle, left_side=True, lower=True, transpose_a=True)
    coef_one = coef[:kept_count]
    coef_two = coef[kept_count:]
    locked_re32 = locked_re.astype(jnp.float32)
    locked_im32 = locked_im.astype(jnp.float32)
    out_re = (
        trial_re.astype(jnp.float32)
        - jnp.einsum("ab,an->bn", coef_one, locked_re32, precision=highest)
        + jnp.einsum("ab,an->bn", coef_two, locked_im32, precision=highest)
    )
    out_im = (
        trial_im.astype(jnp.float32)
        - jnp.einsum("ab,an->bn", coef_one, locked_im32, precision=highest)
        - jnp.einsum("ab,an->bn", coef_two, locked_re32, precision=highest)
    )
    return (out_re, out_im)


def solve_coef(gram_sums):
    gram_a, gram_q, proj_re, proj_im = gram_sums
    gram = jnp.concatenate(
        [jnp.concatenate([gram_a, gram_q], axis=1), jnp.concatenate([gram_q.T, gram_a], axis=1)],
        axis=0,
    )
    rhs_both = jnp.concatenate([proj_re, proj_im], axis=0)
    lower = jnp.linalg.cholesky(gram)
    middle = lax.linalg.triangular_solve(lower, rhs_both, left_side=True, lower=True)
    return lax.linalg.triangular_solve(lower, middle, left_side=True, lower=True, transpose_a=True)


def maxwell_pass(chunks, waves, inv_diag, inv_corr, to_space_fn, to_spectrum_fn):
    space = jnp.concatenate([transform(to_space_fn(chunk), 2, 1.0) for chunk in chunks], axis=2)
    weighted = apply_tensor(space, inv_diag, inv_corr)
    homes = []
    for comp in range(weighted.shape[2]):
        home = to_spectrum_fn(transform(weighted[:, :, comp : comp + 1], 2, -1.0))
        home = transform(home, 3, -1.0)
        homes.append(transform(home, 4, -1.0))
    home = jnp.concatenate(homes, axis=2)
    return (curl_times_i(waves, home), space, weighted)


def per_device(wide_count, trial_bands, locked_bands, inv_diag, inv_corr):
    band_count = trial_bands.shape[0]
    kept_count = locked_bands.shape[0]
    local_x = trial_bands.shape[3]
    grid_len = trial_bands.shape[4]
    rows = jnp.concatenate(
        [locked_bands.reshape((2 * kept_count,) + locked_bands.shape[2:]),
         trial_bands.reshape((2 * band_count,) + trial_bands.shape[2:])],
        axis=0,
    )
    pairs = jnp.einsum("icxyz,jcxyz->ij", rows, rows, preferred_element_type=jnp.float32)
    pairs = butterfly_sum(pairs, "wide", wide_count)
    lk = pairs[: 2 * kept_count, : 2 * kept_count].reshape(kept_count, 2, kept_count, 2)
    lt = pairs[: 2 * kept_count, 2 * kept_count :].reshape(kept_count, 2, band_count, 2)
    gram_a = lk[:, 0, :, 0] + lk[:, 1, :, 1]
    gram_q = lk[:, 1, :, 0] - lk[:, 0, :, 1]
    proj_re = lt[:, 0, :, 0] + lt[:, 1, :, 1]
    proj_im = lt[:, 0, :, 1] - lt[:, 1, :, 0]
    gram_sums = (gram_a, gram_q, proj_re, proj_im)
    coef = solve_coef(gram_sums)
    start_x = lax.axis_index("wide") * local_x
    full_axis = jnp.arange(grid_len, dtype=jnp.int32)
    wave_x = signed_wave(start_x + jnp.arange(local_x, dtype=jnp.int32), grid_len)
    wave_full = signed_wave(full_axis, grid_len)
    waves = (wave_x, wave_full, wave_full)

    def send_out_one(field):
        return lax.all_to_all(field, "wide", split_axis=4, concat_axis=3, tiled=True)

    def send_home_one(field):
        return lax.all_to_all(field, "wide", split_axis=3, concat_axis=4, tiled=True)

    chunks = [front_pass((comp,), coef.T, wave_x, trial_bands, locked_bands) for comp in range(3)]
    results = [maxwell_pass(chunks, waves, inv_diag, inv_corr, send_out_one, send_home_one)]
    applied_st, space, weighted = [
        jnp.concatenate([entry[slot] for entry in results], axis=1) for slot in range(3)
    ]
    applied = jnp.stack([applied_st[0], applied_st[1]], axis=1).astype(jnp.bfloat16)
    scale_all = 1.0 / float(grid_len * grid_len * grid_len)
    left_re = space[0].reshape(band_count, -1)
    left_im = space[1].reshape(band_count, -1)
    right_re = weighted[0].reshape(band_count, -1)
    right_im = weighted[1].reshape(band_count, -1)
    part_re = jnp.einsum("an,bn->ab", left_re, right_re, precision=highest) + jnp.einsum(
        "an,bn->ab", left_im, right_im, precision=highest
    )
    part_im = jnp.einsum("an,bn->ab", left_re, right_im, precision=highest) - jnp.einsum(
        "an,bn->ab", left_im, right_re, precision=highest
    )
    total_re, total_im = lax.psum((part_re, part_im), "wide")
    rayleigh = jnp.stack([total_re * scale_all, total_im * scale_all], axis=0)
    return (applied, rayleigh)


def solution(mesh):
    in_specs = (
        P("groups", None, None, "wide", None, None),
        P("groups", None, None, "wide", None, None),
        P("groups", None, "wide", None),
        P("groups", None, "wide", None),
    )
    out_specs = (P("groups", None, None, "wide", None, None), P("groups", None, None))
    wide_count = mesh.shape["wide"]
    return jax.shard_map(
        functools.partial(per_device, wide_count), mesh=mesh, in_specs=in_specs, out_specs=out_specs, check_vma=False
    )
```

```python
import functools
import math

import ml_dtypes
import numpy as np

import jax
import jax.numpy as jnp
from jax import lax
from jax.sharding import PartitionSpec as P
from jax.experimental import pallas as pl
from jax.experimental.pallas import tpu as pltpu

highest = lax.Precision.HIGHEST
three_pass = lax.Precision.HIGH


def signed_wave(indices, length):
    shifted = jnp.where(indices < length // 2, indices, indices - length)
    return shifted.astype(jnp.float32) / (length / 2.0)


def cross_wave(wave_x, wave_y, wave_z, vectors):
    comp_x = vectors[..., 0, :, :, :]
    comp_y = vectors[..., 1, :, :, :]
    comp_z = vectors[..., 2, :, :, :]
    along_x = wave_x[:, None, None]
    along_y = wave_y[None, :, None]
    along_z = wave_z[None, None, :]
    return jnp.stack(
        [
            along_y * comp_z - along_z * comp_y,
            along_z * comp_x - along_x * comp_z,
            along_x * comp_y - along_y * comp_x,
        ],
        axis=-4,
    )


def curl_times_i(waves, stacked):
    wave_x, wave_y, wave_z = waves
    return jnp.stack(
        [
            -cross_wave(wave_x, wave_y, wave_z, stacked[1]),
            cross_wave(wave_x, wave_y, wave_z, stacked[0]),
        ],
        axis=0,
    )


def apply_tensor(vectors, inv_diag, inv_corr):
    coupling_xy = inv_corr[0] * jnp.sqrt(inv_diag[0] * inv_diag[1])
    coupling_xz = inv_corr[1] * jnp.sqrt(inv_diag[0] * inv_diag[2])
    coupling_yz = inv_corr[2] * jnp.sqrt(inv_diag[1] * inv_diag[2])
    comp_x = vectors[..., 0, :, :, :]
    comp_y = vectors[..., 1, :, :, :]
    comp_z = vectors[..., 2, :, :, :]
    out_x = inv_diag[0] * comp_x + coupling_xy * comp_y + coupling_xz * comp_z
    out_y = coupling_xy * comp_x + inv_diag[1] * comp_y + coupling_yz * comp_z
    out_z = coupling_xz * comp_x + coupling_yz * comp_y + inv_diag[2] * comp_z
    return jnp.stack([out_x, out_y, out_z], axis=-4)


def complex_table(length, orient):
    indices = jnp.arange(length, dtype=jnp.int32)
    phases = indices[:, None] * indices[None, :] % length
    angles = phases.astype(jnp.float32) * (2.0 * math.pi / length)
    norm_factor = 1.0 / math.sqrt(length)
    cos_table = jnp.cos(angles) * norm_factor
    sin_table = jnp.sin(angles) * norm_factor * orient
    return jnp.stack(
        [jnp.stack([cos_table, sin_table], axis=0), jnp.stack([-sin_table, cos_table], axis=0)],
        axis=0,
    )


def transform(stacked, axis_dim, orient):
    table = complex_table(stacked.shape[axis_dim + 1], orient)
    if axis_dim == 2:
        return jnp.einsum("pbckyz,pqkn->qbcnyz", stacked, table, precision=three_pass)
    if axis_dim == 3:
        return jnp.einsum("pbcxkz,pqkn->qbcxnz", stacked, table, precision=three_pass)
    return jnp.einsum("pbcxyk,pqkn->qbcxyn", stacked, table, precision=three_pass)


def split_hi_lo(values):
    scaled = values * 65537.0
    top = scaled - (scaled - values)
    return top.astype(jnp.bfloat16), (values - top).astype(jnp.bfloat16)


def dot_right(values, table_hi, table_lo):
    high, low = split_hi_lo(values)
    f32 = jnp.float32
    return (
        jnp.dot(high, table_hi, preferred_element_type=f32)
        + jnp.dot(low, table_hi, preferred_element_type=f32)
        + jnp.dot(high, table_lo, preferred_element_type=f32)
    )


def dot_left(table_hi, table_lo, values):
    high, low = split_hi_lo(values)
    f32 = jnp.float32
    return (
        jnp.dot(table_hi, high, preferred_element_type=f32)
        + jnp.dot(table_hi, low, preferred_element_type=f32)
        + jnp.dot(table_lo, high, preferred_element_type=f32)
    )


def front_kernel(comps, coef_ref, qx_ref, trial_ref, locked_ref, chi_ref, clo_ref, shi_ref, slo_ref, out_ref):
    band = pl.program_id(0)
    plane = pl.program_id(1)
    kept = locked_ref.shape[0]
    size = trial_ref.shape[-1]
    f32 = jnp.float32
    first = [coef_ref[band, k] for k in range(kept)]
    second = [coef_ref[band, kept + k] for k in range(kept)]
    needed = sorted({(c + 1) % 3 for c in comps} | {(c + 2) % 3 for c in comps})
    part_re = {}
    part_im = {}
    for comp in needed:
        acc_re = trial_ref[0, 0, comp, 0].astype(f32)
        acc_im = trial_ref[0, 1, comp, 0].astype(f32)
        for k in range(kept):
            l_re = locked_ref[k, 0, comp, 0].astype(f32)
            l_im = locked_ref[k, 1, comp, 0].astype(f32)
            acc_re = acc_re - first[k] * l_re + second[k] * l_im
            acc_im = acc_im - first[k] * l_im - second[k] * l_re
        part_re[comp] = acc_re
        part_im[comp] = acc_im
    rows = lax.broadcasted_iota(jnp.int32, (size, 1), 0)
    cols = lax.broadcasted_iota(jnp.int32, (1, size), 1)
    half = size // 2
    wave_y = jnp.where(rows < half, rows, rows - size).astype(f32) / (size / 2.0)
    wave_z = jnp.where(cols < half, cols, cols - size).astype(f32) / (size / 2.0)
    waves = (qx_ref[plane], wave_y, wave_z)
    c_hi = chi_ref[...]
    c_lo = clo_ref[...]
    s_hi = shi_ref[...]
    s_lo = slo_ref[...]
    for slot, comp in enumerate(comps):
        a = (comp + 1) % 3
        b = (comp + 2) % 3
        cur_re = -(waves[a] * part_im[b] - waves[b] * part_im[a])
        cur_im = waves[a] * part_re[b] - waves[b] * part_re[a]
        z_re = dot_right(cur_re, c_hi, c_lo) - dot_right(cur_im, s_hi, s_lo)
        z_im = dot_right(cur_re, s_hi, s_lo) + dot_right(cur_im, c_hi, c_lo)
        y_re = dot_left(c_hi, c_lo, z_re) - dot_left(s_hi, s_lo, z_im)
        y_im = dot_left(s_hi, s_lo, z_re) + dot_left(c_hi, c_lo, z_im)
        out_ref[0, 0, slot, 0] = y_re
        out_ref[1, 0, slot, 0] = y_im


def numpy_split(table):
    full = table.astype(np.float32)
    high = full.astype(ml_dtypes.bfloat16)
    low = (full - high.astype(np.float32)).astype(ml_dtypes.bfloat16)
    return jnp.asarray(high), jnp.asarray(low)


def dft_tables(length, orient):
    indices = np.arange(length, dtype=np.int64)
    phases = indices[:, None] * indices[None, :] % length
    angles = phases.astype(np.float64) * (2.0 * math.pi / length)
    norm_factor = 1.0 / math.sqrt(length)
    c_hi, c_lo = numpy_split(np.cos(angles) * norm_factor)
    s_hi, s_lo = numpy_split(np.sin(angles) * norm_factor * orient)
    return c_hi, c_lo, s_hi, s_lo


def front_pass(comps, coef_rows, wave_x, trial_bands, locked_bands):
    band_count, _, _, local_x, size, _ = trial_bands.shape
    kept = locked_bands.shape[0]
    tables = dft_tables(size, 1.0)
    smem = pl.BlockSpec(memory_space=pltpu.SMEM)
    table_spec = pl.BlockSpec((size, size), lambda b, x: (0, 0))
    width = len(comps)
    return pl.pallas_call(
        functools.partial(front_kernel, comps),
        grid=(band_count, local_x),
        in_specs=[
            smem,
            smem,
            pl.BlockSpec((1, 2, 3, 1, size, size), lambda b, x: (b, 0, 0, x, 0, 0)),
            pl.BlockSpec((kept, 2, 3, 1, size, size), lambda b, x: (0, 0, 0, x, 0, 0)),
            table_spec,
            table_spec,
            table_spec,
            table_spec,
        ],
        out_specs=pl.BlockSpec((2, 1, width, 1, size, size), lambda b, x: (0, b, 0, x, 0, 0)),
        out_shape=jax.ShapeDtypeStruct((2, band_count, width, local_x, size, size), jnp.float32),
    )(coef_rows, wave_x, trial_bands, locked_bands, *tables)


def butterfly_sum(values, axis, count):
    if count & (count - 1):
        return lax.psum(values, axis)
    step = 1
    while step < count:
        pairs = [(index, index ^ step) for index in range(count)]
        values = values + lax.ppermute(values, axis, pairs)
        step *= 2
    return values


def inner_sum(left_rows, right_rows):
    return jnp.einsum("an,bn->ab", left_rows, right_rows, preferred_element_type=jnp.float32)


def remove_locked(gram_sums, trial_re, trial_im, locked_re, locked_im):
    gram_a, gram_q, proj_re, proj_im = gram_sums
    kept_count = gram_a.shape[0]
    gram = jnp.concatenate(
        [jnp.concatenate([gram_a, gram_q], axis=1), jnp.concatenate([gram_q.T, gram_a], axis=1)],
        axis=0,
    )
    rhs_both = jnp.concatenate([proj_re, proj_im], axis=0)
    lower = jnp.linalg.cholesky(gram)
    middle = lax.linalg.triangular_solve(lower, rhs_both, left_side=True, lower=True)
    coef = lax.linalg.triangular_solve(lower, middle, left_side=True, lower=True, transpose_a=True)
    coef_one = coef[:kept_count]
    coef_two = coef[kept_count:]
    locked_re32 = locked_re.astype(jnp.float32)
    locked_im32 = locked_im.astype(jnp.float32)
    out_re = (
        trial_re.astype(jnp.float32)
        - jnp.einsum("ab,an->bn", coef_one, locked_re32, precision=highest)
        + jnp.einsum("ab,an->bn", coef_two, locked_im32, precision=highest)
    )
    out_im = (
        trial_im.astype(jnp.float32)
        - jnp.einsum("ab,an->bn", coef_one, locked_im32, precision=highest)
        - jnp.einsum("ab,an->bn", coef_two, locked_re32, precision=highest)
    )
    return (out_re, out_im)


def solve_coef(gram_sums):
    gram_a, gram_q, proj_re, proj_im = gram_sums
    gram = jnp.concatenate(
        [jnp.concatenate([gram_a, gram_q], axis=1), jnp.concatenate([gram_q.T, gram_a], axis=1)],
        axis=0,
    )
    rhs_both = jnp.concatenate([proj_re, proj_im], axis=0)
    lower = jnp.linalg.cholesky(gram)
    middle = lax.linalg.triangular_solve(lower, rhs_both, left_side=True, lower=True)
    return lax.linalg.triangular_solve(lower, middle, left_side=True, lower=True, transpose_a=True)


def maxwell_pass(chunks, waves, inv_diag, inv_corr, to_space_fn, to_spectrum_fn):
    space = jnp.concatenate([transform(to_space_fn(chunk), 2, 1.0) for chunk in chunks], axis=2)
    weighted = apply_tensor(space, inv_diag, inv_corr)
    homes = []
    for comp in range(weighted.shape[2]):
        home = to_spectrum_fn(transform(weighted[:, :, comp : comp + 1], 2, -1.0))
        home = transform(home, 3, -1.0)
        homes.append(transform(home, 4, -1.0))
    home = jnp.concatenate(homes, axis=2)
    return (curl_times_i(waves, home), space, weighted)


def per_device(wide_count, trial_bands, locked_bands, inv_diag, inv_corr):
    band_count = trial_bands.shape[0]
    kept_count = locked_bands.shape[0]
    local_x = trial_bands.shape[3]
    grid_len = trial_bands.shape[4]
    rows = jnp.concatenate(
        [locked_bands.reshape((2 * kept_count,) + locked_bands.shape[2:]),
         trial_bands.reshape((2 * band_count,) + trial_bands.shape[2:])],
        axis=0,
    )
    pairs = jnp.einsum("icxyz,jcxyz->ij", rows, rows, preferred_element_type=jnp.float32)
    pairs = butterfly_sum(pairs, "wide", wide_count)
    lk = pairs[: 2 * kept_count, : 2 * kept_count].reshape(kept_count, 2, kept_count, 2)
    lt = pairs[: 2 * kept_count, 2 * kept_count :].reshape(kept_count, 2, band_count, 2)
    gram_a = lk[:, 0, :, 0] + lk[:, 1, :, 1]
    gram_q = lk[:, 1, :, 0] - lk[:, 0, :, 1]
    proj_re = lt[:, 0, :, 0] + lt[:, 1, :, 1]
    proj_im = lt[:, 0, :, 1] - lt[:, 1, :, 0]
    gram_sums = (gram_a, gram_q, proj_re, proj_im)
    coef = solve_coef(gram_sums)
    start_x = lax.axis_index("wide") * local_x
    full_axis = jnp.arange(grid_len, dtype=jnp.int32)
    wave_x = signed_wave(start_x + jnp.arange(local_x, dtype=jnp.int32), grid_len)
    wave_full = signed_wave(full_axis, grid_len)
    waves = (wave_x, wave_full, wave_full)

    def send_out_one(field):
        return lax.all_to_all(field, "wide", split_axis=4, concat_axis=3, tiled=True)

    def send_home_one(field):
        return lax.all_to_all(field, "wide", split_axis=3, concat_axis=4, tiled=True)

    chunks = [front_pass((comp,), coef.T, wave_x, trial_bands, locked_bands) for comp in range(3)]
    results = [maxwell_pass(chunks, waves, inv_diag, inv_corr, send_out_one, send_home_one)]
    applied_st, space, weighted = [
        jnp.concatenate([entry[slot] for entry in results], axis=1) for slot in range(3)
    ]
    applied = jnp.stack([applied_st[0], applied_st[1]], axis=1).astype(jnp.bfloat16)
    scale_all = 1.0 / float(grid_len * grid_len * grid_len)
    left_re = space[0].reshape(band_count, -1)
    left_im = space[1].reshape(band_count, -1)
    right_re = weighted[0].reshape(band_count, -1)
    right_im = weighted[1].reshape(band_count, -1)
    part_re = jnp.einsum("an,bn->ab", left_re, right_re, precision=highest) + jnp.einsum(
        "an,bn->ab", left_im, right_im, precision=highest
    )
    part_im = jnp.einsum("an,bn->ab", left_re, right_im, precision=highest) - jnp.einsum(
        "an,bn->ab", left_im, right_re, precision=highest
    )
    total_re, total_im = butterfly_sum(jnp.stack([part_re, part_im], axis=0), "wide", wide_count)
    rayleigh = jnp.stack([total_re * scale_all, total_im * scale_all], axis=0)
    return (applied, rayleigh)


def solution(mesh):
    in_specs = (
        P("groups", None, None, "wide", None, None),
        P("groups", None, None, "wide", None, None),
        P("groups", None, "wide", None),
        P("groups", None, "wide", None),
    )
    out_specs = (P("groups", None, None, "wide", None, None), P("groups", None, None))
    wide_count = mesh.shape["wide"]
    return jax.shard_map(
        functools.partial(per_device, wide_count), mesh=mesh, in_specs=in_specs, out_specs=out_specs, check_vma=False
    )
```

```python
import functools
import math

import ml_dtypes
import numpy as np

import jax
import jax.numpy as jnp
from jax import lax
from jax.sharding import PartitionSpec as P
from jax.experimental import pallas as pl
from jax.experimental.pallas import tpu as pltpu

highest = lax.Precision.HIGHEST
three_pass = lax.Precision.HIGH


def signed_wave(indices, length):
    shifted = jnp.where(indices < length // 2, indices, indices - length)
    return shifted.astype(jnp.float32) / (length / 2.0)


def cross_wave(wave_x, wave_y, wave_z, vectors):
    comp_x = vectors[..., 0, :, :, :]
    comp_y = vectors[..., 1, :, :, :]
    comp_z = vectors[..., 2, :, :, :]
    along_x = wave_x[:, None, None]
    along_y = wave_y[None, :, None]
    along_z = wave_z[None, None, :]
    return jnp.stack(
        [
            along_y * comp_z - along_z * comp_y,
            along_z * comp_x - along_x * comp_z,
            along_x * comp_y - along_y * comp_x,
        ],
        axis=-4,
    )


def curl_times_i(waves, stacked):
    wave_x, wave_y, wave_z = waves
    return jnp.stack(
        [
            -cross_wave(wave_x, wave_y, wave_z, stacked[1]),
            cross_wave(wave_x, wave_y, wave_z, stacked[0]),
        ],
        axis=0,
    )


def apply_tensor(vectors, inv_diag, inv_corr):
    coupling_xy = inv_corr[0] * jnp.sqrt(inv_diag[0] * inv_diag[1])
    coupling_xz = inv_corr[1] * jnp.sqrt(inv_diag[0] * inv_diag[2])
    coupling_yz = inv_corr[2] * jnp.sqrt(inv_diag[1] * inv_diag[2])
    comp_x = vectors[..., 0, :, :, :]
    comp_y = vectors[..., 1, :, :, :]
    comp_z = vectors[..., 2, :, :, :]
    out_x = inv_diag[0] * comp_x + coupling_xy * comp_y + coupling_xz * comp_z
    out_y = coupling_xy * comp_x + inv_diag[1] * comp_y + coupling_yz * comp_z
    out_z = coupling_xz * comp_x + coupling_yz * comp_y + inv_diag[2] * comp_z
    return jnp.stack([out_x, out_y, out_z], axis=-4)


def complex_table(length, orient):
    indices = jnp.arange(length, dtype=jnp.int32)
    phases = indices[:, None] * indices[None, :] % length
    angles = phases.astype(jnp.float32) * (2.0 * math.pi / length)
    norm_factor = 1.0 / math.sqrt(length)
    cos_table = jnp.cos(angles) * norm_factor
    sin_table = jnp.sin(angles) * norm_factor * orient
    return jnp.stack(
        [jnp.stack([cos_table, sin_table], axis=0), jnp.stack([-sin_table, cos_table], axis=0)],
        axis=0,
    )


def transform(stacked, axis_dim, orient):
    table = complex_table(stacked.shape[axis_dim + 1], orient)
    if axis_dim == 2:
        return jnp.einsum("pbckyz,pqkn->qbcnyz", stacked, table, precision=three_pass)
    if axis_dim == 3:
        return jnp.einsum("pbcxkz,pqkn->qbcxnz", stacked, table, precision=three_pass)
    return jnp.einsum("pbcxyk,pqkn->qbcxyn", stacked, table, precision=three_pass)


def split_hi_lo(values):
    scaled = values * 65537.0
    top = scaled - (scaled - values)
    return top.astype(jnp.bfloat16), (values - top).astype(jnp.bfloat16)


def dot_right(values, table_hi, table_lo):
    high, low = split_hi_lo(values)
    f32 = jnp.float32
    return (
        jnp.dot(high, table_hi, preferred_element_type=f32)
        + jnp.dot(low, table_hi, preferred_element_type=f32)
        + jnp.dot(high, table_lo, preferred_element_type=f32)
    )


def dot_left(table_hi, table_lo, values):
    high, low = split_hi_lo(values)
    f32 = jnp.float32
    return (
        jnp.dot(table_hi, high, preferred_element_type=f32)
        + jnp.dot(table_hi, low, preferred_element_type=f32)
        + jnp.dot(table_lo, high, preferred_element_type=f32)
    )


def front_kernel(comps, coef_ref, qx_ref, trial_ref, locked_ref, chi_ref, clo_ref, shi_ref, slo_ref, out_ref):
    band = pl.program_id(0)
    plane = pl.program_id(1)
    kept = locked_ref.shape[0]
    size = trial_ref.shape[-1]
    f32 = jnp.float32
    first = [coef_ref[band, k] for k in range(kept)]
    second = [coef_ref[band, kept + k] for k in range(kept)]
    needed = sorted({(c + 1) % 3 for c in comps} | {(c + 2) % 3 for c in comps})
    part_re = {}
    part_im = {}
    for comp in needed:
        acc_re = trial_ref[0, 0, comp, 0].astype(f32)
        acc_im = trial_ref[0, 1, comp, 0].astype(f32)
        for k in range(kept):
            l_re = locked_ref[k, 0, comp, 0].astype(f32)
            l_im = locked_ref[k, 1, comp, 0].astype(f32)
            acc_re = acc_re - first[k] * l_re + second[k] * l_im
            acc_im = acc_im - first[k] * l_im - second[k] * l_re
        part_re[comp] = acc_re
        part_im[comp] = acc_im
    rows = lax.broadcasted_iota(jnp.int32, (size, 1), 0)
    cols = lax.broadcasted_iota(jnp.int32, (1, size), 1)
    half = size // 2
    wave_y = jnp.where(rows < half, rows, rows - size).astype(f32) / (size / 2.0)
    wave_z = jnp.where(cols < half, cols, cols - size).astype(f32) / (size / 2.0)
    waves = (qx_ref[plane], wave_y, wave_z)
    c_hi = chi_ref[...]
    c_lo = clo_ref[...]
    s_hi = shi_ref[...]
    s_lo = slo_ref[...]
    for slot, comp in enumerate(comps):
        a = (comp + 1) % 3
        b = (comp + 2) % 3
        cur_re = -(waves[a] * part_im[b] - waves[b] * part_im[a])
        cur_im = waves[a] * part_re[b] - waves[b] * part_re[a]
        z_re = dot_right(cur_re, c_hi, c_lo) - dot_right(cur_im, s_hi, s_lo)
        z_im = dot_right(cur_re, s_hi, s_lo) + dot_right(cur_im, c_hi, c_lo)
        y_re = dot_left(c_hi, c_lo, z_re) - dot_left(s_hi, s_lo, z_im)
        y_im = dot_left(s_hi, s_lo, z_re) + dot_left(c_hi, c_lo, z_im)
        out_ref[0, 0, slot, 0] = y_re
        out_ref[1, 0, slot, 0] = y_im


def numpy_split(table):
    full = table.astype(np.float32)
    high = full.astype(ml_dtypes.bfloat16)
    low = (full - high.astype(np.float32)).astype(ml_dtypes.bfloat16)
    return jnp.asarray(high), jnp.asarray(low)


def dft_tables(length, orient):
    indices = np.arange(length, dtype=np.int64)
    phases = indices[:, None] * indices[None, :] % length
    angles = phases.astype(np.float64) * (2.0 * math.pi / length)
    norm_factor = 1.0 / math.sqrt(length)
    c_hi, c_lo = numpy_split(np.cos(angles) * norm_factor)
    s_hi, s_lo = numpy_split(np.sin(angles) * norm_factor * orient)
    return c_hi, c_lo, s_hi, s_lo


def front_pass(comps, coef_rows, wave_x, trial_bands, locked_bands):
    band_count, _, _, local_x, size, _ = trial_bands.shape
    kept = locked_bands.shape[0]
    tables = dft_tables(size, 1.0)
    smem = pl.BlockSpec(memory_space=pltpu.SMEM)
    table_spec = pl.BlockSpec((size, size), lambda b, x: (0, 0))
    width = len(comps)
    return pl.pallas_call(
        functools.partial(front_kernel, comps),
        grid=(band_count, local_x),
        in_specs=[
            smem,
            smem,
            pl.BlockSpec((1, 2, 3, 1, size, size), lambda b, x: (b, 0, 0, x, 0, 0)),
            pl.BlockSpec((kept, 2, 3, 1, size, size), lambda b, x: (0, 0, 0, x, 0, 0)),
            table_spec,
            table_spec,
            table_spec,
            table_spec,
        ],
        out_specs=pl.BlockSpec((2, 1, width, 1, size, size), lambda b, x: (0, b, 0, x, 0, 0)),
        out_shape=jax.ShapeDtypeStruct((2, band_count, width, local_x, size, size), jnp.float32),
    )(coef_rows, wave_x, trial_bands, locked_bands, *tables)


def butterfly_sum(values, axis, count):
    if count & (count - 1):
        return lax.psum(values, axis)
    step = 1
    while step < count:
        pairs = [(index, index ^ step) for index in range(count)]
        values = values + lax.ppermute(values, axis, pairs)
        step *= 2
    return values


def inner_sum(left_rows, right_rows):
    return jnp.einsum("an,bn->ab", left_rows, right_rows, preferred_element_type=jnp.float32)


def remove_locked(gram_sums, trial_re, trial_im, locked_re, locked_im):
    gram_a, gram_q, proj_re, proj_im = gram_sums
    kept_count = gram_a.shape[0]
    gram = jnp.concatenate(
        [jnp.concatenate([gram_a, gram_q], axis=1), jnp.concatenate([gram_q.T, gram_a], axis=1)],
        axis=0,
    )
    rhs_both = jnp.concatenate([proj_re, proj_im], axis=0)
    lower = jnp.linalg.cholesky(gram)
    middle = lax.linalg.triangular_solve(lower, rhs_both, left_side=True, lower=True)
    coef = lax.linalg.triangular_solve(lower, middle, left_side=True, lower=True, transpose_a=True)
    coef_one = coef[:kept_count]
    coef_two = coef[kept_count:]
    locked_re32 = locked_re.astype(jnp.float32)
    locked_im32 = locked_im.astype(jnp.float32)
    out_re = (
        trial_re.astype(jnp.float32)
        - jnp.einsum("ab,an->bn", coef_one, locked_re32, precision=highest)
        + jnp.einsum("ab,an->bn", coef_two, locked_im32, precision=highest)
    )
    out_im = (
        trial_im.astype(jnp.float32)
        - jnp.einsum("ab,an->bn", coef_one, locked_im32, precision=highest)
        - jnp.einsum("ab,an->bn", coef_two, locked_re32, precision=highest)
    )
    return (out_re, out_im)


def solve_coef(gram_sums):
    gram_a, gram_q, proj_re, proj_im = gram_sums
    gram = jnp.concatenate(
        [jnp.concatenate([gram_a, gram_q], axis=1), jnp.concatenate([gram_q.T, gram_a], axis=1)],
        axis=0,
    )
    rhs_both = jnp.concatenate([proj_re, proj_im], axis=0)
    lower = jnp.linalg.cholesky(gram)
    middle = lax.linalg.triangular_solve(lower, rhs_both, left_side=True, lower=True)
    return lax.linalg.triangular_solve(lower, middle, left_side=True, lower=True, transpose_a=True)


def maxwell_pass(chunks, waves, inv_diag, inv_corr, to_space_fn, to_spectrum_fn):
    space = jnp.concatenate([transform(to_space_fn(chunk), 2, 1.0) for chunk in chunks], axis=2)
    weighted = apply_tensor(space, inv_diag, inv_corr)
    home = to_spectrum_fn(transform(weighted, 2, -1.0))
    home = transform(home, 3, -1.0)
    home = transform(home, 4, -1.0)
    return (curl_times_i(waves, home), space, weighted)


def per_device(wide_count, trial_bands, locked_bands, inv_diag, inv_corr):
    band_count = trial_bands.shape[0]
    kept_count = locked_bands.shape[0]
    local_x = trial_bands.shape[3]
    grid_len = trial_bands.shape[4]
    rows = jnp.concatenate(
        [locked_bands.reshape((2 * kept_count,) + locked_bands.shape[2:]),
         trial_bands.reshape((2 * band_count,) + trial_bands.shape[2:])],
        axis=0,
    )
    pairs = jnp.einsum("icxyz,jcxyz->ij", rows, rows, preferred_element_type=jnp.float32)
    pairs = butterfly_sum(pairs, "wide", wide_count)
    lk = pairs[: 2 * kept_count, : 2 * kept_count].reshape(kept_count, 2, kept_count, 2)
    lt = pairs[: 2 * kept_count, 2 * kept_count :].reshape(kept_count, 2, band_count, 2)
    gram_a = lk[:, 0, :, 0] + lk[:, 1, :, 1]
    gram_q = lk[:, 1, :, 0] - lk[:, 0, :, 1]
    proj_re = lt[:, 0, :, 0] + lt[:, 1, :, 1]
    proj_im = lt[:, 0, :, 1] - lt[:, 1, :, 0]
    gram_sums = (gram_a, gram_q, proj_re, proj_im)
    coef = solve_coef(gram_sums)
    start_x = lax.axis_index("wide") * local_x
    full_axis = jnp.arange(grid_len, dtype=jnp.int32)
    wave_x = signed_wave(start_x + jnp.arange(local_x, dtype=jnp.int32), grid_len)
    wave_full = signed_wave(full_axis, grid_len)
    waves = (wave_x, wave_full, wave_full)

    def send_out_one(field):
        return lax.all_to_all(field, "wide", split_axis=4, concat_axis=3, tiled=True)

    def send_home_one(field):
        return lax.all_to_all(field, "wide", split_axis=3, concat_axis=4, tiled=True)

    chunks = [front_pass((comp,), coef.T, wave_x, trial_bands, locked_bands) for comp in range(3)]
    results = [maxwell_pass(chunks, waves, inv_diag, inv_corr, send_out_one, send_home_one)]
    applied_st, space, weighted = [
        jnp.concatenate([entry[slot] for entry in results], axis=1) for slot in range(3)
    ]
    applied = jnp.stack([applied_st[0], applied_st[1]], axis=1).astype(jnp.bfloat16)
    scale_all = 1.0 / float(grid_len * grid_len * grid_len)
    left_re = space[0].reshape(band_count, -1)
    left_im = space[1].reshape(band_count, -1)
    right_re = weighted[0].reshape(band_count, -1)
    right_im = weighted[1].reshape(band_count, -1)
    part_re = jnp.einsum("an,bn->ab", left_re, right_re, precision=highest) + jnp.einsum(
        "an,bn->ab", left_im, right_im, precision=highest
    )
    part_im = jnp.einsum("an,bn->ab", left_re, right_im, precision=highest) - jnp.einsum(
        "an,bn->ab", left_im, right_re, precision=highest
    )
    total_re, total_im = butterfly_sum(jnp.stack([part_re, part_im], axis=0), "wide", wide_count)
    rayleigh = jnp.stack([total_re * scale_all, total_im * scale_all], axis=0)
    return (applied, rayleigh)


def solution(mesh):
    in_specs = (
        P("groups", None, None, "wide", None, None),
        P("groups", None, None, "wide", None, None),
        P("groups", None, "wide", None),
        P("groups", None, "wide", None),
    )
    out_specs = (P("groups", None, None, "wide", None, None), P("groups", None, None))
    wide_count = mesh.shape["wide"]
    return jax.shard_map(
        functools.partial(per_device, wide_count), mesh=mesh, in_specs=in_specs, out_specs=out_specs, check_vma=False
    )
```

```python
import functools
import math

import ml_dtypes
import numpy as np

import jax
import jax.numpy as jnp
from jax import lax
from jax.sharding import PartitionSpec as P
from jax.experimental import pallas as pl
from jax.experimental.pallas import tpu as pltpu

highest = lax.Precision.HIGHEST
three_pass = lax.Precision.HIGH


def signed_wave(indices, length):
    shifted = jnp.where(indices < length // 2, indices, indices - length)
    return shifted.astype(jnp.float32) / (length / 2.0)


def cross_wave(wave_x, wave_y, wave_z, vectors):
    comp_x = vectors[..., 0, :, :, :]
    comp_y = vectors[..., 1, :, :, :]
    comp_z = vectors[..., 2, :, :, :]
    along_x = wave_x[:, None, None]
    along_y = wave_y[None, :, None]
    along_z = wave_z[None, None, :]
    return jnp.stack(
        [
            along_y * comp_z - along_z * comp_y,
            along_z * comp_x - along_x * comp_z,
            along_x * comp_y - along_y * comp_x,
        ],
        axis=-4,
    )


def curl_times_i(waves, stacked):
    wave_x, wave_y, wave_z = waves
    return jnp.stack(
        [
            -cross_wave(wave_x, wave_y, wave_z, stacked[1]),
            cross_wave(wave_x, wave_y, wave_z, stacked[0]),
        ],
        axis=0,
    )


def apply_tensor(vectors, inv_diag, inv_corr):
    coupling_xy = inv_corr[0] * jnp.sqrt(inv_diag[0] * inv_diag[1])
    coupling_xz = inv_corr[1] * jnp.sqrt(inv_diag[0] * inv_diag[2])
    coupling_yz = inv_corr[2] * jnp.sqrt(inv_diag[1] * inv_diag[2])
    comp_x = vectors[..., 0, :, :, :]
    comp_y = vectors[..., 1, :, :, :]
    comp_z = vectors[..., 2, :, :, :]
    out_x = inv_diag[0] * comp_x + coupling_xy * comp_y + coupling_xz * comp_z
    out_y = coupling_xy * comp_x + inv_diag[1] * comp_y + coupling_yz * comp_z
    out_z = coupling_xz * comp_x + coupling_yz * comp_y + inv_diag[2] * comp_z
    return jnp.stack([out_x, out_y, out_z], axis=-4)


def complex_table(length, orient):
    indices = jnp.arange(length, dtype=jnp.int32)
    phases = indices[:, None] * indices[None, :] % length
    angles = phases.astype(jnp.float32) * (2.0 * math.pi / length)
    norm_factor = 1.0 / math.sqrt(length)
    cos_table = jnp.cos(angles) * norm_factor
    sin_table = jnp.sin(angles) * norm_factor * orient
    return jnp.stack(
        [jnp.stack([cos_table, sin_table], axis=0), jnp.stack([-sin_table, cos_table], axis=0)],
        axis=0,
    )


def transform(stacked, axis_dim, orient):
    table = complex_table(stacked.shape[axis_dim + 1], orient)
    if axis_dim == 2:
        return jnp.einsum("pbckyz,pqkn->qbcnyz", stacked, table, precision=three_pass)
    if axis_dim == 3:
        return jnp.einsum("pbcxkz,pqkn->qbcxnz", stacked, table, precision=three_pass)
    return jnp.einsum("pbcxyk,pqkn->qbcxyn", stacked, table, precision=three_pass)


def split_hi_lo(values):
    scaled = values * 65537.0
    top = scaled - (scaled - values)
    return top.astype(jnp.bfloat16), (values - top).astype(jnp.bfloat16)


def dot_right(values, table_hi, table_lo):
    high, low = split_hi_lo(values)
    f32 = jnp.float32
    return (
        jnp.dot(high, table_hi, preferred_element_type=f32)
        + jnp.dot(low, table_hi, preferred_element_type=f32)
        + jnp.dot(high, table_lo, preferred_element_type=f32)
    )


def dot_left(table_hi, table_lo, values):
    high, low = split_hi_lo(values)
    f32 = jnp.float32
    return (
        jnp.dot(table_hi, high, preferred_element_type=f32)
        + jnp.dot(table_hi, low, preferred_element_type=f32)
        + jnp.dot(table_lo, high, preferred_element_type=f32)
    )


def front_kernel(comps, coef_ref, qx_ref, trial_ref, locked_ref, chi_ref, clo_ref, shi_ref, slo_ref, out_ref):
    band = pl.program_id(0)
    plane = pl.program_id(1)
    kept = locked_ref.shape[0]
    size = trial_ref.shape[-1]
    f32 = jnp.float32
    first = [coef_ref[band, k] for k in range(kept)]
    second = [coef_ref[band, kept + k] for k in range(kept)]
    needed = sorted({(c + 1) % 3 for c in comps} | {(c + 2) % 3 for c in comps})
    part_re = {}
    part_im = {}
    for comp in needed:
        acc_re = trial_ref[0, 0, comp, 0].astype(f32)
        acc_im = trial_ref[0, 1, comp, 0].astype(f32)
        for k in range(kept):
            l_re = locked_ref[k, 0, comp, 0].astype(f32)
            l_im = locked_ref[k, 1, comp, 0].astype(f32)
            acc_re = acc_re - first[k] * l_re + second[k] * l_im
            acc_im = acc_im - first[k] * l_im - second[k] * l_re
        part_re[comp] = acc_re
        part_im[comp] = acc_im
    rows = lax.broadcasted_iota(jnp.int32, (size, 1), 0)
    cols = lax.broadcasted_iota(jnp.int32, (1, size), 1)
    half = size // 2
    wave_y = jnp.where(rows < half, rows, rows - size).astype(f32) / (size / 2.0)
    wave_z = jnp.where(cols < half, cols, cols - size).astype(f32) / (size / 2.0)
    waves = (qx_ref[plane], wave_y, wave_z)
    c_hi = chi_ref[...]
    c_lo = clo_ref[...]
    s_hi = shi_ref[...]
    s_lo = slo_ref[...]
    for slot, comp in enumerate(comps):
        a = (comp + 1) % 3
        b = (comp + 2) % 3
        cur_re = -(waves[a] * part_im[b] - waves[b] * part_im[a])
        cur_im = waves[a] * part_re[b] - waves[b] * part_re[a]
        z_re = dot_right(cur_re, c_hi, c_lo) - dot_right(cur_im, s_hi, s_lo)
        z_im = dot_right(cur_re, s_hi, s_lo) + dot_right(cur_im, c_hi, c_lo)
        y_re = dot_left(c_hi, c_lo, z_re) - dot_left(s_hi, s_lo, z_im)
        y_im = dot_left(s_hi, s_lo, z_re) + dot_left(c_hi, c_lo, z_im)
        out_ref[0, 0, slot, 0] = y_re
        out_ref[1, 0, slot, 0] = y_im


def numpy_split(table):
    full = table.astype(np.float32)
    high = full.astype(ml_dtypes.bfloat16)
    low = (full - high.astype(np.float32)).astype(ml_dtypes.bfloat16)
    return jnp.asarray(high), jnp.asarray(low)


def dft_tables(length, orient):
    indices = np.arange(length, dtype=np.int64)
    phases = indices[:, None] * indices[None, :] % length
    angles = phases.astype(np.float64) * (2.0 * math.pi / length)
    norm_factor = 1.0 / math.sqrt(length)
    c_hi, c_lo = numpy_split(np.cos(angles) * norm_factor)
    s_hi, s_lo = numpy_split(np.sin(angles) * norm_factor * orient)
    return c_hi, c_lo, s_hi, s_lo


def front_pass(comps, coef_rows, wave_x, trial_bands, locked_bands):
    band_count, _, _, local_x, size, _ = trial_bands.shape
    kept = locked_bands.shape[0]
    tables = dft_tables(size, 1.0)
    smem = pl.BlockSpec(memory_space=pltpu.SMEM)
    table_spec = pl.BlockSpec((size, size), lambda b, x: (0, 0))
    width = len(comps)
    return pl.pallas_call(
        functools.partial(front_kernel, comps),
        grid=(band_count, local_x),
        in_specs=[
            smem,
            smem,
            pl.BlockSpec((1, 2, 3, 1, size, size), lambda b, x: (b, 0, 0, x, 0, 0)),
            pl.BlockSpec((kept, 2, 3, 1, size, size), lambda b, x: (0, 0, 0, x, 0, 0)),
            table_spec,
            table_spec,
            table_spec,
            table_spec,
        ],
        out_specs=pl.BlockSpec((2, 1, width, 1, size, size), lambda b, x: (0, b, 0, x, 0, 0)),
        out_shape=jax.ShapeDtypeStruct((2, band_count, width, local_x, size, size), jnp.float32),
    )(coef_rows, wave_x, trial_bands, locked_bands, *tables)


def butterfly_sum(values, axis, count):
    if count & (count - 1):
        return lax.psum(values, axis)
    step = 1
    while step < count:
        pairs = [(index, index ^ step) for index in range(count)]
        values = values + lax.ppermute(values, axis, pairs)
        step *= 2
    return values


def inner_sum(left_rows, right_rows):
    return jnp.einsum("an,bn->ab", left_rows, right_rows, preferred_element_type=jnp.float32)


def remove_locked(gram_sums, trial_re, trial_im, locked_re, locked_im):
    gram_a, gram_q, proj_re, proj_im = gram_sums
    kept_count = gram_a.shape[0]
    gram = jnp.concatenate(
        [jnp.concatenate([gram_a, gram_q], axis=1), jnp.concatenate([gram_q.T, gram_a], axis=1)],
        axis=0,
    )
    rhs_both = jnp.concatenate([proj_re, proj_im], axis=0)
    lower = jnp.linalg.cholesky(gram)
    middle = lax.linalg.triangular_solve(lower, rhs_both, left_side=True, lower=True)
    coef = lax.linalg.triangular_solve(lower, middle, left_side=True, lower=True, transpose_a=True)
    coef_one = coef[:kept_count]
    coef_two = coef[kept_count:]
    locked_re32 = locked_re.astype(jnp.float32)
    locked_im32 = locked_im.astype(jnp.float32)
    out_re = (
        trial_re.astype(jnp.float32)
        - jnp.einsum("ab,an->bn", coef_one, locked_re32, precision=highest)
        + jnp.einsum("ab,an->bn", coef_two, locked_im32, precision=highest)
    )
    out_im = (
        trial_im.astype(jnp.float32)
        - jnp.einsum("ab,an->bn", coef_one, locked_im32, precision=highest)
        - jnp.einsum("ab,an->bn", coef_two, locked_re32, precision=highest)
    )
    return (out_re, out_im)


def solve_coef(gram_sums):
    gram_a, gram_q, proj_re, proj_im = gram_sums
    gram = jnp.concatenate(
        [jnp.concatenate([gram_a, gram_q], axis=1), jnp.concatenate([gram_q.T, gram_a], axis=1)],
        axis=0,
    )
    rhs_both = jnp.concatenate([proj_re, proj_im], axis=0)
    lower = jnp.linalg.cholesky(gram)
    middle = lax.linalg.triangular_solve(lower, rhs_both, left_side=True, lower=True)
    return lax.linalg.triangular_solve(lower, middle, left_side=True, lower=True, transpose_a=True)


def maxwell_pass(chunks, waves, inv_diag, inv_corr, to_space_fn, to_spectrum_fn):
    space = jnp.concatenate([transform(to_space_fn(chunk), 2, 1.0) for chunk in chunks], axis=2)
    weighted = apply_tensor(space, inv_diag, inv_corr)
    homes = []
    for comp in range(weighted.shape[2]):
        home = to_spectrum_fn(transform(weighted[:, :, comp : comp + 1], 2, -1.0))
        home = transform(home, 3, -1.0)
        homes.append(transform(home, 4, -1.0))
    home = jnp.concatenate(homes, axis=2)
    return (curl_times_i(waves, home), space, weighted)


def per_device(wide_count, trial_bands, locked_bands, inv_diag, inv_corr):
    band_count = trial_bands.shape[0]
    kept_count = locked_bands.shape[0]
    local_x = trial_bands.shape[3]
    grid_len = trial_bands.shape[4]
    rows = jnp.concatenate(
        [locked_bands.reshape((2 * kept_count,) + locked_bands.shape[2:]),
         trial_bands.reshape((2 * band_count,) + trial_bands.shape[2:])],
        axis=0,
    )
    pairs = jnp.einsum("icxyz,jcxyz->ij", rows, rows, preferred_element_type=jnp.float32)
    pairs = butterfly_sum(pairs, "wide", wide_count)
    lk = pairs[: 2 * kept_count, : 2 * kept_count].reshape(kept_count, 2, kept_count, 2)
    lt = pairs[: 2 * kept_count, 2 * kept_count :].reshape(kept_count, 2, band_count, 2)
    gram_a = lk[:, 0, :, 0] + lk[:, 1, :, 1]
    gram_q = lk[:, 1, :, 0] - lk[:, 0, :, 1]
    proj_re = lt[:, 0, :, 0] + lt[:, 1, :, 1]
    proj_im = lt[:, 0, :, 1] - lt[:, 1, :, 0]
    gram_sums = (gram_a, gram_q, proj_re, proj_im)
    coef = solve_coef(gram_sums)
    start_x = lax.axis_index("wide") * local_x
    full_axis = jnp.arange(grid_len, dtype=jnp.int32)
    wave_x = signed_wave(start_x + jnp.arange(local_x, dtype=jnp.int32), grid_len)
    wave_full = signed_wave(full_axis, grid_len)
    waves = (wave_x, wave_full, wave_full)

    def exchange_rows(field, split_dim, keep_dim):
        parts, bands, comps = field.shape[0], field.shape[1], field.shape[2]
        order = (split_dim, 1, 2, keep_dim, 0, 5)
        moved = jnp.transpose(field, order).reshape(wide_count, -1)
        moved = lax.all_to_all(moved, "wide", split_axis=0, concat_axis=0, tiled=True)
        local_split = field.shape[split_dim] // wide_count
        moved = moved.reshape(
            wide_count, local_split, bands, comps, field.shape[keep_dim], parts, field.shape[5]
        )
        return moved

    def send_out_one(field):
        moved = exchange_rows(field, 4, 3)
        moved = jnp.transpose(moved, (5, 2, 3, 0, 4, 1, 6))
        shape = moved.shape
        return moved.reshape(shape[0], shape[1], shape[2], shape[3] * shape[4], shape[5], shape[6])

    def send_home_one(field):
        moved = exchange_rows(field, 3, 4)
        moved = jnp.transpose(moved, (5, 2, 3, 1, 0, 4, 6))
        shape = moved.shape
        return moved.reshape(shape[0], shape[1], shape[2], shape[3], shape[4] * shape[5], shape[6])

    chunks = [front_pass((comp,), coef.T, wave_x, trial_bands, locked_bands) for comp in range(3)]
    results = [maxwell_pass(chunks, waves, inv_diag, inv_corr, send_out_one, send_home_one)]
    applied_st, space, weighted = [
        jnp.concatenate([entry[slot] for entry in results], axis=1) for slot in range(3)
    ]
    applied = jnp.stack([applied_st[0], applied_st[1]], axis=1).astype(jnp.bfloat16)
    scale_all = 1.0 / float(grid_len * grid_len * grid_len)
    left_re = space[0].reshape(band_count, -1)
    left_im = space[1].reshape(band_count, -1)
    right_re = weighted[0].reshape(band_count, -1)
    right_im = weighted[1].reshape(band_count, -1)
    part_re = jnp.einsum("an,bn->ab", left_re, right_re, precision=highest) + jnp.einsum(
        "an,bn->ab", left_im, right_im, precision=highest
    )
    part_im = jnp.einsum("an,bn->ab", left_re, right_im, precision=highest) - jnp.einsum(
        "an,bn->ab", left_im, right_re, precision=highest
    )
    total_re, total_im = butterfly_sum(jnp.stack([part_re, part_im], axis=0), "wide", wide_count)
    rayleigh = jnp.stack([total_re * scale_all, total_im * scale_all], axis=0)
    return (applied, rayleigh)


def solution(mesh):
    in_specs = (
        P("groups", None, None, "wide", None, None),
        P("groups", None, None, "wide", None, None),
        P("groups", None, "wide", None),
        P("groups", None, "wide", None),
    )
    out_specs = (P("groups", None, None, "wide", None, None), P("groups", None, None))
    wide_count = mesh.shape["wide"]
    return jax.shard_map(
        functools.partial(per_device, wide_count), mesh=mesh, in_specs=in_specs, out_specs=out_specs, check_vma=False
    )
```

```python
import functools
import math

import ml_dtypes
import numpy as np

import jax
import jax.numpy as jnp
from jax import lax
from jax.sharding import PartitionSpec as P
from jax.experimental import pallas as pl
from jax.experimental.pallas import tpu as pltpu

highest = lax.Precision.HIGHEST
three_pass = lax.Precision.HIGH


def signed_wave(indices, length):
    shifted = jnp.where(indices < length // 2, indices, indices - length)
    return shifted.astype(jnp.float32) / (length / 2.0)


def cross_wave(wave_x, wave_y, wave_z, vectors):
    comp_x = vectors[..., 0, :, :, :]
    comp_y = vectors[..., 1, :, :, :]
    comp_z = vectors[..., 2, :, :, :]
    along_x = wave_x[:, None, None]
    along_y = wave_y[None, :, None]
    along_z = wave_z[None, None, :]
    return jnp.stack(
        [
            along_y * comp_z - along_z * comp_y,
            along_z * comp_x - along_x * comp_z,
            along_x * comp_y - along_y * comp_x,
        ],
        axis=-4,
    )


def curl_times_i(waves, stacked):
    wave_x, wave_y, wave_z = waves
    return jnp.stack(
        [
            -cross_wave(wave_x, wave_y, wave_z, stacked[1]),
            cross_wave(wave_x, wave_y, wave_z, stacked[0]),
        ],
        axis=0,
    )


def apply_tensor(vectors, inv_diag, inv_corr):
    coupling_xy = inv_corr[0] * jnp.sqrt(inv_diag[0] * inv_diag[1])
    coupling_xz = inv_corr[1] * jnp.sqrt(inv_diag[0] * inv_diag[2])
    coupling_yz = inv_corr[2] * jnp.sqrt(inv_diag[1] * inv_diag[2])
    comp_x = vectors[..., 0, :, :, :]
    comp_y = vectors[..., 1, :, :, :]
    comp_z = vectors[..., 2, :, :, :]
    out_x = inv_diag[0] * comp_x + coupling_xy * comp_y + coupling_xz * comp_z
    out_y = coupling_xy * comp_x + inv_diag[1] * comp_y + coupling_yz * comp_z
    out_z = coupling_xz * comp_x + coupling_yz * comp_y + inv_diag[2] * comp_z
    return jnp.stack([out_x, out_y, out_z], axis=-4)


def complex_table(length, orient):
    indices = jnp.arange(length, dtype=jnp.int32)
    phases = indices[:, None] * indices[None, :] % length
    angles = phases.astype(jnp.float32) * (2.0 * math.pi / length)
    norm_factor = 1.0 / math.sqrt(length)
    cos_table = jnp.cos(angles) * norm_factor
    sin_table = jnp.sin(angles) * norm_factor * orient
    return jnp.stack(
        [jnp.stack([cos_table, sin_table], axis=0), jnp.stack([-sin_table, cos_table], axis=0)],
        axis=0,
    )


def transform(stacked, axis_dim, orient):
    table = complex_table(stacked.shape[axis_dim + 1], orient)
    if axis_dim == 2:
        return jnp.einsum("pbckyz,pqkn->qbcnyz", stacked, table, precision=three_pass)
    if axis_dim == 3:
        return jnp.einsum("pbcxkz,pqkn->qbcxnz", stacked, table, precision=three_pass)
    return jnp.einsum("pbcxyk,pqkn->qbcxyn", stacked, table, precision=three_pass)


def split_hi_lo(values):
    scaled = values * 65537.0
    top = scaled - (scaled - values)
    return top.astype(jnp.bfloat16), (values - top).astype(jnp.bfloat16)


def dot_right(values, table_hi, table_lo):
    high, low = split_hi_lo(values)
    f32 = jnp.float32
    return (
        jnp.dot(high, table_hi, preferred_element_type=f32)
        + jnp.dot(low, table_hi, preferred_element_type=f32)
        + jnp.dot(high, table_lo, preferred_element_type=f32)
    )


def dot_left(table_hi, table_lo, values):
    high, low = split_hi_lo(values)
    f32 = jnp.float32
    return (
        jnp.dot(table_hi, high, preferred_element_type=f32)
        + jnp.dot(table_hi, low, preferred_element_type=f32)
        + jnp.dot(table_lo, high, preferred_element_type=f32)
    )


def front_kernel(comps, coef_ref, qx_ref, trial_ref, locked_ref, chi_ref, clo_ref, shi_ref, slo_ref, out_ref):
    band = pl.program_id(0)
    plane = pl.program_id(1)
    kept = locked_ref.shape[0]
    size = trial_ref.shape[-1]
    f32 = jnp.float32
    first = [coef_ref[band, k] for k in range(kept)]
    second = [coef_ref[band, kept + k] for k in range(kept)]
    needed = sorted({(c + 1) % 3 for c in comps} | {(c + 2) % 3 for c in comps})
    part_re = {}
    part_im = {}
    for comp in needed:
        acc_re = trial_ref[0, 0, comp, 0].astype(f32)
        acc_im = trial_ref[0, 1, comp, 0].astype(f32)
        for k in range(kept):
            l_re = locked_ref[k, 0, comp, 0].astype(f32)
            l_im = locked_ref[k, 1, comp, 0].astype(f32)
            acc_re = acc_re - first[k] * l_re + second[k] * l_im
            acc_im = acc_im - first[k] * l_im - second[k] * l_re
        part_re[comp] = acc_re
        part_im[comp] = acc_im
    rows = lax.broadcasted_iota(jnp.int32, (size, 1), 0)
    cols = lax.broadcasted_iota(jnp.int32, (1, size), 1)
    half = size // 2
    wave_y = jnp.where(rows < half, rows, rows - size).astype(f32) / (size / 2.0)
    wave_z = jnp.where(cols < half, cols, cols - size).astype(f32) / (size / 2.0)
    waves = (qx_ref[plane], wave_y, wave_z)
    c_hi = chi_ref[...]
    c_lo = clo_ref[...]
    s_hi = shi_ref[...]
    s_lo = slo_ref[...]
    for slot, comp in enumerate(comps):
        a = (comp + 1) % 3
        b = (comp + 2) % 3
        cur_re = -(waves[a] * part_im[b] - waves[b] * part_im[a])
        cur_im = waves[a] * part_re[b] - waves[b] * part_re[a]
        z_re = dot_right(cur_re, c_hi, c_lo) - dot_right(cur_im, s_hi, s_lo)
        z_im = dot_right(cur_re, s_hi, s_lo) + dot_right(cur_im, c_hi, c_lo)
        y_re = dot_left(c_hi, c_lo, z_re) - dot_left(s_hi, s_lo, z_im)
        y_im = dot_left(s_hi, s_lo, z_re) + dot_left(c_hi, c_lo, z_im)
        out_ref[0, 0, slot, 0] = y_re
        out_ref[1, 0, slot, 0] = y_im


def numpy_split(table):
    full = table.astype(np.float32)
    high = full.astype(ml_dtypes.bfloat16)
    low = (full - high.astype(np.float32)).astype(ml_dtypes.bfloat16)
    return jnp.asarray(high), jnp.asarray(low)


def dft_tables(length, orient):
    indices = np.arange(length, dtype=np.int64)
    phases = indices[:, None] * indices[None, :] % length
    angles = phases.astype(np.float64) * (2.0 * math.pi / length)
    norm_factor = 1.0 / math.sqrt(length)
    c_hi, c_lo = numpy_split(np.cos(angles) * norm_factor)
    s_hi, s_lo = numpy_split(np.sin(angles) * norm_factor * orient)
    return c_hi, c_lo, s_hi, s_lo


def front_pass(comps, coef_rows, wave_x, trial_bands, locked_bands):
    band_count, _, _, local_x, size, _ = trial_bands.shape
    kept = locked_bands.shape[0]
    tables = dft_tables(size, 1.0)
    smem = pl.BlockSpec(memory_space=pltpu.SMEM)
    table_spec = pl.BlockSpec((size, size), lambda b, x: (0, 0))
    width = len(comps)
    return pl.pallas_call(
        functools.partial(front_kernel, comps),
        grid=(band_count, local_x),
        in_specs=[
            smem,
            smem,
            pl.BlockSpec((1, 2, 3, 1, size, size), lambda b, x: (b, 0, 0, x, 0, 0)),
            pl.BlockSpec((kept, 2, 3, 1, size, size), lambda b, x: (0, 0, 0, x, 0, 0)),
            table_spec,
            table_spec,
            table_spec,
            table_spec,
        ],
        out_specs=pl.BlockSpec((2, 1, width, 1, size, size), lambda b, x: (0, b, 0, x, 0, 0)),
        out_shape=jax.ShapeDtypeStruct((2, band_count, width, local_x, size, size), jnp.float32),
    )(coef_rows, wave_x, trial_bands, locked_bands, *tables)


def butterfly_sum(values, axis, count):
    if count & (count - 1):
        return lax.psum(values, axis)
    step = 1
    while step < count:
        pairs = [(index, index ^ step) for index in range(count)]
        values = values + lax.ppermute(values, axis, pairs)
        step *= 2
    return values


def inner_sum(left_rows, right_rows):
    return jnp.einsum("an,bn->ab", left_rows, right_rows, preferred_element_type=jnp.float32)


def remove_locked(gram_sums, trial_re, trial_im, locked_re, locked_im):
    gram_a, gram_q, proj_re, proj_im = gram_sums
    kept_count = gram_a.shape[0]
    gram = jnp.concatenate(
        [jnp.concatenate([gram_a, gram_q], axis=1), jnp.concatenate([gram_q.T, gram_a], axis=1)],
        axis=0,
    )
    rhs_both = jnp.concatenate([proj_re, proj_im], axis=0)
    lower = jnp.linalg.cholesky(gram)
    middle = lax.linalg.triangular_solve(lower, rhs_both, left_side=True, lower=True)
    coef = lax.linalg.triangular_solve(lower, middle, left_side=True, lower=True, transpose_a=True)
    coef_one = coef[:kept_count]
    coef_two = coef[kept_count:]
    locked_re32 = locked_re.astype(jnp.float32)
    locked_im32 = locked_im.astype(jnp.float32)
    out_re = (
        trial_re.astype(jnp.float32)
        - jnp.einsum("ab,an->bn", coef_one, locked_re32, precision=highest)
        + jnp.einsum("ab,an->bn", coef_two, locked_im32, precision=highest)
    )
    out_im = (
        trial_im.astype(jnp.float32)
        - jnp.einsum("ab,an->bn", coef_one, locked_im32, precision=highest)
        - jnp.einsum("ab,an->bn", coef_two, locked_re32, precision=highest)
    )
    return (out_re, out_im)


def solve_coef(gram_sums):
    gram_a, gram_q, proj_re, proj_im = gram_sums
    gram = jnp.concatenate(
        [jnp.concatenate([gram_a, gram_q], axis=1), jnp.concatenate([gram_q.T, gram_a], axis=1)],
        axis=0,
    )
    rhs_both = jnp.concatenate([proj_re, proj_im], axis=0)
    lower = jnp.linalg.cholesky(gram)
    middle = lax.linalg.triangular_solve(lower, rhs_both, left_side=True, lower=True)
    return lax.linalg.triangular_solve(lower, middle, left_side=True, lower=True, transpose_a=True)


def maxwell_pass(chunks, waves, inv_diag, inv_corr, to_space_fn, to_spectrum_fn):
    space = jnp.concatenate([transform(to_space_fn(chunk), 2, 1.0) for chunk in chunks], axis=2)
    weighted = apply_tensor(space, inv_diag, inv_corr)
    homes = []
    for comp in range(weighted.shape[2]):
        home = to_spectrum_fn(transform(weighted[:, :, comp : comp + 1], 2, -1.0))
        home = transform(home, 3, -1.0)
        homes.append(transform(home, 4, -1.0))
    home = jnp.concatenate(homes, axis=2)
    return (curl_times_i(waves, home), space, weighted)


def per_device(wide_count, trial_bands, locked_bands, inv_diag, inv_corr):
    band_count = trial_bands.shape[0]
    kept_count = locked_bands.shape[0]
    local_x = trial_bands.shape[3]
    grid_len = trial_bands.shape[4]
    rows = jnp.concatenate(
        [locked_bands.reshape((2 * kept_count,) + locked_bands.shape[2:]),
         trial_bands.reshape((2 * band_count,) + trial_bands.shape[2:])],
        axis=0,
    )
    pairs = jnp.einsum("icxyz,jcxyz->ij", rows, rows, preferred_element_type=jnp.float32)
    pairs = butterfly_sum(pairs, "wide", wide_count)
    lk = pairs[: 2 * kept_count, : 2 * kept_count].reshape(kept_count, 2, kept_count, 2)
    lt = pairs[: 2 * kept_count, 2 * kept_count :].reshape(kept_count, 2, band_count, 2)
    gram_a = lk[:, 0, :, 0] + lk[:, 1, :, 1]
    gram_q = lk[:, 1, :, 0] - lk[:, 0, :, 1]
    proj_re = lt[:, 0, :, 0] + lt[:, 1, :, 1]
    proj_im = lt[:, 0, :, 1] - lt[:, 1, :, 0]
    gram_sums = (gram_a, gram_q, proj_re, proj_im)
    coef = solve_coef(gram_sums)
    start_x = lax.axis_index("wide") * local_x
    full_axis = jnp.arange(grid_len, dtype=jnp.int32)
    wave_x = signed_wave(start_x + jnp.arange(local_x, dtype=jnp.int32), grid_len)
    wave_full = signed_wave(full_axis, grid_len)
    waves = (wave_x, wave_full, wave_full)

    def exchange_rows(field, split_dim, keep_dim):
        parts, bands, comps = field.shape[0], field.shape[1], field.shape[2]
        order = (split_dim, 1, 2, keep_dim, 0, 5)
        moved = jnp.transpose(field, order).reshape(wide_count, -1, 128)
        moved = lax.all_to_all(moved, "wide", split_axis=0, concat_axis=0, tiled=True)
        local_split = field.shape[split_dim] // wide_count
        moved = moved.reshape(
            wide_count, local_split, bands, comps, field.shape[keep_dim], parts, field.shape[5]
        )
        return moved

    def send_out_one(field):
        moved = exchange_rows(field, 4, 3)
        moved = jnp.transpose(moved, (5, 2, 3, 0, 4, 1, 6))
        shape = moved.shape
        return moved.reshape(shape[0], shape[1], shape[2], shape[3] * shape[4], shape[5], shape[6])

    def send_home_one(field):
        moved = exchange_rows(field, 3, 4)
        moved = jnp.transpose(moved, (5, 2, 3, 1, 0, 4, 6))
        shape = moved.shape
        return moved.reshape(shape[0], shape[1], shape[2], shape[3], shape[4] * shape[5], shape[6])

    chunks = [front_pass((comp,), coef.T, wave_x, trial_bands, locked_bands) for comp in range(3)]
    results = [maxwell_pass(chunks, waves, inv_diag, inv_corr, send_out_one, send_home_one)]
    applied_st, space, weighted = [
        jnp.concatenate([entry[slot] for entry in results], axis=1) for slot in range(3)
    ]
    applied = jnp.stack([applied_st[0], applied_st[1]], axis=1).astype(jnp.bfloat16)
    scale_all = 1.0 / float(grid_len * grid_len * grid_len)
    left_re = space[0].reshape(band_count, -1)
    left_im = space[1].reshape(band_count, -1)
    right_re = weighted[0].reshape(band_count, -1)
    right_im = weighted[1].reshape(band_count, -1)
    part_re = jnp.einsum("an,bn->ab", left_re, right_re, precision=highest) + jnp.einsum(
        "an,bn->ab", left_im, right_im, precision=highest
    )
    part_im = jnp.einsum("an,bn->ab", left_re, right_im, precision=highest) - jnp.einsum(
        "an,bn->ab", left_im, right_re, precision=highest
    )
    total_re, total_im = butterfly_sum(jnp.stack([part_re, part_im], axis=0), "wide", wide_count)
    rayleigh = jnp.stack([total_re * scale_all, total_im * scale_all], axis=0)
    return (applied, rayleigh)


def solution(mesh):
    in_specs = (
        P("groups", None, None, "wide", None, None),
        P("groups", None, None, "wide", None, None),
        P("groups", None, "wide", None),
        P("groups", None, "wide", None),
    )
    out_specs = (P("groups", None, None, "wide", None, None), P("groups", None, None))
    wide_count = mesh.shape["wide"]
    return jax.shard_map(
        functools.partial(per_device, wide_count), mesh=mesh, in_specs=in_specs, out_specs=out_specs, check_vma=False
    )
```

```python
import functools
import math

import ml_dtypes
import numpy as np

import jax
import jax.numpy as jnp
from jax import lax
from jax.sharding import PartitionSpec as P
from jax.experimental import pallas as pl
from jax.experimental.pallas import tpu as pltpu

highest = lax.Precision.HIGHEST
three_pass = lax.Precision.HIGH


def signed_wave(indices, length):
    shifted = jnp.where(indices < length // 2, indices, indices - length)
    return shifted.astype(jnp.float32) / (length / 2.0)


def cross_wave(wave_x, wave_y, wave_z, vectors):
    comp_x = vectors[..., 0, :, :, :]
    comp_y = vectors[..., 1, :, :, :]
    comp_z = vectors[..., 2, :, :, :]
    along_x = wave_x[:, None, None]
    along_y = wave_y[None, :, None]
    along_z = wave_z[None, None, :]
    return jnp.stack(
        [
            along_y * comp_z - along_z * comp_y,
            along_z * comp_x - along_x * comp_z,
            along_x * comp_y - along_y * comp_x,
        ],
        axis=-4,
    )


def curl_times_i(waves, stacked):
    wave_x, wave_y, wave_z = waves
    return jnp.stack(
        [
            -cross_wave(wave_x, wave_y, wave_z, stacked[1]),
            cross_wave(wave_x, wave_y, wave_z, stacked[0]),
        ],
        axis=0,
    )


def apply_tensor(vectors, inv_diag, inv_corr):
    coupling_xy = inv_corr[0] * jnp.sqrt(inv_diag[0] * inv_diag[1])
    coupling_xz = inv_corr[1] * jnp.sqrt(inv_diag[0] * inv_diag[2])
    coupling_yz = inv_corr[2] * jnp.sqrt(inv_diag[1] * inv_diag[2])
    comp_x = vectors[..., 0, :, :, :]
    comp_y = vectors[..., 1, :, :, :]
    comp_z = vectors[..., 2, :, :, :]
    out_x = inv_diag[0] * comp_x + coupling_xy * comp_y + coupling_xz * comp_z
    out_y = coupling_xy * comp_x + inv_diag[1] * comp_y + coupling_yz * comp_z
    out_z = coupling_xz * comp_x + coupling_yz * comp_y + inv_diag[2] * comp_z
    return jnp.stack([out_x, out_y, out_z], axis=-4)


def complex_table(length, orient):
    indices = jnp.arange(length, dtype=jnp.int32)
    phases = indices[:, None] * indices[None, :] % length
    angles = phases.astype(jnp.float32) * (2.0 * math.pi / length)
    norm_factor = 1.0 / math.sqrt(length)
    cos_table = jnp.cos(angles) * norm_factor
    sin_table = jnp.sin(angles) * norm_factor * orient
    return jnp.stack(
        [jnp.stack([cos_table, sin_table], axis=0), jnp.stack([-sin_table, cos_table], axis=0)],
        axis=0,
    )


def transform(stacked, axis_dim, orient):
    table = complex_table(stacked.shape[axis_dim + 1], orient)
    if axis_dim == 2:
        return jnp.einsum("pbckyz,pqkn->qbcnyz", stacked, table, precision=three_pass)
    if axis_dim == 3:
        return jnp.einsum("pbcxkz,pqkn->qbcxnz", stacked, table, precision=three_pass)
    return jnp.einsum("pbcxyk,pqkn->qbcxyn", stacked, table, precision=three_pass)


def split_hi_lo(values):
    scaled = values * 65537.0
    top = scaled - (scaled - values)
    return top.astype(jnp.bfloat16), (values - top).astype(jnp.bfloat16)


def dot_right(values, table_hi, table_lo):
    high, low = split_hi_lo(values)
    f32 = jnp.float32
    return (
        jnp.dot(high, table_hi, preferred_element_type=f32)
        + jnp.dot(low, table_hi, preferred_element_type=f32)
        + jnp.dot(high, table_lo, preferred_element_type=f32)
    )


def dot_left(table_hi, table_lo, values):
    high, low = split_hi_lo(values)
    f32 = jnp.float32
    return (
        jnp.dot(table_hi, high, preferred_element_type=f32)
        + jnp.dot(table_hi, low, preferred_element_type=f32)
        + jnp.dot(table_lo, high, preferred_element_type=f32)
    )


def front_kernel(comps, coef_ref, qx_ref, trial_ref, locked_ref, chi_ref, clo_ref, shi_ref, slo_ref, out_ref):
    band = pl.program_id(0)
    plane = pl.program_id(1)
    kept = locked_ref.shape[0]
    size = trial_ref.shape[-1]
    f32 = jnp.float32
    first = [coef_ref[band, k] for k in range(kept)]
    second = [coef_ref[band, kept + k] for k in range(kept)]
    needed = sorted({(c + 1) % 3 for c in comps} | {(c + 2) % 3 for c in comps})
    part_re = {}
    part_im = {}
    for comp in needed:
        acc_re = trial_ref[0, 0, comp, 0].astype(f32)
        acc_im = trial_ref[0, 1, comp, 0].astype(f32)
        for k in range(kept):
            l_re = locked_ref[k, 0, comp, 0].astype(f32)
            l_im = locked_ref[k, 1, comp, 0].astype(f32)
            acc_re = acc_re - first[k] * l_re + second[k] * l_im
            acc_im = acc_im - first[k] * l_im - second[k] * l_re
        part_re[comp] = acc_re
        part_im[comp] = acc_im
    rows = lax.broadcasted_iota(jnp.int32, (size, 1), 0)
    cols = lax.broadcasted_iota(jnp.int32, (1, size), 1)
    half = size // 2
    wave_y = jnp.where(rows < half, rows, rows - size).astype(f32) / (size / 2.0)
    wave_z = jnp.where(cols < half, cols, cols - size).astype(f32) / (size / 2.0)
    waves = (qx_ref[plane], wave_y, wave_z)
    c_hi = chi_ref[...]
    c_lo = clo_ref[...]
    s_hi = shi_ref[...]
    s_lo = slo_ref[...]
    for slot, comp in enumerate(comps):
        a = (comp + 1) % 3
        b = (comp + 2) % 3
        cur_re = -(waves[a] * part_im[b] - waves[b] * part_im[a])
        cur_im = waves[a] * part_re[b] - waves[b] * part_re[a]
        z_re = dot_right(cur_re, c_hi, c_lo) - dot_right(cur_im, s_hi, s_lo)
        z_im = dot_right(cur_re, s_hi, s_lo) + dot_right(cur_im, c_hi, c_lo)
        y_re = dot_left(c_hi, c_lo, z_re) - dot_left(s_hi, s_lo, z_im)
        y_im = dot_left(s_hi, s_lo, z_re) + dot_left(c_hi, c_lo, z_im)
        out_ref[0, 0, slot, 0] = y_re
        out_ref[1, 0, slot, 0] = y_im


def numpy_split(table):
    full = table.astype(np.float32)
    high = full.astype(ml_dtypes.bfloat16)
    low = (full - high.astype(np.float32)).astype(ml_dtypes.bfloat16)
    return jnp.asarray(high), jnp.asarray(low)


def dft_tables(length, orient):
    indices = np.arange(length, dtype=np.int64)
    phases = indices[:, None] * indices[None, :] % length
    angles = phases.astype(np.float64) * (2.0 * math.pi / length)
    norm_factor = 1.0 / math.sqrt(length)
    c_hi, c_lo = numpy_split(np.cos(angles) * norm_factor)
    s_hi, s_lo = numpy_split(np.sin(angles) * norm_factor * orient)
    return c_hi, c_lo, s_hi, s_lo


def front_pass(comps, coef_rows, wave_x, trial_bands, locked_bands):
    band_count, _, _, local_x, size, _ = trial_bands.shape
    kept = locked_bands.shape[0]
    tables = dft_tables(size, 1.0)
    smem = pl.BlockSpec(memory_space=pltpu.SMEM)
    table_spec = pl.BlockSpec((size, size), lambda b, x: (0, 0))
    width = len(comps)
    return pl.pallas_call(
        functools.partial(front_kernel, comps),
        grid=(band_count, local_x),
        in_specs=[
            smem,
            smem,
            pl.BlockSpec((1, 2, 3, 1, size, size), lambda b, x: (b, 0, 0, x, 0, 0)),
            pl.BlockSpec((kept, 2, 3, 1, size, size), lambda b, x: (0, 0, 0, x, 0, 0)),
            table_spec,
            table_spec,
            table_spec,
            table_spec,
        ],
        out_specs=pl.BlockSpec((2, 1, width, 1, size, size), lambda b, x: (0, b, 0, x, 0, 0)),
        out_shape=jax.ShapeDtypeStruct((2, band_count, width, local_x, size, size), jnp.float32),
    )(coef_rows, wave_x, trial_bands, locked_bands, *tables)


def butterfly_sum(values, axis, count):
    if count & (count - 1):
        return lax.psum(values, axis)
    step = 1
    while step < count:
        pairs = [(index, index ^ step) for index in range(count)]
        values = values + lax.ppermute(values, axis, pairs)
        step *= 2
    return values


def inner_sum(left_rows, right_rows):
    return jnp.einsum("an,bn->ab", left_rows, right_rows, preferred_element_type=jnp.float32)


def remove_locked(gram_sums, trial_re, trial_im, locked_re, locked_im):
    gram_a, gram_q, proj_re, proj_im = gram_sums
    kept_count = gram_a.shape[0]
    gram = jnp.concatenate(
        [jnp.concatenate([gram_a, gram_q], axis=1), jnp.concatenate([gram_q.T, gram_a], axis=1)],
        axis=0,
    )
    rhs_both = jnp.concatenate([proj_re, proj_im], axis=0)
    lower = jnp.linalg.cholesky(gram)
    middle = lax.linalg.triangular_solve(lower, rhs_both, left_side=True, lower=True)
    coef = lax.linalg.triangular_solve(lower, middle, left_side=True, lower=True, transpose_a=True)
    coef_one = coef[:kept_count]
    coef_two = coef[kept_count:]
    locked_re32 = locked_re.astype(jnp.float32)
    locked_im32 = locked_im.astype(jnp.float32)
    out_re = (
        trial_re.astype(jnp.float32)
        - jnp.einsum("ab,an->bn", coef_one, locked_re32, precision=highest)
        + jnp.einsum("ab,an->bn", coef_two, locked_im32, precision=highest)
    )
    out_im = (
        trial_im.astype(jnp.float32)
        - jnp.einsum("ab,an->bn", coef_one, locked_im32, precision=highest)
        - jnp.einsum("ab,an->bn", coef_two, locked_re32, precision=highest)
    )
    return (out_re, out_im)


def solve_coef(gram_sums):
    gram_a, gram_q, proj_re, proj_im = gram_sums
    gram = jnp.concatenate(
        [jnp.concatenate([gram_a, gram_q], axis=1), jnp.concatenate([gram_q.T, gram_a], axis=1)],
        axis=0,
    )
    rhs_both = jnp.concatenate([proj_re, proj_im], axis=0)
    lower = jnp.linalg.cholesky(gram)
    middle = lax.linalg.triangular_solve(lower, rhs_both, left_side=True, lower=True)
    return lax.linalg.triangular_solve(lower, middle, left_side=True, lower=True, transpose_a=True)


def maxwell_pass(chunks, waves, inv_diag, inv_corr, to_space_fn, to_spectrum_fn):
    space = jnp.concatenate([transform(to_space_fn(chunk), 2, 1.0) for chunk in chunks], axis=2)
    weighted = apply_tensor(space, inv_diag, inv_corr)
    homes = []
    for comp in range(weighted.shape[2]):
        source = transform(weighted[:, :, comp : comp + 1], 2, -1.0)
        if comp >= 2:
            source, _ = lax.optimization_barrier((source, homes[comp - 2]))
        home = to_spectrum_fn(source)
        home = transform(home, 3, -1.0)
        homes.append(transform(home, 4, -1.0))
    home = jnp.concatenate(homes, axis=2)
    return (curl_times_i(waves, home), space, weighted)


def per_device(wide_count, trial_bands, locked_bands, inv_diag, inv_corr):
    band_count = trial_bands.shape[0]
    kept_count = locked_bands.shape[0]
    local_x = trial_bands.shape[3]
    grid_len = trial_bands.shape[4]
    rows = jnp.concatenate(
        [locked_bands.reshape((2 * kept_count,) + locked_bands.shape[2:]),
         trial_bands.reshape((2 * band_count,) + trial_bands.shape[2:])],
        axis=0,
    )
    pairs = jnp.einsum("icxyz,jcxyz->ij", rows, rows, preferred_element_type=jnp.float32)
    pairs = butterfly_sum(pairs, "wide", wide_count)
    lk = pairs[: 2 * kept_count, : 2 * kept_count].reshape(kept_count, 2, kept_count, 2)
    lt = pairs[: 2 * kept_count, 2 * kept_count :].reshape(kept_count, 2, band_count, 2)
    gram_a = lk[:, 0, :, 0] + lk[:, 1, :, 1]
    gram_q = lk[:, 1, :, 0] - lk[:, 0, :, 1]
    proj_re = lt[:, 0, :, 0] + lt[:, 1, :, 1]
    proj_im = lt[:, 0, :, 1] - lt[:, 1, :, 0]
    gram_sums = (gram_a, gram_q, proj_re, proj_im)
    coef = solve_coef(gram_sums)
    start_x = lax.axis_index("wide") * local_x
    full_axis = jnp.arange(grid_len, dtype=jnp.int32)
    wave_x = signed_wave(start_x + jnp.arange(local_x, dtype=jnp.int32), grid_len)
    wave_full = signed_wave(full_axis, grid_len)
    waves = (wave_x, wave_full, wave_full)

    def exchange_rows(field, split_dim, keep_dim):
        parts, bands, comps = field.shape[0], field.shape[1], field.shape[2]
        order = (split_dim, 1, 2, keep_dim, 0, 5)
        moved = jnp.transpose(field, order).reshape(wide_count, -1, 128)
        moved = lax.all_to_all(moved, "wide", split_axis=0, concat_axis=0, tiled=True)
        local_split = field.shape[split_dim] // wide_count
        moved = moved.reshape(
            wide_count, local_split, bands, comps, field.shape[keep_dim], parts, field.shape[5]
        )
        return moved

    def send_out_one(field):
        moved = exchange_rows(field, 4, 3)
        moved = jnp.transpose(moved, (5, 2, 3, 0, 4, 1, 6))
        shape = moved.shape
        return moved.reshape(shape[0], shape[1], shape[2], shape[3] * shape[4], shape[5], shape[6])

    def send_home_one(field):
        moved = exchange_rows(field, 3, 4)
        moved = jnp.transpose(moved, (5, 2, 3, 1, 0, 4, 6))
        shape = moved.shape
        return moved.reshape(shape[0], shape[1], shape[2], shape[3], shape[4] * shape[5], shape[6])

    chunks = [front_pass((comp,), coef.T, wave_x, trial_bands, locked_bands) for comp in range(3)]
    results = [maxwell_pass(chunks, waves, inv_diag, inv_corr, send_out_one, send_home_one)]
    applied_st, space, weighted = [
        jnp.concatenate([entry[slot] for entry in results], axis=1) for slot in range(3)
    ]
    applied = jnp.stack([applied_st[0], applied_st[1]], axis=1).astype(jnp.bfloat16)
    scale_all = 1.0 / float(grid_len * grid_len * grid_len)
    left_re = space[0].reshape(band_count, -1)
    left_im = space[1].reshape(band_count, -1)
    right_re = weighted[0].reshape(band_count, -1)
    right_im = weighted[1].reshape(band_count, -1)
    part_re = jnp.einsum("an,bn->ab", left_re, right_re, precision=highest) + jnp.einsum(
        "an,bn->ab", left_im, right_im, precision=highest
    )
    part_im = jnp.einsum("an,bn->ab", left_re, right_im, precision=highest) - jnp.einsum(
        "an,bn->ab", left_im, right_re, precision=highest
    )
    total_re, total_im = butterfly_sum(jnp.stack([part_re, part_im], axis=0), "wide", wide_count)
    rayleigh = jnp.stack([total_re * scale_all, total_im * scale_all], axis=0)
    return (applied, rayleigh)


def solution(mesh):
    in_specs = (
        P("groups", None, None, "wide", None, None),
        P("groups", None, None, "wide", None, None),
        P("groups", None, "wide", None),
        P("groups", None, "wide", None),
    )
    out_specs = (P("groups", None, None, "wide", None, None), P("groups", None, None))
    wide_count = mesh.shape["wide"]
    return jax.shard_map(
        functools.partial(per_device, wide_count), mesh=mesh, in_specs=in_specs, out_specs=out_specs, check_vma=False
    )
```

```python
import functools
import math

import ml_dtypes
import numpy as np

import jax
import jax.numpy as jnp
from jax import lax
from jax.sharding import PartitionSpec as P
from jax.experimental import pallas as pl
from jax.experimental.pallas import tpu as pltpu

highest = lax.Precision.HIGHEST
three_pass = lax.Precision.HIGH


def signed_wave(indices, length):
    shifted = jnp.where(indices < length // 2, indices, indices - length)
    return shifted.astype(jnp.float32) / (length / 2.0)


def cross_wave(wave_x, wave_y, wave_z, vectors):
    comp_x = vectors[..., 0, :, :, :]
    comp_y = vectors[..., 1, :, :, :]
    comp_z = vectors[..., 2, :, :, :]
    along_x = wave_x[:, None, None]
    along_y = wave_y[None, :, None]
    along_z = wave_z[None, None, :]
    return jnp.stack(
        [
            along_y * comp_z - along_z * comp_y,
            along_z * comp_x - along_x * comp_z,
            along_x * comp_y - along_y * comp_x,
        ],
        axis=-4,
    )


def curl_times_i(waves, stacked):
    wave_x, wave_y, wave_z = waves
    return jnp.stack(
        [
            -cross_wave(wave_x, wave_y, wave_z, stacked[1]),
            cross_wave(wave_x, wave_y, wave_z, stacked[0]),
        ],
        axis=0,
    )


def apply_tensor(vectors, inv_diag, inv_corr):
    coupling_xy = inv_corr[0] * jnp.sqrt(inv_diag[0] * inv_diag[1])
    coupling_xz = inv_corr[1] * jnp.sqrt(inv_diag[0] * inv_diag[2])
    coupling_yz = inv_corr[2] * jnp.sqrt(inv_diag[1] * inv_diag[2])
    comp_x = vectors[..., 0, :, :, :]
    comp_y = vectors[..., 1, :, :, :]
    comp_z = vectors[..., 2, :, :, :]
    out_x = inv_diag[0] * comp_x + coupling_xy * comp_y + coupling_xz * comp_z
    out_y = coupling_xy * comp_x + inv_diag[1] * comp_y + coupling_yz * comp_z
    out_z = coupling_xz * comp_x + coupling_yz * comp_y + inv_diag[2] * comp_z
    return jnp.stack([out_x, out_y, out_z], axis=-4)


def complex_table(length, orient):
    indices = jnp.arange(length, dtype=jnp.int32)
    phases = indices[:, None] * indices[None, :] % length
    angles = phases.astype(jnp.float32) * (2.0 * math.pi / length)
    norm_factor = 1.0 / math.sqrt(length)
    cos_table = jnp.cos(angles) * norm_factor
    sin_table = jnp.sin(angles) * norm_factor * orient
    return jnp.stack(
        [jnp.stack([cos_table, sin_table], axis=0), jnp.stack([-sin_table, cos_table], axis=0)],
        axis=0,
    )


def transform(stacked, axis_dim, orient):
    table = complex_table(stacked.shape[axis_dim + 1], orient)
    if axis_dim == 2:
        return jnp.einsum("pbckyz,pqkn->qbcnyz", stacked, table, precision=three_pass)
    if axis_dim == 3:
        return jnp.einsum("pbcxkz,pqkn->qbcxnz", stacked, table, precision=three_pass)
    return jnp.einsum("pbcxyk,pqkn->qbcxyn", stacked, table, precision=three_pass)


def split_hi_lo(values):
    scaled = values * 65537.0
    top = scaled - (scaled - values)
    return top.astype(jnp.bfloat16), (values - top).astype(jnp.bfloat16)


def dot_right(values, table_hi, table_lo):
    high, low = split_hi_lo(values)
    f32 = jnp.float32
    return (
        jnp.dot(high, table_hi, preferred_element_type=f32)
        + jnp.dot(low, table_hi, preferred_element_type=f32)
        + jnp.dot(high, table_lo, preferred_element_type=f32)
    )


def dot_left(table_hi, table_lo, values):
    high, low = split_hi_lo(values)
    f32 = jnp.float32
    return (
        jnp.dot(table_hi, high, preferred_element_type=f32)
        + jnp.dot(table_hi, low, preferred_element_type=f32)
        + jnp.dot(table_lo, high, preferred_element_type=f32)
    )


def front_kernel(comps, coef_ref, qx_ref, trial_ref, locked_ref, chi_ref, clo_ref, shi_ref, slo_ref, out_ref):
    band = pl.program_id(0)
    plane = pl.program_id(1)
    kept = locked_ref.shape[0]
    size = trial_ref.shape[-1]
    f32 = jnp.float32
    first = [coef_ref[band, k] for k in range(kept)]
    second = [coef_ref[band, kept + k] for k in range(kept)]
    needed = sorted({(c + 1) % 3 for c in comps} | {(c + 2) % 3 for c in comps})
    part_re = {}
    part_im = {}
    for comp in needed:
        acc_re = trial_ref[0, 0, comp, 0].astype(f32)
        acc_im = trial_ref[0, 1, comp, 0].astype(f32)
        for k in range(kept):
            l_re = locked_ref[k, 0, comp, 0].astype(f32)
            l_im = locked_ref[k, 1, comp, 0].astype(f32)
            acc_re = acc_re - first[k] * l_re + second[k] * l_im
            acc_im = acc_im - first[k] * l_im - second[k] * l_re
        part_re[comp] = acc_re
        part_im[comp] = acc_im
    rows = lax.broadcasted_iota(jnp.int32, (size, 1), 0)
    cols = lax.broadcasted_iota(jnp.int32, (1, size), 1)
    half = size // 2
    wave_y = jnp.where(rows < half, rows, rows - size).astype(f32) / (size / 2.0)
    wave_z = jnp.where(cols < half, cols, cols - size).astype(f32) / (size / 2.0)
    waves = (qx_ref[plane], wave_y, wave_z)
    c_hi = chi_ref[...]
    c_lo = clo_ref[...]
    s_hi = shi_ref[...]
    s_lo = slo_ref[...]
    for slot, comp in enumerate(comps):
        a = (comp + 1) % 3
        b = (comp + 2) % 3
        cur_re = -(waves[a] * part_im[b] - waves[b] * part_im[a])
        cur_im = waves[a] * part_re[b] - waves[b] * part_re[a]
        z_re = dot_right(cur_re, c_hi, c_lo) - dot_right(cur_im, s_hi, s_lo)
        z_im = dot_right(cur_re, s_hi, s_lo) + dot_right(cur_im, c_hi, c_lo)
        y_re = dot_left(c_hi, c_lo, z_re) - dot_left(s_hi, s_lo, z_im)
        y_im = dot_left(s_hi, s_lo, z_re) + dot_left(c_hi, c_lo, z_im)
        out_ref[0, 0, slot, 0] = y_re
        out_ref[1, 0, slot, 0] = y_im


def numpy_split(table):
    full = table.astype(np.float32)
    high = full.astype(ml_dtypes.bfloat16)
    low = (full - high.astype(np.float32)).astype(ml_dtypes.bfloat16)
    return jnp.asarray(high), jnp.asarray(low)


def gram_kernel(groups, locked_ref, trial_ref, out_ref):
    step = pl.program_id(0)
    size = locked_ref.shape[-1]
    chunks = size // 8
    kept = locked_ref.shape[0]

    @pl.when(step == 0)
    def _():
        out_ref[...] = jnp.zeros_like(out_ref)

    def load(row, comp, chunk):
        start = pl.multiple_of(chunk * 8, 8)
        if row < 2 * kept:
            piece = locked_ref[row // 2, row % 2, comp, 0, pl.ds(start, 8), :]
        else:
            other = row - 2 * kept
            piece = trial_ref[other // 2, other % 2, comp, 0, pl.ds(start, 8), :]
        return piece.astype(jnp.float32)

    for group in groups:
        needed = sorted({i for _, i, _ in group} | {j for _, _, j in group})

        def body(index, accs, group=group, needed=needed):
            comp = index // chunks
            chunk = index % chunks
            values = {row: load(row, comp, chunk) for row in needed}
            return tuple(acc + values[i] * values[j] for acc, (_, i, j) in zip(accs, group))

        init = tuple(jnp.zeros((8, size), jnp.float32) for _ in group)
        accs = lax.fori_loop(0, 3 * chunks, body, init)
        for acc, (slot, _, _) in zip(accs, group):
            out_ref[slot] += acc


def gram_pairs(kept, bands):
    rows = 2 * kept
    pairs = [(i, j) for i in range(rows) for j in range(i, rows)]
    pairs += [(i, rows + t) for i in range(rows) for t in range(2 * bands)]
    return pairs


def gram_pass(trial_bands, locked_bands):
    band_count, _, _, local_x, size, _ = trial_bands.shape
    kept = locked_bands.shape[0]
    pairs = gram_pairs(kept, band_count)
    slots = [(slot, i, j) for slot, (i, j) in enumerate(pairs)]
    width = 12
    groups = [slots[start : start + width] for start in range(0, len(slots), width)]
    partial = pl.pallas_call(
        functools.partial(gram_kernel, groups),
        grid=(local_x,),
        in_specs=[
            pl.BlockSpec((kept, 2, 3, 1, size, size), lambda x: (0, 0, 0, x, 0, 0)),
            pl.BlockSpec((band_count, 2, 3, 1, size, size), lambda x: (0, 0, 0, x, 0, 0)),
        ],
        out_specs=pl.BlockSpec((len(pairs), 8, size), lambda x: (0, 0, 0)),
        out_shape=jax.ShapeDtypeStruct((len(pairs), 8, size), jnp.float32),
    )(locked_bands, trial_bands)
    return jnp.sum(partial, axis=(1, 2))


def pair_matrix(sums, kept, bands):
    pairs = gram_pairs(kept, bands)
    total = 2 * kept + 2 * bands
    index = np.zeros((total, total), dtype=np.int32)
    for slot, (i, j) in enumerate(pairs):
        index[i, j] = slot
        index[j, i] = slot
    return sums[jnp.asarray(index)]


def dft_tables(length, orient):
    indices = np.arange(length, dtype=np.int64)
    phases = indices[:, None] * indices[None, :] % length
    angles = phases.astype(np.float64) * (2.0 * math.pi / length)
    norm_factor = 1.0 / math.sqrt(length)
    c_hi, c_lo = numpy_split(np.cos(angles) * norm_factor)
    s_hi, s_lo = numpy_split(np.sin(angles) * norm_factor * orient)
    return c_hi, c_lo, s_hi, s_lo


def front_pass(comps, coef_rows, wave_x, trial_bands, locked_bands):
    band_count, _, _, local_x, size, _ = trial_bands.shape
    kept = locked_bands.shape[0]
    tables = dft_tables(size, 1.0)
    smem = pl.BlockSpec(memory_space=pltpu.SMEM)
    table_spec = pl.BlockSpec((size, size), lambda b, x: (0, 0))
    width = len(comps)
    return pl.pallas_call(
        functools.partial(front_kernel, comps),
        grid=(band_count, local_x),
        in_specs=[
            smem,
            smem,
            pl.BlockSpec((1, 2, 3, 1, size, size), lambda b, x: (b, 0, 0, x, 0, 0)),
            pl.BlockSpec((kept, 2, 3, 1, size, size), lambda b, x: (0, 0, 0, x, 0, 0)),
            table_spec,
            table_spec,
            table_spec,
            table_spec,
        ],
        out_specs=pl.BlockSpec((2, 1, width, 1, size, size), lambda b, x: (0, b, 0, x, 0, 0)),
        out_shape=jax.ShapeDtypeStruct((2, band_count, width, local_x, size, size), jnp.float32),
    )(coef_rows, wave_x, trial_bands, locked_bands, *tables)


def butterfly_sum(values, axis, count):
    if count & (count - 1):
        return lax.psum(values, axis)
    step = 1
    while step < count:
        pairs = [(index, index ^ step) for index in range(count)]
        values = values + lax.ppermute(values, axis, pairs)
        step *= 2
    return values


def inner_sum(left_rows, right_rows):
    return jnp.einsum("an,bn->ab", left_rows, right_rows, preferred_element_type=jnp.float32)


def remove_locked(gram_sums, trial_re, trial_im, locked_re, locked_im):
    gram_a, gram_q, proj_re, proj_im = gram_sums
    kept_count = gram_a.shape[0]
    gram = jnp.concatenate(
        [jnp.concatenate([gram_a, gram_q], axis=1), jnp.concatenate([gram_q.T, gram_a], axis=1)],
        axis=0,
    )
    rhs_both = jnp.concatenate([proj_re, proj_im], axis=0)
    lower = jnp.linalg.cholesky(gram)
    middle = lax.linalg.triangular_solve(lower, rhs_both, left_side=True, lower=True)
    coef = lax.linalg.triangular_solve(lower, middle, left_side=True, lower=True, transpose_a=True)
    coef_one = coef[:kept_count]
    coef_two = coef[kept_count:]
    locked_re32 = locked_re.astype(jnp.float32)
    locked_im32 = locked_im.astype(jnp.float32)
    out_re = (
        trial_re.astype(jnp.float32)
        - jnp.einsum("ab,an->bn", coef_one, locked_re32, precision=highest)
        + jnp.einsum("ab,an->bn", coef_two, locked_im32, precision=highest)
    )
    out_im = (
        trial_im.astype(jnp.float32)
        - jnp.einsum("ab,an->bn", coef_one, locked_im32, precision=highest)
        - jnp.einsum("ab,an->bn", coef_two, locked_re32, precision=highest)
    )
    return (out_re, out_im)


def solve_coef(gram_sums):
    gram_a, gram_q, proj_re, proj_im = gram_sums
    gram = jnp.concatenate(
        [jnp.concatenate([gram_a, gram_q], axis=1), jnp.concatenate([gram_q.T, gram_a], axis=1)],
        axis=0,
    )
    rhs_both = jnp.concatenate([proj_re, proj_im], axis=0)
    lower = jnp.linalg.cholesky(gram)
    middle = lax.linalg.triangular_solve(lower, rhs_both, left_side=True, lower=True)
    return lax.linalg.triangular_solve(lower, middle, left_side=True, lower=True, transpose_a=True)


def maxwell_pass(chunks, waves, inv_diag, inv_corr, to_space_fn, to_spectrum_fn):
    space = jnp.concatenate([transform(to_space_fn(chunk), 2, 1.0) for chunk in chunks], axis=2)
    weighted = apply_tensor(space, inv_diag, inv_corr)
    homes = []
    for comp in range(weighted.shape[2]):
        source = transform(weighted[:, :, comp : comp + 1], 2, -1.0)
        if comp >= 2:
            source, _ = lax.optimization_barrier((source, homes[comp - 2]))
        home = to_spectrum_fn(source)
        home = transform(home, 3, -1.0)
        homes.append(transform(home, 4, -1.0))
    home = jnp.concatenate(homes, axis=2)
    return (curl_times_i(waves, home), space, weighted)


def per_device(wide_count, trial_bands, locked_bands, inv_diag, inv_corr):
    band_count = trial_bands.shape[0]
    kept_count = locked_bands.shape[0]
    local_x = trial_bands.shape[3]
    grid_len = trial_bands.shape[4]
    sums = butterfly_sum(gram_pass(trial_bands, locked_bands), "wide", wide_count)
    pairs = pair_matrix(sums, kept_count, band_count)
    lk = pairs[: 2 * kept_count, : 2 * kept_count].reshape(kept_count, 2, kept_count, 2)
    lt = pairs[: 2 * kept_count, 2 * kept_count :].reshape(kept_count, 2, band_count, 2)
    gram_a = lk[:, 0, :, 0] + lk[:, 1, :, 1]
    gram_q = lk[:, 1, :, 0] - lk[:, 0, :, 1]
    proj_re = lt[:, 0, :, 0] + lt[:, 1, :, 1]
    proj_im = lt[:, 0, :, 1] - lt[:, 1, :, 0]
    gram_sums = (gram_a, gram_q, proj_re, proj_im)
    coef = solve_coef(gram_sums)
    start_x = lax.axis_index("wide") * local_x
    full_axis = jnp.arange(grid_len, dtype=jnp.int32)
    wave_x = signed_wave(start_x + jnp.arange(local_x, dtype=jnp.int32), grid_len)
    wave_full = signed_wave(full_axis, grid_len)
    waves = (wave_x, wave_full, wave_full)

    def exchange_rows(field, split_dim, keep_dim):
        parts, bands, comps = field.shape[0], field.shape[1], field.shape[2]
        order = (split_dim, 1, 2, keep_dim, 0, 5)
        moved = jnp.transpose(field, order).reshape(wide_count, -1, 128)
        moved = lax.all_to_all(moved, "wide", split_axis=0, concat_axis=0, tiled=True)
        local_split = field.shape[split_dim] // wide_count
        moved = moved.reshape(
            wide_count, local_split, bands, comps, field.shape[keep_dim], parts, field.shape[5]
        )
        return moved

    def send_out_one(field):
        moved = exchange_rows(field, 4, 3)
        moved = jnp.transpose(moved, (5, 2, 3, 0, 4, 1, 6))
        shape = moved.shape
        return moved.reshape(shape[0], shape[1], shape[2], shape[3] * shape[4], shape[5], shape[6])

    def send_home_one(field):
        moved = exchange_rows(field, 3, 4)
        moved = jnp.transpose(moved, (5, 2, 3, 1, 0, 4, 6))
        shape = moved.shape
        return moved.reshape(shape[0], shape[1], shape[2], shape[3], shape[4] * shape[5], shape[6])

    chunks = [front_pass((comp,), coef.T, wave_x, trial_bands, locked_bands) for comp in range(3)]
    results = [maxwell_pass(chunks, waves, inv_diag, inv_corr, send_out_one, send_home_one)]
    applied_st, space, weighted = [
        jnp.concatenate([entry[slot] for entry in results], axis=1) for slot in range(3)
    ]
    applied = jnp.stack([applied_st[0], applied_st[1]], axis=1).astype(jnp.bfloat16)
    scale_all = 1.0 / float(grid_len * grid_len * grid_len)
    left_re = space[0].reshape(band_count, -1)
    left_im = space[1].reshape(band_count, -1)
    right_re = weighted[0].reshape(band_count, -1)
    right_im = weighted[1].reshape(band_count, -1)
    part_re = jnp.einsum("an,bn->ab", left_re, right_re, precision=highest) + jnp.einsum(
        "an,bn->ab", left_im, right_im, precision=highest
    )
    part_im = jnp.einsum("an,bn->ab", left_re, right_im, precision=highest) - jnp.einsum(
        "an,bn->ab", left_im, right_re, precision=highest
    )
    total_re, total_im = butterfly_sum(jnp.stack([part_re, part_im], axis=0), "wide", wide_count)
    rayleigh = jnp.stack([total_re * scale_all, total_im * scale_all], axis=0)
    return (applied, rayleigh)


def solution(mesh):
    in_specs = (
        P("groups", None, None, "wide", None, None),
        P("groups", None, None, "wide", None, None),
        P("groups", None, "wide", None),
        P("groups", None, "wide", None),
    )
    out_specs = (P("groups", None, None, "wide", None, None), P("groups", None, None))
    wide_count = mesh.shape["wide"]
    return jax.shard_map(
        functools.partial(per_device, wide_count), mesh=mesh, in_specs=in_specs, out_specs=out_specs, check_vma=False
    )
```

```python
import functools
import math

import ml_dtypes
import numpy as np

import jax
import jax.numpy as jnp
from jax import lax
from jax.sharding import PartitionSpec as P
from jax.experimental import pallas as pl
from jax.experimental.pallas import tpu as pltpu

highest = lax.Precision.HIGHEST
three_pass = lax.Precision.HIGH


def signed_wave(indices, length):
    shifted = jnp.where(indices < length // 2, indices, indices - length)
    return shifted.astype(jnp.float32) / (length / 2.0)


def cross_wave(wave_x, wave_y, wave_z, vectors):
    comp_x = vectors[..., 0, :, :, :]
    comp_y = vectors[..., 1, :, :, :]
    comp_z = vectors[..., 2, :, :, :]
    along_x = wave_x[:, None, None]
    along_y = wave_y[None, :, None]
    along_z = wave_z[None, None, :]
    return jnp.stack(
        [
            along_y * comp_z - along_z * comp_y,
            along_z * comp_x - along_x * comp_z,
            along_x * comp_y - along_y * comp_x,
        ],
        axis=-4,
    )


def curl_times_i(waves, stacked):
    wave_x, wave_y, wave_z = waves
    return jnp.stack(
        [
            -cross_wave(wave_x, wave_y, wave_z, stacked[1]),
            cross_wave(wave_x, wave_y, wave_z, stacked[0]),
        ],
        axis=0,
    )


def apply_tensor(vectors, inv_diag, inv_corr):
    coupling_xy = inv_corr[0] * jnp.sqrt(inv_diag[0] * inv_diag[1])
    coupling_xz = inv_corr[1] * jnp.sqrt(inv_diag[0] * inv_diag[2])
    coupling_yz = inv_corr[2] * jnp.sqrt(inv_diag[1] * inv_diag[2])
    comp_x = vectors[..., 0, :, :, :]
    comp_y = vectors[..., 1, :, :, :]
    comp_z = vectors[..., 2, :, :, :]
    out_x = inv_diag[0] * comp_x + coupling_xy * comp_y + coupling_xz * comp_z
    out_y = coupling_xy * comp_x + inv_diag[1] * comp_y + coupling_yz * comp_z
    out_z = coupling_xz * comp_x + coupling_yz * comp_y + inv_diag[2] * comp_z
    return jnp.stack([out_x, out_y, out_z], axis=-4)


def complex_table(length, orient, order=None):
    indices = jnp.arange(length, dtype=jnp.int32)
    sources = indices if order is None else jnp.asarray(order, dtype=jnp.int32)
    phases = sources[:, None] * indices[None, :] % length
    angles = phases.astype(jnp.float32) * (2.0 * math.pi / length)
    norm_factor = 1.0 / math.sqrt(length)
    cos_table = jnp.cos(angles) * norm_factor
    sin_table = jnp.sin(angles) * norm_factor * orient
    return jnp.stack(
        [jnp.stack([cos_table, sin_table], axis=0), jnp.stack([-sin_table, cos_table], axis=0)],
        axis=0,
    )


def transform(stacked, axis_dim, orient, order=None):
    table = complex_table(stacked.shape[axis_dim + 1], orient, order)
    if axis_dim == 2:
        return jnp.einsum("pbckyz,pqkn->qbcnyz", stacked, table, precision=three_pass)
    if axis_dim == 3:
        return jnp.einsum("pbcxkz,pqkn->qbcxnz", stacked, table, precision=three_pass)
    return jnp.einsum("pbcxyk,pqkn->qbcxyn", stacked, table, precision=three_pass)


def split_hi_lo(values):
    scaled = values * 65537.0
    top = scaled - (scaled - values)
    return top.astype(jnp.bfloat16), (values - top).astype(jnp.bfloat16)


def dot_right(values, table_hi, table_lo):
    high, low = split_hi_lo(values)
    f32 = jnp.float32
    return (
        jnp.dot(high, table_hi, preferred_element_type=f32)
        + jnp.dot(low, table_hi, preferred_element_type=f32)
        + jnp.dot(high, table_lo, preferred_element_type=f32)
    )


def dot_left(table_hi, table_lo, values):
    high, low = split_hi_lo(values)
    f32 = jnp.float32
    return (
        jnp.dot(table_hi, high, preferred_element_type=f32)
        + jnp.dot(table_hi, low, preferred_element_type=f32)
        + jnp.dot(table_lo, high, preferred_element_type=f32)
    )


def front_kernel(comps, coef_ref, qx_ref, trial_ref, locked_ref, chi_ref, clo_ref, shi_ref, slo_ref, out_ref):
    band = pl.program_id(0)
    plane = pl.program_id(1)
    kept = locked_ref.shape[0]
    size = trial_ref.shape[-1]
    f32 = jnp.float32
    first = [coef_ref[band, k] for k in range(kept)]
    second = [coef_ref[band, kept + k] for k in range(kept)]
    needed = sorted({(c + 1) % 3 for c in comps} | {(c + 2) % 3 for c in comps})
    part_re = {}
    part_im = {}
    for comp in needed:
        acc_re = trial_ref[0, 0, comp, 0].astype(f32)
        acc_im = trial_ref[0, 1, comp, 0].astype(f32)
        for k in range(kept):
            l_re = locked_ref[k, 0, comp, 0].astype(f32)
            l_im = locked_ref[k, 1, comp, 0].astype(f32)
            acc_re = acc_re - first[k] * l_re + second[k] * l_im
            acc_im = acc_im - first[k] * l_im - second[k] * l_re
        part_re[comp] = acc_re
        part_im[comp] = acc_im
    rows = lax.broadcasted_iota(jnp.int32, (size, 1), 0)
    cols = lax.broadcasted_iota(jnp.int32, (1, size), 1)
    half = size // 2
    wave_y = jnp.where(rows < half, rows, rows - size).astype(f32) / (size / 2.0)
    wave_z = jnp.where(cols < half, cols, cols - size).astype(f32) / (size / 2.0)
    waves = (qx_ref[plane], wave_y, wave_z)
    c_hi = chi_ref[...]
    c_lo = clo_ref[...]
    s_hi = shi_ref[...]
    s_lo = slo_ref[...]
    for slot, comp in enumerate(comps):
        a = (comp + 1) % 3
        b = (comp + 2) % 3
        cur_re = -(waves[a] * part_im[b] - waves[b] * part_im[a])
        cur_im = waves[a] * part_re[b] - waves[b] * part_re[a]
        z_re = dot_right(cur_re, c_hi, c_lo) - dot_right(cur_im, s_hi, s_lo)
        z_im = dot_right(cur_re, s_hi, s_lo) + dot_right(cur_im, c_hi, c_lo)
        y_re = dot_left(c_hi, c_lo, z_re) - dot_left(s_hi, s_lo, z_im)
        y_im = dot_left(s_hi, s_lo, z_re) + dot_left(c_hi, c_lo, z_im)
        out_ref[0, 0, slot, 0] = y_re
        out_ref[1, 0, slot, 0] = y_im


def numpy_split(table):
    full = table.astype(np.float32)
    high = full.astype(ml_dtypes.bfloat16)
    low = (full - high.astype(np.float32)).astype(ml_dtypes.bfloat16)
    return jnp.asarray(high), jnp.asarray(low)


def dft_tables(length, orient):
    indices = np.arange(length, dtype=np.int64)
    phases = indices[:, None] * indices[None, :] % length
    angles = phases.astype(np.float64) * (2.0 * math.pi / length)
    norm_factor = 1.0 / math.sqrt(length)
    c_hi, c_lo = numpy_split(np.cos(angles) * norm_factor)
    s_hi, s_lo = numpy_split(np.sin(angles) * norm_factor * orient)
    return c_hi, c_lo, s_hi, s_lo


def front_pass(comps, coef_rows, wave_x, trial_bands, locked_bands, start, count):
    band_count, _, _, _, size, _ = trial_bands.shape
    kept = locked_bands.shape[0]
    tables = dft_tables(size, 1.0)
    smem = pl.BlockSpec(memory_space=pltpu.SMEM)
    table_spec = pl.BlockSpec((size, size), lambda b, x: (0, 0))
    width = len(comps)
    return pl.pallas_call(
        functools.partial(front_kernel, comps),
        grid=(band_count, count),
        in_specs=[
            smem,
            smem,
            pl.BlockSpec((1, 2, 3, 1, size, size), lambda b, x: (b, 0, 0, x + start, 0, 0)),
            pl.BlockSpec((kept, 2, 3, 1, size, size), lambda b, x: (0, 0, 0, x + start, 0, 0)),
            table_spec,
            table_spec,
            table_spec,
            table_spec,
        ],
        out_specs=pl.BlockSpec((2, 1, width, 1, size, size), lambda b, x: (0, b, 0, x, 0, 0)),
        out_shape=jax.ShapeDtypeStruct((2, band_count, width, count, size, size), jnp.float32),
    )(coef_rows, wave_x[start : start + count], trial_bands, locked_bands, *tables)


def butterfly_sum(values, axis, count):
    if count & (count - 1):
        return lax.psum(values, axis)
    step = 1
    while step < count:
        pairs = [(index, index ^ step) for index in range(count)]
        values = values + lax.ppermute(values, axis, pairs)
        step *= 2
    return values


def inner_sum(left_rows, right_rows):
    return jnp.einsum("an,bn->ab", left_rows, right_rows, preferred_element_type=jnp.float32)


def remove_locked(gram_sums, trial_re, trial_im, locked_re, locked_im):
    gram_a, gram_q, proj_re, proj_im = gram_sums
    kept_count = gram_a.shape[0]
    gram = jnp.concatenate(
        [jnp.concatenate([gram_a, gram_q], axis=1), jnp.concatenate([gram_q.T, gram_a], axis=1)],
        axis=0,
    )
    rhs_both = jnp.concatenate([proj_re, proj_im], axis=0)
    lower = jnp.linalg.cholesky(gram)
    middle = lax.linalg.triangular_solve(lower, rhs_both, left_side=True, lower=True)
    coef = lax.linalg.triangular_solve(lower, middle, left_side=True, lower=True, transpose_a=True)
    coef_one = coef[:kept_count]
    coef_two = coef[kept_count:]
    locked_re32 = locked_re.astype(jnp.float32)
    locked_im32 = locked_im.astype(jnp.float32)
    out_re = (
        trial_re.astype(jnp.float32)
        - jnp.einsum("ab,an->bn", coef_one, locked_re32, precision=highest)
        + jnp.einsum("ab,an->bn", coef_two, locked_im32, precision=highest)
    )
    out_im = (
        trial_im.astype(jnp.float32)
        - jnp.einsum("ab,an->bn", coef_one, locked_im32, precision=highest)
        - jnp.einsum("ab,an->bn", coef_two, locked_re32, precision=highest)
    )
    return (out_re, out_im)


def solve_coef(gram_sums):
    gram_a, gram_q, proj_re, proj_im = gram_sums
    gram = jnp.concatenate(
        [jnp.concatenate([gram_a, gram_q], axis=1), jnp.concatenate([gram_q.T, gram_a], axis=1)],
        axis=0,
    )
    rhs_both = jnp.concatenate([proj_re, proj_im], axis=0)
    lower = jnp.linalg.cholesky(gram)
    middle = lax.linalg.triangular_solve(lower, rhs_both, left_side=True, lower=True)
    return lax.linalg.triangular_solve(lower, middle, left_side=True, lower=True, transpose_a=True)


def maxwell_pass(chunks, order, waves, inv_diag, inv_corr, to_space_fn, to_spectrum_fn):
    moved = jnp.concatenate([to_space_fn(chunk) for chunk in chunks], axis=3)
    space = transform(moved, 2, 1.0, order)
    weighted = apply_tensor(space, inv_diag, inv_corr)
    homes = []
    for comp in range(weighted.shape[2]):
        source = transform(weighted[:, :, comp : comp + 1], 2, -1.0)
        if comp >= 2:
            source, _ = lax.optimization_barrier((source, homes[comp - 2]))
        home = to_spectrum_fn(source)
        home = transform(home, 3, -1.0)
        homes.append(transform(home, 4, -1.0))
    home = jnp.concatenate(homes, axis=2)
    return (curl_times_i(waves, home), space, weighted)


def per_device(wide_count, trial_bands, locked_bands, inv_diag, inv_corr):
    band_count = trial_bands.shape[0]
    kept_count = locked_bands.shape[0]
    local_x = trial_bands.shape[3]
    grid_len = trial_bands.shape[4]
    rows = jnp.concatenate(
        [locked_bands.reshape((2 * kept_count,) + locked_bands.shape[2:]),
         trial_bands.reshape((2 * band_count,) + trial_bands.shape[2:])],
        axis=0,
    )
    pairs = jnp.einsum("icxyz,jcxyz->ij", rows, rows, preferred_element_type=jnp.float32)
    pairs = butterfly_sum(pairs, "wide", wide_count)
    lk = pairs[: 2 * kept_count, : 2 * kept_count].reshape(kept_count, 2, kept_count, 2)
    lt = pairs[: 2 * kept_count, 2 * kept_count :].reshape(kept_count, 2, band_count, 2)
    gram_a = lk[:, 0, :, 0] + lk[:, 1, :, 1]
    gram_q = lk[:, 1, :, 0] - lk[:, 0, :, 1]
    proj_re = lt[:, 0, :, 0] + lt[:, 1, :, 1]
    proj_im = lt[:, 0, :, 1] - lt[:, 1, :, 0]
    gram_sums = (gram_a, gram_q, proj_re, proj_im)
    coef = solve_coef(gram_sums)
    start_x = lax.axis_index("wide") * local_x
    full_axis = jnp.arange(grid_len, dtype=jnp.int32)
    wave_x = signed_wave(start_x + jnp.arange(local_x, dtype=jnp.int32), grid_len)
    wave_full = signed_wave(full_axis, grid_len)
    waves = (wave_x, wave_full, wave_full)

    def exchange_rows(field, split_dim, keep_dim):
        parts, bands, comps = field.shape[0], field.shape[1], field.shape[2]
        order = (split_dim, 1, 2, keep_dim, 0, 5)
        moved = jnp.transpose(field, order).reshape(wide_count, -1, 128)
        moved = lax.all_to_all(moved, "wide", split_axis=0, concat_axis=0, tiled=True)
        local_split = field.shape[split_dim] // wide_count
        moved = moved.reshape(
            wide_count, local_split, bands, comps, field.shape[keep_dim], parts, field.shape[5]
        )
        return moved

    def send_out_one(field):
        moved = exchange_rows(field, 4, 3)
        moved = jnp.transpose(moved, (5, 2, 3, 0, 4, 1, 6))
        shape = moved.shape
        return moved.reshape(shape[0], shape[1], shape[2], shape[3] * shape[4], shape[5], shape[6])

    def send_home_one(field):
        moved = exchange_rows(field, 3, 4)
        moved = jnp.transpose(moved, (5, 2, 3, 1, 0, 4, 6))
        shape = moved.shape
        return moved.reshape(shape[0], shape[1], shape[2], shape[3], shape[4] * shape[5], shape[6])

    first = (local_x + 1) // 2
    spans = [(0, first), (first, local_x - first)] if local_x > 1 else [(0, local_x)]
    chunks = [
        front_pass((0, 1, 2), coef.T, wave_x, trial_bands, locked_bands, start, count)
        for start, count in spans
    ]
    order = np.concatenate(
        [
            (np.arange(wide_count)[:, None] * local_x + start + np.arange(count)[None, :]).reshape(-1)
            for start, count in spans
        ]
    )
    results = [maxwell_pass(chunks, order, waves, inv_diag, inv_corr, send_out_one, send_home_one)]
    applied_st, space, weighted = [
        jnp.concatenate([entry[slot] for entry in results], axis=1) for slot in range(3)
    ]
    applied = jnp.stack([applied_st[0], applied_st[1]], axis=1).astype(jnp.bfloat16)
    scale_all = 1.0 / float(grid_len * grid_len * grid_len)
    left_re = space[0].reshape(band_count, -1)
    left_im = space[1].reshape(band_count, -1)
    right_re = weighted[0].reshape(band_count, -1)
    right_im = weighted[1].reshape(band_count, -1)
    part_re = jnp.einsum("an,bn->ab", left_re, right_re, precision=highest) + jnp.einsum(
        "an,bn->ab", left_im, right_im, precision=highest
    )
    part_im = jnp.einsum("an,bn->ab", left_re, right_im, precision=highest) - jnp.einsum(
        "an,bn->ab", left_im, right_re, precision=highest
    )
    total_re, total_im = butterfly_sum(jnp.stack([part_re, part_im], axis=0), "wide", wide_count)
    rayleigh = jnp.stack([total_re * scale_all, total_im * scale_all], axis=0)
    return (applied, rayleigh)


def solution(mesh):
    in_specs = (
        P("groups", None, None, "wide", None, None),
        P("groups", None, None, "wide", None, None),
        P("groups", None, "wide", None),
        P("groups", None, "wide", None),
    )
    out_specs = (P("groups", None, None, "wide", None, None), P("groups", None, None))
    wide_count = mesh.shape["wide"]
    return jax.shard_map(
        functools.partial(per_device, wide_count), mesh=mesh, in_specs=in_specs, out_specs=out_specs, check_vma=False
    )
```

```python
import functools
import math

import ml_dtypes
import numpy as np

import jax
import jax.numpy as jnp
from jax import lax
from jax.sharding import PartitionSpec as P
from jax.experimental import pallas as pl
from jax.experimental.pallas import tpu as pltpu

highest = lax.Precision.HIGHEST
three_pass = lax.Precision.HIGH


def signed_wave(indices, length):
    shifted = jnp.where(indices < length // 2, indices, indices - length)
    return shifted.astype(jnp.float32) / (length / 2.0)


def cross_wave(wave_x, wave_y, wave_z, vectors):
    comp_x = vectors[..., 0, :, :, :]
    comp_y = vectors[..., 1, :, :, :]
    comp_z = vectors[..., 2, :, :, :]
    along_x = wave_x[:, None, None]
    along_y = wave_y[None, :, None]
    along_z = wave_z[None, None, :]
    return jnp.stack(
        [
            along_y * comp_z - along_z * comp_y,
            along_z * comp_x - along_x * comp_z,
            along_x * comp_y - along_y * comp_x,
        ],
        axis=-4,
    )


def curl_times_i(waves, stacked):
    wave_x, wave_y, wave_z = waves
    return jnp.stack(
        [
            -cross_wave(wave_x, wave_y, wave_z, stacked[1]),
            cross_wave(wave_x, wave_y, wave_z, stacked[0]),
        ],
        axis=0,
    )


def apply_tensor(vectors, inv_diag, inv_corr):
    coupling_xy = inv_corr[0] * jnp.sqrt(inv_diag[0] * inv_diag[1])
    coupling_xz = inv_corr[1] * jnp.sqrt(inv_diag[0] * inv_diag[2])
    coupling_yz = inv_corr[2] * jnp.sqrt(inv_diag[1] * inv_diag[2])
    comp_x = vectors[..., 0, :, :, :]
    comp_y = vectors[..., 1, :, :, :]
    comp_z = vectors[..., 2, :, :, :]
    out_x = inv_diag[0] * comp_x + coupling_xy * comp_y + coupling_xz * comp_z
    out_y = coupling_xy * comp_x + inv_diag[1] * comp_y + coupling_yz * comp_z
    out_z = coupling_xz * comp_x + coupling_yz * comp_y + inv_diag[2] * comp_z
    return jnp.stack([out_x, out_y, out_z], axis=-4)


def complex_table(length, orient, order=None):
    indices = jnp.arange(length, dtype=jnp.int32)
    sources = indices if order is None else jnp.asarray(order, dtype=jnp.int32)
    phases = sources[:, None] * indices[None, :] % length
    angles = phases.astype(jnp.float32) * (2.0 * math.pi / length)
    norm_factor = 1.0 / math.sqrt(length)
    cos_table = jnp.cos(angles) * norm_factor
    sin_table = jnp.sin(angles) * norm_factor * orient
    return jnp.stack(
        [jnp.stack([cos_table, sin_table], axis=0), jnp.stack([-sin_table, cos_table], axis=0)],
        axis=0,
    )


def transform(stacked, axis_dim, orient, order=None):
    table = complex_table(stacked.shape[axis_dim + 1], orient, order)
    if axis_dim == 2:
        return jnp.einsum("pbckyz,pqkn->qbcnyz", stacked, table, precision=three_pass)
    if axis_dim == 3:
        return jnp.einsum("pbcxkz,pqkn->qbcxnz", stacked, table, precision=three_pass)
    return jnp.einsum("pbcxyk,pqkn->qbcxyn", stacked, table, precision=three_pass)


def split_hi_lo(values):
    scaled = values * 65537.0
    top = scaled - (scaled - values)
    return top.astype(jnp.bfloat16), (values - top).astype(jnp.bfloat16)


def dot_right(values, table_hi, table_lo):
    high, low = split_hi_lo(values)
    f32 = jnp.float32
    return (
        jnp.dot(high, table_hi, preferred_element_type=f32)
        + jnp.dot(low, table_hi, preferred_element_type=f32)
        + jnp.dot(high, table_lo, preferred_element_type=f32)
    )


def dot_left(table_hi, table_lo, values):
    high, low = split_hi_lo(values)
    f32 = jnp.float32
    return (
        jnp.dot(table_hi, high, preferred_element_type=f32)
        + jnp.dot(table_hi, low, preferred_element_type=f32)
        + jnp.dot(table_lo, high, preferred_element_type=f32)
    )


def front_kernel(comps, coef_ref, qx_ref, trial_ref, locked_ref, chi_ref, clo_ref, shi_ref, slo_ref, out_ref):
    band = pl.program_id(0)
    plane = pl.program_id(1)
    kept = locked_ref.shape[0]
    size = trial_ref.shape[-1]
    f32 = jnp.float32
    first = [coef_ref[band, k] for k in range(kept)]
    second = [coef_ref[band, kept + k] for k in range(kept)]
    needed = sorted({(c + 1) % 3 for c in comps} | {(c + 2) % 3 for c in comps})
    part_re = {}
    part_im = {}
    for comp in needed:
        acc_re = trial_ref[0, 0, comp, 0].astype(f32)
        acc_im = trial_ref[0, 1, comp, 0].astype(f32)
        for k in range(kept):
            l_re = locked_ref[k, 0, comp, 0].astype(f32)
            l_im = locked_ref[k, 1, comp, 0].astype(f32)
            acc_re = acc_re - first[k] * l_re + second[k] * l_im
            acc_im = acc_im - first[k] * l_im - second[k] * l_re
        part_re[comp] = acc_re
        part_im[comp] = acc_im
    rows = lax.broadcasted_iota(jnp.int32, (size, 1), 0)
    cols = lax.broadcasted_iota(jnp.int32, (1, size), 1)
    half = size // 2
    wave_y = jnp.where(rows < half, rows, rows - size).astype(f32) / (size / 2.0)
    wave_z = jnp.where(cols < half, cols, cols - size).astype(f32) / (size / 2.0)
    waves = (qx_ref[plane], wave_y, wave_z)
    c_hi = chi_ref[...]
    c_lo = clo_ref[...]
    s_hi = shi_ref[...]
    s_lo = slo_ref[...]
    for slot, comp in enumerate(comps):
        a = (comp + 1) % 3
        b = (comp + 2) % 3
        cur_re = -(waves[a] * part_im[b] - waves[b] * part_im[a])
        cur_im = waves[a] * part_re[b] - waves[b] * part_re[a]
        z_re = dot_right(cur_re, c_hi, c_lo) - dot_right(cur_im, s_hi, s_lo)
        z_im = dot_right(cur_re, s_hi, s_lo) + dot_right(cur_im, c_hi, c_lo)
        y_re = dot_left(c_hi, c_lo, z_re) - dot_left(s_hi, s_lo, z_im)
        y_im = dot_left(s_hi, s_lo, z_re) + dot_left(c_hi, c_lo, z_im)
        out_ref[0, 0, slot, 0] = y_re
        out_ref[1, 0, slot, 0] = y_im


def numpy_split(table):
    full = table.astype(np.float32)
    high = full.astype(ml_dtypes.bfloat16)
    low = (full - high.astype(np.float32)).astype(ml_dtypes.bfloat16)
    return jnp.asarray(high), jnp.asarray(low)


def dft_tables(length, orient):
    indices = np.arange(length, dtype=np.int64)
    phases = indices[:, None] * indices[None, :] % length
    angles = phases.astype(np.float64) * (2.0 * math.pi / length)
    norm_factor = 1.0 / math.sqrt(length)
    c_hi, c_lo = numpy_split(np.cos(angles) * norm_factor)
    s_hi, s_lo = numpy_split(np.sin(angles) * norm_factor * orient)
    return c_hi, c_lo, s_hi, s_lo


def front_pass(comps, coef_rows, wave_x, trial_bands, locked_bands, start, count):
    band_count, _, _, _, size, _ = trial_bands.shape
    kept = locked_bands.shape[0]
    tables = dft_tables(size, 1.0)
    smem = pl.BlockSpec(memory_space=pltpu.SMEM)
    table_spec = pl.BlockSpec((size, size), lambda b, x: (0, 0))
    width = len(comps)
    return pl.pallas_call(
        functools.partial(front_kernel, comps),
        grid=(band_count, count),
        in_specs=[
            smem,
            smem,
            pl.BlockSpec((1, 2, 3, 1, size, size), lambda b, x: (b, 0, 0, x + start, 0, 0)),
            pl.BlockSpec((kept, 2, 3, 1, size, size), lambda b, x: (0, 0, 0, x + start, 0, 0)),
            table_spec,
            table_spec,
            table_spec,
            table_spec,
        ],
        out_specs=pl.BlockSpec((2, 1, width, 1, size, size), lambda b, x: (0, b, 0, x, 0, 0)),
        out_shape=jax.ShapeDtypeStruct((2, band_count, width, count, size, size), jnp.float32),
    )(coef_rows, wave_x[start : start + count], trial_bands, locked_bands, *tables)


def butterfly_sum(values, axis, count):
    if count & (count - 1):
        return lax.psum(values, axis)
    step = 1
    while step < count:
        pairs = [(index, index ^ step) for index in range(count)]
        values = values + lax.ppermute(values, axis, pairs)
        step *= 2
    return values


def inner_sum(left_rows, right_rows):
    return jnp.einsum("an,bn->ab", left_rows, right_rows, preferred_element_type=jnp.float32)


def remove_locked(gram_sums, trial_re, trial_im, locked_re, locked_im):
    gram_a, gram_q, proj_re, proj_im = gram_sums
    kept_count = gram_a.shape[0]
    gram = jnp.concatenate(
        [jnp.concatenate([gram_a, gram_q], axis=1), jnp.concatenate([gram_q.T, gram_a], axis=1)],
        axis=0,
    )
    rhs_both = jnp.concatenate([proj_re, proj_im], axis=0)
    lower = jnp.linalg.cholesky(gram)
    middle = lax.linalg.triangular_solve(lower, rhs_both, left_side=True, lower=True)
    coef = lax.linalg.triangular_solve(lower, middle, left_side=True, lower=True, transpose_a=True)
    coef_one = coef[:kept_count]
    coef_two = coef[kept_count:]
    locked_re32 = locked_re.astype(jnp.float32)
    locked_im32 = locked_im.astype(jnp.float32)
    out_re = (
        trial_re.astype(jnp.float32)
        - jnp.einsum("ab,an->bn", coef_one, locked_re32, precision=highest)
        + jnp.einsum("ab,an->bn", coef_two, locked_im32, precision=highest)
    )
    out_im = (
        trial_im.astype(jnp.float32)
        - jnp.einsum("ab,an->bn", coef_one, locked_im32, precision=highest)
        - jnp.einsum("ab,an->bn", coef_two, locked_re32, precision=highest)
    )
    return (out_re, out_im)


def solve_coef(gram_sums):
    gram_a, gram_q, proj_re, proj_im = gram_sums
    gram = jnp.concatenate(
        [jnp.concatenate([gram_a, gram_q], axis=1), jnp.concatenate([gram_q.T, gram_a], axis=1)],
        axis=0,
    )
    rhs_both = jnp.concatenate([proj_re, proj_im], axis=0)
    lower = jnp.linalg.cholesky(gram)
    middle = lax.linalg.triangular_solve(lower, rhs_both, left_side=True, lower=True)
    return lax.linalg.triangular_solve(lower, middle, left_side=True, lower=True, transpose_a=True)


def maxwell_pass(chunks, order, waves, inv_diag, inv_corr, to_space_fn, to_spectrum_fn):
    moved = jnp.concatenate([to_space_fn(chunk) for chunk in chunks], axis=3)
    space = transform(moved, 2, 1.0, order)
    weighted = apply_tensor(space, inv_diag, inv_corr)
    homes = []
    for comp in range(weighted.shape[2]):
        source = transform(weighted[:, :, comp : comp + 1], 2, -1.0)
        if comp >= 2:
            source, _ = lax.optimization_barrier((source, homes[comp - 2]))
        home = to_spectrum_fn(source)
        home = transform(home, 3, -1.0)
        homes.append(transform(home, 4, -1.0))
    home = jnp.concatenate(homes, axis=2)
    return (curl_times_i(waves, home), space, weighted)


def per_device(wide_count, trial_bands, locked_bands, inv_diag, inv_corr):
    band_count = trial_bands.shape[0]
    kept_count = locked_bands.shape[0]
    local_x = trial_bands.shape[3]
    grid_len = trial_bands.shape[4]
    f32 = jnp.float32
    lk = jnp.einsum("kpcxyz,jqcxyz->kpjq", locked_bands, locked_bands, preferred_element_type=f32)
    lt = jnp.einsum("kpcxyz,bqcxyz->kpbq", locked_bands, trial_bands, preferred_element_type=f32)
    both = butterfly_sum(
        jnp.concatenate([lk.reshape(-1), lt.reshape(-1)]), "wide", wide_count
    )
    lk = both[: lk.size].reshape(lk.shape)
    lt = both[lk.size :].reshape(lt.shape)
    gram_a = lk[:, 0, :, 0] + lk[:, 1, :, 1]
    gram_q = lk[:, 1, :, 0] - lk[:, 0, :, 1]
    proj_re = lt[:, 0, :, 0] + lt[:, 1, :, 1]
    proj_im = lt[:, 0, :, 1] - lt[:, 1, :, 0]
    gram_sums = (gram_a, gram_q, proj_re, proj_im)
    coef = solve_coef(gram_sums)
    start_x = lax.axis_index("wide") * local_x
    full_axis = jnp.arange(grid_len, dtype=jnp.int32)
    wave_x = signed_wave(start_x + jnp.arange(local_x, dtype=jnp.int32), grid_len)
    wave_full = signed_wave(full_axis, grid_len)
    waves = (wave_x, wave_full, wave_full)

    def exchange_rows(field, split_dim, keep_dim):
        parts, bands, comps = field.shape[0], field.shape[1], field.shape[2]
        order = (split_dim, 1, 2, keep_dim, 0, 5)
        moved = jnp.transpose(field, order).reshape(wide_count, -1, 128)
        moved = lax.all_to_all(moved, "wide", split_axis=0, concat_axis=0, tiled=True)
        local_split = field.shape[split_dim] // wide_count
        moved = moved.reshape(
            wide_count, local_split, bands, comps, field.shape[keep_dim], parts, field.shape[5]
        )
        return moved

    def send_out_one(field):
        moved = exchange_rows(field, 4, 3)
        moved = jnp.transpose(moved, (5, 2, 3, 0, 4, 1, 6))
        shape = moved.shape
        return moved.reshape(shape[0], shape[1], shape[2], shape[3] * shape[4], shape[5], shape[6])

    def send_home_one(field):
        moved = exchange_rows(field, 3, 4)
        moved = jnp.transpose(moved, (5, 2, 3, 1, 0, 4, 6))
        shape = moved.shape
        return moved.reshape(shape[0], shape[1], shape[2], shape[3], shape[4] * shape[5], shape[6])

    first = (local_x + 1) // 2
    spans = [(0, first), (first, local_x - first)] if local_x > 1 else [(0, local_x)]
    chunks = [
        front_pass((0, 1, 2), coef.T, wave_x, trial_bands, locked_bands, start, count)
        for start, count in spans
    ]
    order = np.concatenate(
        [
            (np.arange(wide_count)[:, None] * local_x + start + np.arange(count)[None, :]).reshape(-1)
            for start, count in spans
        ]
    )
    results = [maxwell_pass(chunks, order, waves, inv_diag, inv_corr, send_out_one, send_home_one)]
    applied_st, space, weighted = [
        jnp.concatenate([entry[slot] for entry in results], axis=1) for slot in range(3)
    ]
    applied = jnp.stack([applied_st[0], applied_st[1]], axis=1).astype(jnp.bfloat16)
    scale_all = 1.0 / float(grid_len * grid_len * grid_len)
    left_re = space[0].reshape(band_count, -1)
    left_im = space[1].reshape(band_count, -1)
    right_re = weighted[0].reshape(band_count, -1)
    right_im = weighted[1].reshape(band_count, -1)
    part_re = jnp.einsum("an,bn->ab", left_re, right_re, precision=highest) + jnp.einsum(
        "an,bn->ab", left_im, right_im, precision=highest
    )
    part_im = jnp.einsum("an,bn->ab", left_re, right_im, precision=highest) - jnp.einsum(
        "an,bn->ab", left_im, right_re, precision=highest
    )
    total_re, total_im = butterfly_sum(jnp.stack([part_re, part_im], axis=0), "wide", wide_count)
    rayleigh = jnp.stack([total_re * scale_all, total_im * scale_all], axis=0)
    return (applied, rayleigh)


def solution(mesh):
    in_specs = (
        P("groups", None, None, "wide", None, None),
        P("groups", None, None, "wide", None, None),
        P("groups", None, "wide", None),
        P("groups", None, "wide", None),
    )
    out_specs = (P("groups", None, None, "wide", None, None), P("groups", None, None))
    wide_count = mesh.shape["wide"]
    return jax.shard_map(
        functools.partial(per_device, wide_count), mesh=mesh, in_specs=in_specs, out_specs=out_specs, check_vma=False
    )
```

```python
import functools
import math

import ml_dtypes
import numpy as np

import jax
import jax.numpy as jnp
from jax import lax
from jax.sharding import PartitionSpec as P
from jax.experimental import pallas as pl
from jax.experimental.pallas import tpu as pltpu

highest = lax.Precision.HIGHEST
three_pass = lax.Precision.HIGH


def signed_wave(indices, length):
    shifted = jnp.where(indices < length // 2, indices, indices - length)
    return shifted.astype(jnp.float32) / (length / 2.0)


def cross_wave(wave_x, wave_y, wave_z, vectors):
    comp_x = vectors[..., 0, :, :, :]
    comp_y = vectors[..., 1, :, :, :]
    comp_z = vectors[..., 2, :, :, :]
    along_x = wave_x[:, None, None]
    along_y = wave_y[None, :, None]
    along_z = wave_z[None, None, :]
    return jnp.stack(
        [
            along_y * comp_z - along_z * comp_y,
            along_z * comp_x - along_x * comp_z,
            along_x * comp_y - along_y * comp_x,
        ],
        axis=-4,
    )


def curl_times_i(waves, stacked):
    wave_x, wave_y, wave_z = waves
    return jnp.stack(
        [
            -cross_wave(wave_x, wave_y, wave_z, stacked[1]),
            cross_wave(wave_x, wave_y, wave_z, stacked[0]),
        ],
        axis=0,
    )


def apply_tensor(vectors, inv_diag, inv_corr):
    coupling_xy = inv_corr[0] * jnp.sqrt(inv_diag[0] * inv_diag[1])
    coupling_xz = inv_corr[1] * jnp.sqrt(inv_diag[0] * inv_diag[2])
    coupling_yz = inv_corr[2] * jnp.sqrt(inv_diag[1] * inv_diag[2])
    comp_x = vectors[..., 0, :, :, :]
    comp_y = vectors[..., 1, :, :, :]
    comp_z = vectors[..., 2, :, :, :]
    out_x = inv_diag[0] * comp_x + coupling_xy * comp_y + coupling_xz * comp_z
    out_y = coupling_xy * comp_x + inv_diag[1] * comp_y + coupling_yz * comp_z
    out_z = coupling_xz * comp_x + coupling_yz * comp_y + inv_diag[2] * comp_z
    return jnp.stack([out_x, out_y, out_z], axis=-4)


def complex_table(length, orient, order=None, targets=None):
    indices = jnp.arange(length, dtype=jnp.int32)
    sources = indices if order is None else jnp.asarray(order, dtype=jnp.int32)
    outputs = indices if targets is None else jnp.asarray(targets, dtype=jnp.int32)
    phases = sources[:, None] * outputs[None, :] % length
    angles = phases.astype(jnp.float32) * (2.0 * math.pi / length)
    norm_factor = 1.0 / math.sqrt(length)
    cos_table = jnp.cos(angles) * norm_factor
    sin_table = jnp.sin(angles) * norm_factor * orient
    return jnp.stack(
        [jnp.stack([cos_table, sin_table], axis=0), jnp.stack([-sin_table, cos_table], axis=0)],
        axis=0,
    )


def transform(stacked, axis_dim, orient, order=None, targets=None):
    table = complex_table(stacked.shape[axis_dim + 1], orient, order, targets)
    if axis_dim == 2:
        return jnp.einsum("pbckyz,pqkn->qbcnyz", stacked, table, precision=three_pass)
    if axis_dim == 3:
        return jnp.einsum("pbcxkz,pqkn->qbcxnz", stacked, table, precision=three_pass)
    return jnp.einsum("pbcxyk,pqkn->qbcxyn", stacked, table, precision=three_pass)


def split_hi_lo(values):
    scaled = values * 65537.0
    top = scaled - (scaled - values)
    return top.astype(jnp.bfloat16), (values - top).astype(jnp.bfloat16)


def dot_right(values, table_hi, table_lo):
    high, low = split_hi_lo(values)
    f32 = jnp.float32
    return (
        jnp.dot(high, table_hi, preferred_element_type=f32)
        + jnp.dot(low, table_hi, preferred_element_type=f32)
        + jnp.dot(high, table_lo, preferred_element_type=f32)
    )


def dot_left(table_hi, table_lo, values):
    high, low = split_hi_lo(values)
    f32 = jnp.float32
    return (
        jnp.dot(table_hi, high, preferred_element_type=f32)
        + jnp.dot(table_hi, low, preferred_element_type=f32)
        + jnp.dot(table_lo, high, preferred_element_type=f32)
    )


def front_kernel(comps, coef_ref, qx_ref, trial_ref, locked_ref, chi_ref, clo_ref, shi_ref, slo_ref, out_ref):
    band = pl.program_id(0)
    plane = pl.program_id(1)
    kept = locked_ref.shape[0]
    size = trial_ref.shape[-1]
    f32 = jnp.float32
    first = [coef_ref[band, k] for k in range(kept)]
    second = [coef_ref[band, kept + k] for k in range(kept)]
    needed = sorted({(c + 1) % 3 for c in comps} | {(c + 2) % 3 for c in comps})
    part_re = {}
    part_im = {}
    for comp in needed:
        acc_re = trial_ref[0, 0, comp, 0].astype(f32)
        acc_im = trial_ref[0, 1, comp, 0].astype(f32)
        for k in range(kept):
            l_re = locked_ref[k, 0, comp, 0].astype(f32)
            l_im = locked_ref[k, 1, comp, 0].astype(f32)
            acc_re = acc_re - first[k] * l_re + second[k] * l_im
            acc_im = acc_im - first[k] * l_im - second[k] * l_re
        part_re[comp] = acc_re
        part_im[comp] = acc_im
    rows = lax.broadcasted_iota(jnp.int32, (size, 1), 0)
    cols = lax.broadcasted_iota(jnp.int32, (1, size), 1)
    half = size // 2
    wave_y = jnp.where(rows < half, rows, rows - size).astype(f32) / (size / 2.0)
    wave_z = jnp.where(cols < half, cols, cols - size).astype(f32) / (size / 2.0)
    waves = (qx_ref[plane], wave_y, wave_z)
    c_hi = chi_ref[...]
    c_lo = clo_ref[...]
    s_hi = shi_ref[...]
    s_lo = slo_ref[...]
    for slot, comp in enumerate(comps):
        a = (comp + 1) % 3
        b = (comp + 2) % 3
        cur_re = -(waves[a] * part_im[b] - waves[b] * part_im[a])
        cur_im = waves[a] * part_re[b] - waves[b] * part_re[a]
        z_re = dot_right(cur_re, c_hi, c_lo) - dot_right(cur_im, s_hi, s_lo)
        z_im = dot_right(cur_re, s_hi, s_lo) + dot_right(cur_im, c_hi, c_lo)
        y_re = dot_left(c_hi, c_lo, z_re) - dot_left(s_hi, s_lo, z_im)
        y_im = dot_left(s_hi, s_lo, z_re) + dot_left(c_hi, c_lo, z_im)
        out_ref[0, 0, slot, 0] = y_re
        out_ref[1, 0, slot, 0] = y_im


def numpy_split(table):
    full = table.astype(np.float32)
    high = full.astype(ml_dtypes.bfloat16)
    low = (full - high.astype(np.float32)).astype(ml_dtypes.bfloat16)
    return jnp.asarray(high), jnp.asarray(low)


def dft_tables(length, orient):
    indices = np.arange(length, dtype=np.int64)
    phases = indices[:, None] * indices[None, :] % length
    angles = phases.astype(np.float64) * (2.0 * math.pi / length)
    norm_factor = 1.0 / math.sqrt(length)
    c_hi, c_lo = numpy_split(np.cos(angles) * norm_factor)
    s_hi, s_lo = numpy_split(np.sin(angles) * norm_factor * orient)
    return c_hi, c_lo, s_hi, s_lo


def front_pass(comps, coef_rows, wave_x, trial_bands, locked_bands, start, count):
    band_count, _, _, _, size, _ = trial_bands.shape
    kept = locked_bands.shape[0]
    tables = dft_tables(size, 1.0)
    smem = pl.BlockSpec(memory_space=pltpu.SMEM)
    table_spec = pl.BlockSpec((size, size), lambda b, x: (0, 0))
    width = len(comps)
    return pl.pallas_call(
        functools.partial(front_kernel, comps),
        grid=(band_count, count),
        in_specs=[
            smem,
            smem,
            pl.BlockSpec((1, 2, 3, 1, size, size), lambda b, x: (b, 0, 0, x + start, 0, 0)),
            pl.BlockSpec((kept, 2, 3, 1, size, size), lambda b, x: (0, 0, 0, x + start, 0, 0)),
            table_spec,
            table_spec,
            table_spec,
            table_spec,
        ],
        out_specs=pl.BlockSpec((2, 1, width, 1, size, size), lambda b, x: (0, b, 0, x, 0, 0)),
        out_shape=jax.ShapeDtypeStruct((2, band_count, width, count, size, size), jnp.float32),
    )(coef_rows, wave_x[start : start + count], trial_bands, locked_bands, *tables)


def butterfly_sum(values, axis, count):
    if count & (count - 1):
        return lax.psum(values, axis)
    step = 1
    while step < count:
        pairs = [(index, index ^ step) for index in range(count)]
        values = values + lax.ppermute(values, axis, pairs)
        step *= 2
    return values


def inner_sum(left_rows, right_rows):
    return jnp.einsum("an,bn->ab", left_rows, right_rows, preferred_element_type=jnp.float32)


def remove_locked(gram_sums, trial_re, trial_im, locked_re, locked_im):
    gram_a, gram_q, proj_re, proj_im = gram_sums
    kept_count = gram_a.shape[0]
    gram = jnp.concatenate(
        [jnp.concatenate([gram_a, gram_q], axis=1), jnp.concatenate([gram_q.T, gram_a], axis=1)],
        axis=0,
    )
    rhs_both = jnp.concatenate([proj_re, proj_im], axis=0)
    lower = jnp.linalg.cholesky(gram)
    middle = lax.linalg.triangular_solve(lower, rhs_both, left_side=True, lower=True)
    coef = lax.linalg.triangular_solve(lower, middle, left_side=True, lower=True, transpose_a=True)
    coef_one = coef[:kept_count]
    coef_two = coef[kept_count:]
    locked_re32 = locked_re.astype(jnp.float32)
    locked_im32 = locked_im.astype(jnp.float32)
    out_re = (
        trial_re.astype(jnp.float32)
        - jnp.einsum("ab,an->bn", coef_one, locked_re32, precision=highest)
        + jnp.einsum("ab,an->bn", coef_two, locked_im32, precision=highest)
    )
    out_im = (
        trial_im.astype(jnp.float32)
        - jnp.einsum("ab,an->bn", coef_one, locked_im32, precision=highest)
        - jnp.einsum("ab,an->bn", coef_two, locked_re32, precision=highest)
    )
    return (out_re, out_im)


def solve_coef(gram_sums):
    gram_a, gram_q, proj_re, proj_im = gram_sums
    gram = jnp.concatenate(
        [jnp.concatenate([gram_a, gram_q], axis=1), jnp.concatenate([gram_q.T, gram_a], axis=1)],
        axis=0,
    )
    rhs_both = jnp.concatenate([proj_re, proj_im], axis=0)
    lower = jnp.linalg.cholesky(gram)
    middle = lax.linalg.triangular_solve(lower, rhs_both, left_side=True, lower=True)
    return lax.linalg.triangular_solve(lower, middle, left_side=True, lower=True, transpose_a=True)


def maxwell_pass(chunks, order, home_spans, waves, inv_diag, inv_corr, to_space_fn, to_spectrum_fn):
    moved = jnp.concatenate([to_space_fn(chunk) for chunk in chunks], axis=3)
    space = transform(moved, 2, 1.0, order)
    weighted = apply_tensor(space, inv_diag, inv_corr)
    wave_x, wave_y, wave_z = waves
    wide_count = space.shape[3] // sum(count for _, count in home_spans)
    local_x = sum(count for _, count in home_spans)
    finished = []
    for index, (start, count) in enumerate(home_spans):
        targets = (np.arange(wide_count)[:, None] * local_x + start + np.arange(count)[None, :]).reshape(-1)
        source = transform(weighted, 2, -1.0, None, targets)
        if index >= 2:
            source, _ = lax.optimization_barrier((source, finished[index - 2]))
        home = to_spectrum_fn(source)
        home = transform(home, 3, -1.0)
        home = transform(home, 4, -1.0)
        finished.append(curl_times_i((wave_x[start : start + count], wave_y, wave_z), home))
    return (jnp.concatenate(finished, axis=3), space, weighted)


def per_device(wide_count, trial_bands, locked_bands, inv_diag, inv_corr):
    band_count = trial_bands.shape[0]
    kept_count = locked_bands.shape[0]
    local_x = trial_bands.shape[3]
    grid_len = trial_bands.shape[4]
    rows = jnp.concatenate(
        [locked_bands.reshape((2 * kept_count,) + locked_bands.shape[2:]),
         trial_bands.reshape((2 * band_count,) + trial_bands.shape[2:])],
        axis=0,
    )
    pairs = jnp.einsum("icxyz,jcxyz->ij", rows, rows, preferred_element_type=jnp.float32)
    pairs = butterfly_sum(pairs, "wide", wide_count)
    lk = pairs[: 2 * kept_count, : 2 * kept_count].reshape(kept_count, 2, kept_count, 2)
    lt = pairs[: 2 * kept_count, 2 * kept_count :].reshape(kept_count, 2, band_count, 2)
    gram_a = lk[:, 0, :, 0] + lk[:, 1, :, 1]
    gram_q = lk[:, 1, :, 0] - lk[:, 0, :, 1]
    proj_re = lt[:, 0, :, 0] + lt[:, 1, :, 1]
    proj_im = lt[:, 0, :, 1] - lt[:, 1, :, 0]
    gram_sums = (gram_a, gram_q, proj_re, proj_im)
    coef = solve_coef(gram_sums)
    start_x = lax.axis_index("wide") * local_x
    full_axis = jnp.arange(grid_len, dtype=jnp.int32)
    wave_x = signed_wave(start_x + jnp.arange(local_x, dtype=jnp.int32), grid_len)
    wave_full = signed_wave(full_axis, grid_len)
    waves = (wave_x, wave_full, wave_full)

    def exchange_rows(field, split_dim, keep_dim):
        parts, bands, comps = field.shape[0], field.shape[1], field.shape[2]
        order = (split_dim, 1, 2, keep_dim, 0, 5)
        moved = jnp.transpose(field, order).reshape(wide_count, -1, 128)
        moved = lax.all_to_all(moved, "wide", split_axis=0, concat_axis=0, tiled=True)
        local_split = field.shape[split_dim] // wide_count
        moved = moved.reshape(
            wide_count, local_split, bands, comps, field.shape[keep_dim], parts, field.shape[5]
        )
        return moved

    def send_out_one(field):
        moved = exchange_rows(field, 4, 3)
        moved = jnp.transpose(moved, (5, 2, 3, 0, 4, 1, 6))
        shape = moved.shape
        return moved.reshape(shape[0], shape[1], shape[2], shape[3] * shape[4], shape[5], shape[6])

    def send_home_one(field):
        moved = exchange_rows(field, 3, 4)
        moved = jnp.transpose(moved, (5, 2, 3, 1, 0, 4, 6))
        shape = moved.shape
        return moved.reshape(shape[0], shape[1], shape[2], shape[3], shape[4] * shape[5], shape[6])

    first = (local_x + 1) // 2
    spans = [(0, first), (first, local_x - first)] if local_x > 1 else [(0, local_x)]
    chunks = [
        front_pass((0, 1, 2), coef.T, wave_x, trial_bands, locked_bands, start, count)
        for start, count in spans
    ]
    order = np.concatenate(
        [
            (np.arange(wide_count)[:, None] * local_x + start + np.arange(count)[None, :]).reshape(-1)
            for start, count in spans
        ]
    )
    pieces = min(3, local_x)
    cuts = [round(index * local_x / pieces) for index in range(pieces + 1)]
    home_spans = [(cuts[index], cuts[index + 1] - cuts[index]) for index in range(pieces)]
    results = [maxwell_pass(chunks, order, home_spans, waves, inv_diag, inv_corr, send_out_one, send_home_one)]
    applied_st, space, weighted = [
        jnp.concatenate([entry[slot] for entry in results], axis=1) for slot in range(3)
    ]
    applied = jnp.stack([applied_st[0], applied_st[1]], axis=1).astype(jnp.bfloat16)
    scale_all = 1.0 / float(grid_len * grid_len * grid_len)
    left_re = space[0].reshape(band_count, -1)
    left_im = space[1].reshape(band_count, -1)
    right_re = weighted[0].reshape(band_count, -1)
    right_im = weighted[1].reshape(band_count, -1)
    part_re = jnp.einsum("an,bn->ab", left_re, right_re, precision=highest) + jnp.einsum(
        "an,bn->ab", left_im, right_im, precision=highest
    )
    part_im = jnp.einsum("an,bn->ab", left_re, right_im, precision=highest) - jnp.einsum(
        "an,bn->ab", left_im, right_re, precision=highest
    )
    total_re, total_im = butterfly_sum(jnp.stack([part_re, part_im], axis=0), "wide", wide_count)
    rayleigh = jnp.stack([total_re * scale_all, total_im * scale_all], axis=0)
    return (applied, rayleigh)


def solution(mesh):
    in_specs = (
        P("groups", None, None, "wide", None, None),
        P("groups", None, None, "wide", None, None),
        P("groups", None, "wide", None),
        P("groups", None, "wide", None),
    )
    out_specs = (P("groups", None, None, "wide", None, None), P("groups", None, None))
    wide_count = mesh.shape["wide"]
    return jax.shard_map(
        functools.partial(per_device, wide_count), mesh=mesh, in_specs=in_specs, out_specs=out_specs, check_vma=False
    )
```

```python
import functools
import math

import ml_dtypes
import numpy as np

import jax
import jax.numpy as jnp
from jax import lax
from jax.sharding import PartitionSpec as P
from jax.experimental import pallas as pl
from jax.experimental.pallas import tpu as pltpu

highest = lax.Precision.HIGHEST
three_pass = lax.Precision.HIGH


def signed_wave(indices, length):
    shifted = jnp.where(indices < length // 2, indices, indices - length)
    return shifted.astype(jnp.float32) / (length / 2.0)


def cross_wave(wave_x, wave_y, wave_z, vectors):
    comp_x = vectors[..., 0, :, :, :]
    comp_y = vectors[..., 1, :, :, :]
    comp_z = vectors[..., 2, :, :, :]
    along_x = wave_x[:, None, None]
    along_y = wave_y[None, :, None]
    along_z = wave_z[None, None, :]
    return jnp.stack(
        [
            along_y * comp_z - along_z * comp_y,
            along_z * comp_x - along_x * comp_z,
            along_x * comp_y - along_y * comp_x,
        ],
        axis=-4,
    )


def curl_times_i(waves, stacked):
    wave_x, wave_y, wave_z = waves
    return jnp.stack(
        [
            -cross_wave(wave_x, wave_y, wave_z, stacked[1]),
            cross_wave(wave_x, wave_y, wave_z, stacked[0]),
        ],
        axis=0,
    )


def apply_tensor(vectors, inv_diag, inv_corr):
    coupling_xy = inv_corr[0] * jnp.sqrt(inv_diag[0] * inv_diag[1])
    coupling_xz = inv_corr[1] * jnp.sqrt(inv_diag[0] * inv_diag[2])
    coupling_yz = inv_corr[2] * jnp.sqrt(inv_diag[1] * inv_diag[2])
    comp_x = vectors[..., 0, :, :, :]
    comp_y = vectors[..., 1, :, :, :]
    comp_z = vectors[..., 2, :, :, :]
    out_x = inv_diag[0] * comp_x + coupling_xy * comp_y + coupling_xz * comp_z
    out_y = coupling_xy * comp_x + inv_diag[1] * comp_y + coupling_yz * comp_z
    out_z = coupling_xz * comp_x + coupling_yz * comp_y + inv_diag[2] * comp_z
    return jnp.stack([out_x, out_y, out_z], axis=-4)


def complex_table(length, orient):
    indices = jnp.arange(length, dtype=jnp.int32)
    phases = indices[:, None] * indices[None, :] % length
    angles = phases.astype(jnp.float32) * (2.0 * math.pi / length)
    norm_factor = 1.0 / math.sqrt(length)
    cos_table = jnp.cos(angles) * norm_factor
    sin_table = jnp.sin(angles) * norm_factor * orient
    return jnp.stack(
        [jnp.stack([cos_table, sin_table], axis=0), jnp.stack([-sin_table, cos_table], axis=0)],
        axis=0,
    )


def transform(stacked, axis_dim, orient):
    table = complex_table(stacked.shape[axis_dim + 1], orient)
    if axis_dim == 2:
        return jnp.einsum("pbckyz,pqkn->qbcnyz", stacked, table, precision=three_pass)
    if axis_dim == 3:
        return jnp.einsum("pbcxkz,pqkn->qbcxnz", stacked, table, precision=three_pass)
    return jnp.einsum("pbcxyk,pqkn->qbcxyn", stacked, table, precision=three_pass)


def split_hi_lo(values):
    scaled = values * 65537.0
    top = scaled - (scaled - values)
    return top.astype(jnp.bfloat16), (values - top).astype(jnp.bfloat16)


def dot_right(values, table_hi, table_lo):
    high, low = split_hi_lo(values)
    f32 = jnp.float32
    return (
        jnp.dot(high, table_hi, preferred_element_type=f32)
        + jnp.dot(low, table_hi, preferred_element_type=f32)
        + jnp.dot(high, table_lo, preferred_element_type=f32)
    )


def dot_left(table_hi, table_lo, values):
    high, low = split_hi_lo(values)
    f32 = jnp.float32
    return (
        jnp.dot(table_hi, high, preferred_element_type=f32)
        + jnp.dot(table_hi, low, preferred_element_type=f32)
        + jnp.dot(table_lo, high, preferred_element_type=f32)
    )


def front_kernel(comps, coef_ref, qx_ref, trial_ref, locked_ref, chi_ref, clo_ref, shi_ref, slo_ref, out_ref):
    band = pl.program_id(0)
    plane = pl.program_id(1)
    kept = locked_ref.shape[0]
    size = trial_ref.shape[-1]
    f32 = jnp.float32
    first = [coef_ref[band, k] for k in range(kept)]
    second = [coef_ref[band, kept + k] for k in range(kept)]
    needed = sorted({(c + 1) % 3 for c in comps} | {(c + 2) % 3 for c in comps})
    part_re = {}
    part_im = {}
    for comp in needed:
        acc_re = trial_ref[0, 0, comp, 0].astype(f32)
        acc_im = trial_ref[0, 1, comp, 0].astype(f32)
        for k in range(kept):
            l_re = locked_ref[k, 0, comp, 0].astype(f32)
            l_im = locked_ref[k, 1, comp, 0].astype(f32)
            acc_re = acc_re - first[k] * l_re + second[k] * l_im
            acc_im = acc_im - first[k] * l_im - second[k] * l_re
        part_re[comp] = acc_re
        part_im[comp] = acc_im
    rows = lax.broadcasted_iota(jnp.int32, (size, 1), 0)
    cols = lax.broadcasted_iota(jnp.int32, (1, size), 1)
    half = size // 2
    wave_y = jnp.where(rows < half, rows, rows - size).astype(f32) / (size / 2.0)
    wave_z = jnp.where(cols < half, cols, cols - size).astype(f32) / (size / 2.0)
    waves = (qx_ref[plane], wave_y, wave_z)
    c_hi = chi_ref[...]
    c_lo = clo_ref[...]
    s_hi = shi_ref[...]
    s_lo = slo_ref[...]
    for slot, comp in enumerate(comps):
        a = (comp + 1) % 3
        b = (comp + 2) % 3
        cur_re = -(waves[a] * part_im[b] - waves[b] * part_im[a])
        cur_im = waves[a] * part_re[b] - waves[b] * part_re[a]
        z_re = dot_right(cur_re, c_hi, c_lo) - dot_right(cur_im, s_hi, s_lo)
        z_im = dot_right(cur_re, s_hi, s_lo) + dot_right(cur_im, c_hi, c_lo)
        y_re = dot_left(c_hi, c_lo, z_re) - dot_left(s_hi, s_lo, z_im)
        y_im = dot_left(s_hi, s_lo, z_re) + dot_left(c_hi, c_lo, z_im)
        out_ref[0, 0, slot, 0] = y_re
        out_ref[1, 0, slot, 0] = y_im


def numpy_split(table):
    full = table.astype(np.float32)
    high = full.astype(ml_dtypes.bfloat16)
    low = (full - high.astype(np.float32)).astype(ml_dtypes.bfloat16)
    return jnp.asarray(high), jnp.asarray(low)


def dft_tables(length, orient):
    indices = np.arange(length, dtype=np.int64)
    phases = indices[:, None] * indices[None, :] % length
    angles = phases.astype(np.float64) * (2.0 * math.pi / length)
    norm_factor = 1.0 / math.sqrt(length)
    c_hi, c_lo = numpy_split(np.cos(angles) * norm_factor)
    s_hi, s_lo = numpy_split(np.sin(angles) * norm_factor * orient)
    return c_hi, c_lo, s_hi, s_lo


def front_pass(comps, coef_rows, wave_x, trial_bands, locked_bands):
    band_count, _, _, local_x, size, _ = trial_bands.shape
    kept = locked_bands.shape[0]
    tables = dft_tables(size, 1.0)
    smem = pl.BlockSpec(memory_space=pltpu.SMEM)
    table_spec = pl.BlockSpec((size, size), lambda b, x: (0, 0))
    width = len(comps)
    return pl.pallas_call(
        functools.partial(front_kernel, comps),
        grid=(band_count, local_x),
        in_specs=[
            smem,
            smem,
            pl.BlockSpec((1, 2, 3, 1, size, size), lambda b, x: (b, 0, 0, x, 0, 0)),
            pl.BlockSpec((kept, 2, 3, 1, size, size), lambda b, x: (0, 0, 0, x, 0, 0)),
            table_spec,
            table_spec,
            table_spec,
            table_spec,
        ],
        out_specs=pl.BlockSpec((2, 1, width, 1, size, size), lambda b, x: (0, b, 0, x, 0, 0)),
        out_shape=jax.ShapeDtypeStruct((2, band_count, width, local_x, size, size), jnp.float32),
    )(coef_rows, wave_x, trial_bands, locked_bands, *tables)


def butterfly_sum(values, axis, count):
    if count & (count - 1):
        return lax.psum(values, axis)
    step = 1
    while step < count:
        pairs = [(index, index ^ step) for index in range(count)]
        values = values + lax.ppermute(values, axis, pairs)
        step *= 2
    return values


def inner_sum(left_rows, right_rows):
    return jnp.einsum("an,bn->ab", left_rows, right_rows, preferred_element_type=jnp.float32)


def remove_locked(gram_sums, trial_re, trial_im, locked_re, locked_im):
    gram_a, gram_q, proj_re, proj_im = gram_sums
    kept_count = gram_a.shape[0]
    gram = jnp.concatenate(
        [jnp.concatenate([gram_a, gram_q], axis=1), jnp.concatenate([gram_q.T, gram_a], axis=1)],
        axis=0,
    )
    rhs_both = jnp.concatenate([proj_re, proj_im], axis=0)
    lower = jnp.linalg.cholesky(gram)
    middle = lax.linalg.triangular_solve(lower, rhs_both, left_side=True, lower=True)
    coef = lax.linalg.triangular_solve(lower, middle, left_side=True, lower=True, transpose_a=True)
    coef_one = coef[:kept_count]
    coef_two = coef[kept_count:]
    locked_re32 = locked_re.astype(jnp.float32)
    locked_im32 = locked_im.astype(jnp.float32)
    out_re = (
        trial_re.astype(jnp.float32)
        - jnp.einsum("ab,an->bn", coef_one, locked_re32, precision=highest)
        + jnp.einsum("ab,an->bn", coef_two, locked_im32, precision=highest)
    )
    out_im = (
        trial_im.astype(jnp.float32)
        - jnp.einsum("ab,an->bn", coef_one, locked_im32, precision=highest)
        - jnp.einsum("ab,an->bn", coef_two, locked_re32, precision=highest)
    )
    return (out_re, out_im)


def solve_coef(gram_sums):
    gram_a, gram_q, proj_re, proj_im = gram_sums
    gram = jnp.concatenate(
        [jnp.concatenate([gram_a, gram_q], axis=1), jnp.concatenate([gram_q.T, gram_a], axis=1)],
        axis=0,
    )
    rhs_both = jnp.concatenate([proj_re, proj_im], axis=0)
    lower = jnp.linalg.cholesky(gram)
    middle = lax.linalg.triangular_solve(lower, rhs_both, left_side=True, lower=True)
    return lax.linalg.triangular_solve(lower, middle, left_side=True, lower=True, transpose_a=True)


def maxwell_pass(chunks, waves, inv_diag, inv_corr, to_space_fn, to_spectrum_fn):
    space = jnp.concatenate([transform(to_space_fn(chunk), 2, 1.0) for chunk in chunks], axis=2)
    weighted = apply_tensor(space, inv_diag, inv_corr)
    homes = []
    for comp in range(weighted.shape[2]):
        source = transform(weighted[:, :, comp : comp + 1], 2, -1.0)
        if comp >= 2:
            source, _ = lax.optimization_barrier((source, homes[comp - 2]))
        home = to_spectrum_fn(source)
        home = transform(home, 3, -1.0)
        homes.append(transform(home, 4, -1.0))
    home = jnp.concatenate(homes, axis=2)
    return (curl_times_i(waves, home), space, weighted)


def per_device(wide_count, trial_bands, locked_bands, inv_diag, inv_corr):
    band_count = trial_bands.shape[0]
    kept_count = locked_bands.shape[0]
    local_x = trial_bands.shape[3]
    grid_len = trial_bands.shape[4]
    rows = jnp.concatenate(
        [locked_bands.reshape((2 * kept_count,) + locked_bands.shape[2:]),
         trial_bands.reshape((2 * band_count,) + trial_bands.shape[2:])],
        axis=0,
    )
    pairs = jnp.einsum("icxyz,jcxyz->ij", rows, rows, preferred_element_type=jnp.float32)
    pairs = jnp.sum(lax.all_gather(pairs, "wide"), axis=0)
    lk = pairs[: 2 * kept_count, : 2 * kept_count].reshape(kept_count, 2, kept_count, 2)
    lt = pairs[: 2 * kept_count, 2 * kept_count :].reshape(kept_count, 2, band_count, 2)
    gram_a = lk[:, 0, :, 0] + lk[:, 1, :, 1]
    gram_q = lk[:, 1, :, 0] - lk[:, 0, :, 1]
    proj_re = lt[:, 0, :, 0] + lt[:, 1, :, 1]
    proj_im = lt[:, 0, :, 1] - lt[:, 1, :, 0]
    gram_sums = (gram_a, gram_q, proj_re, proj_im)
    coef = solve_coef(gram_sums)
    start_x = lax.axis_index("wide") * local_x
    full_axis = jnp.arange(grid_len, dtype=jnp.int32)
    wave_x = signed_wave(start_x + jnp.arange(local_x, dtype=jnp.int32), grid_len)
    wave_full = signed_wave(full_axis, grid_len)
    waves = (wave_x, wave_full, wave_full)

    def exchange_rows(field, split_dim, keep_dim):
        parts, bands, comps = field.shape[0], field.shape[1], field.shape[2]
        order = (split_dim, 1, 2, keep_dim, 0, 5)
        moved = jnp.transpose(field, order).reshape(wide_count, -1, 128)
        moved = lax.all_to_all(moved, "wide", split_axis=0, concat_axis=0, tiled=True)
        local_split = field.shape[split_dim] // wide_count
        moved = moved.reshape(
            wide_count, local_split, bands, comps, field.shape[keep_dim], parts, field.shape[5]
        )
        return moved

    def send_out_one(field):
        moved = exchange_rows(field, 4, 3)
        moved = jnp.transpose(moved, (5, 2, 3, 0, 4, 1, 6))
        shape = moved.shape
        return moved.reshape(shape[0], shape[1], shape[2], shape[3] * shape[4], shape[5], shape[6])

    def send_home_one(field):
        moved = exchange_rows(field, 3, 4)
        moved = jnp.transpose(moved, (5, 2, 3, 1, 0, 4, 6))
        shape = moved.shape
        return moved.reshape(shape[0], shape[1], shape[2], shape[3], shape[4] * shape[5], shape[6])

    chunks = [front_pass((comp,), coef.T, wave_x, trial_bands, locked_bands) for comp in range(3)]
    results = [maxwell_pass(chunks, waves, inv_diag, inv_corr, send_out_one, send_home_one)]
    applied_st, space, weighted = [
        jnp.concatenate([entry[slot] for entry in results], axis=1) for slot in range(3)
    ]
    applied = jnp.stack([applied_st[0], applied_st[1]], axis=1).astype(jnp.bfloat16)
    scale_all = 1.0 / float(grid_len * grid_len * grid_len)
    left_re = space[0].reshape(band_count, -1)
    left_im = space[1].reshape(band_count, -1)
    right_re = weighted[0].reshape(band_count, -1)
    right_im = weighted[1].reshape(band_count, -1)
    part_re = jnp.einsum("an,bn->ab", left_re, right_re, precision=highest) + jnp.einsum(
        "an,bn->ab", left_im, right_im, precision=highest
    )
    part_im = jnp.einsum("an,bn->ab", left_re, right_im, precision=highest) - jnp.einsum(
        "an,bn->ab", left_im, right_re, precision=highest
    )
    total_re, total_im = butterfly_sum(jnp.stack([part_re, part_im], axis=0), "wide", wide_count)
    rayleigh = jnp.stack([total_re * scale_all, total_im * scale_all], axis=0)
    return (applied, rayleigh)


def solution(mesh):
    in_specs = (
        P("groups", None, None, "wide", None, None),
        P("groups", None, None, "wide", None, None),
        P("groups", None, "wide", None),
        P("groups", None, "wide", None),
    )
    out_specs = (P("groups", None, None, "wide", None, None), P("groups", None, None))
    wide_count = mesh.shape["wide"]
    return jax.shard_map(
        functools.partial(per_device, wide_count), mesh=mesh, in_specs=in_specs, out_specs=out_specs, check_vma=False
    )
```

```python
import functools
import math

import ml_dtypes
import numpy as np

import jax
import jax.numpy as jnp
from jax import lax
from jax.sharding import PartitionSpec as P
from jax.experimental import pallas as pl
from jax.experimental.pallas import tpu as pltpu

highest = lax.Precision.HIGHEST
three_pass = lax.Precision.HIGH


def signed_wave(indices, length):
    shifted = jnp.where(indices < length // 2, indices, indices - length)
    return shifted.astype(jnp.float32) / (length / 2.0)


def cross_wave(wave_x, wave_y, wave_z, vectors):
    comp_x = vectors[..., 0, :, :, :]
    comp_y = vectors[..., 1, :, :, :]
    comp_z = vectors[..., 2, :, :, :]
    along_x = wave_x[:, None, None]
    along_y = wave_y[None, :, None]
    along_z = wave_z[None, None, :]
    return jnp.stack(
        [
            along_y * comp_z - along_z * comp_y,
            along_z * comp_x - along_x * comp_z,
            along_x * comp_y - along_y * comp_x,
        ],
        axis=-4,
    )


def curl_times_i(waves, stacked):
    wave_x, wave_y, wave_z = waves
    return jnp.stack(
        [
            -cross_wave(wave_x, wave_y, wave_z, stacked[1]),
            cross_wave(wave_x, wave_y, wave_z, stacked[0]),
        ],
        axis=0,
    )


def apply_tensor(vectors, inv_diag, inv_corr):
    coupling_xy = inv_corr[0] * jnp.sqrt(inv_diag[0] * inv_diag[1])
    coupling_xz = inv_corr[1] * jnp.sqrt(inv_diag[0] * inv_diag[2])
    coupling_yz = inv_corr[2] * jnp.sqrt(inv_diag[1] * inv_diag[2])
    comp_x = vectors[..., 0, :, :, :]
    comp_y = vectors[..., 1, :, :, :]
    comp_z = vectors[..., 2, :, :, :]
    out_x = inv_diag[0] * comp_x + coupling_xy * comp_y + coupling_xz * comp_z
    out_y = coupling_xy * comp_x + inv_diag[1] * comp_y + coupling_yz * comp_z
    out_z = coupling_xz * comp_x + coupling_yz * comp_y + inv_diag[2] * comp_z
    return jnp.stack([out_x, out_y, out_z], axis=-4)


def complex_table(length, orient):
    indices = jnp.arange(length, dtype=jnp.int32)
    phases = indices[:, None] * indices[None, :] % length
    angles = phases.astype(jnp.float32) * (2.0 * math.pi / length)
    norm_factor = 1.0 / math.sqrt(length)
    cos_table = jnp.cos(angles) * norm_factor
    sin_table = jnp.sin(angles) * norm_factor * orient
    return jnp.stack(
        [jnp.stack([cos_table, sin_table], axis=0), jnp.stack([-sin_table, cos_table], axis=0)],
        axis=0,
    )


def transform(stacked, axis_dim, orient):
    table = complex_table(stacked.shape[axis_dim + 1], orient)
    if axis_dim == 2:
        return jnp.einsum("pbckyz,pqkn->qbcnyz", stacked, table, precision=three_pass)
    if axis_dim == 3:
        return jnp.einsum("pbcxkz,pqkn->qbcxnz", stacked, table, precision=three_pass)
    return jnp.einsum("pbcxyk,pqkn->qbcxyn", stacked, table, precision=three_pass)


def split_hi_lo(values):
    scaled = values * 65537.0
    top = scaled - (scaled - values)
    return top.astype(jnp.bfloat16), (values - top).astype(jnp.bfloat16)


def dot_right(values, table_hi, table_lo):
    high, low = split_hi_lo(values)
    f32 = jnp.float32
    return (
        jnp.dot(high, table_hi, preferred_element_type=f32)
        + jnp.dot(low, table_hi, preferred_element_type=f32)
        + jnp.dot(high, table_lo, preferred_element_type=f32)
    )


def dot_left(table_hi, table_lo, values):
    high, low = split_hi_lo(values)
    f32 = jnp.float32
    return (
        jnp.dot(table_hi, high, preferred_element_type=f32)
        + jnp.dot(table_hi, low, preferred_element_type=f32)
        + jnp.dot(table_lo, high, preferred_element_type=f32)
    )


def front_kernel(comps, coef_ref, qx_ref, trial_ref, locked_ref, chi_ref, clo_ref, shi_ref, slo_ref, out_ref):
    band = pl.program_id(0)
    plane = pl.program_id(1)
    kept = locked_ref.shape[0]
    size = trial_ref.shape[-1]
    f32 = jnp.float32
    first = [coef_ref[band, k] for k in range(kept)]
    second = [coef_ref[band, kept + k] for k in range(kept)]
    needed = sorted({(c + 1) % 3 for c in comps} | {(c + 2) % 3 for c in comps})
    part_re = {}
    part_im = {}
    for comp in needed:
        acc_re = trial_ref[0, 0, comp, 0].astype(f32)
        acc_im = trial_ref[0, 1, comp, 0].astype(f32)
        for k in range(kept):
            l_re = locked_ref[k, 0, comp, 0].astype(f32)
            l_im = locked_ref[k, 1, comp, 0].astype(f32)
            acc_re = acc_re - first[k] * l_re + second[k] * l_im
            acc_im = acc_im - first[k] * l_im - second[k] * l_re
        part_re[comp] = acc_re
        part_im[comp] = acc_im
    rows = lax.broadcasted_iota(jnp.int32, (size, 1), 0)
    cols = lax.broadcasted_iota(jnp.int32, (1, size), 1)
    half = size // 2
    wave_y = jnp.where(rows < half, rows, rows - size).astype(f32) / (size / 2.0)
    wave_z = jnp.where(cols < half, cols, cols - size).astype(f32) / (size / 2.0)
    waves = (qx_ref[plane], wave_y, wave_z)
    c_hi = chi_ref[...]
    c_lo = clo_ref[...]
    s_hi = shi_ref[...]
    s_lo = slo_ref[...]
    for slot, comp in enumerate(comps):
        a = (comp + 1) % 3
        b = (comp + 2) % 3
        cur_re = -(waves[a] * part_im[b] - waves[b] * part_im[a])
        cur_im = waves[a] * part_re[b] - waves[b] * part_re[a]
        z_re = dot_right(cur_re, c_hi, c_lo) - dot_right(cur_im, s_hi, s_lo)
        z_im = dot_right(cur_re, s_hi, s_lo) + dot_right(cur_im, c_hi, c_lo)
        y_re = dot_left(c_hi, c_lo, z_re) - dot_left(s_hi, s_lo, z_im)
        y_im = dot_left(s_hi, s_lo, z_re) + dot_left(c_hi, c_lo, z_im)
        out_ref[0, 0, slot, 0] = y_re
        out_ref[1, 0, slot, 0] = y_im


def numpy_split(table):
    full = table.astype(np.float32)
    high = full.astype(ml_dtypes.bfloat16)
    low = (full - high.astype(np.float32)).astype(ml_dtypes.bfloat16)
    return jnp.asarray(high), jnp.asarray(low)


def dft_tables(length, orient):
    indices = np.arange(length, dtype=np.int64)
    phases = indices[:, None] * indices[None, :] % length
    angles = phases.astype(np.float64) * (2.0 * math.pi / length)
    norm_factor = 1.0 / math.sqrt(length)
    c_hi, c_lo = numpy_split(np.cos(angles) * norm_factor)
    s_hi, s_lo = numpy_split(np.sin(angles) * norm_factor * orient)
    return c_hi, c_lo, s_hi, s_lo


def front_pass(comps, coef_rows, wave_x, trial_bands, locked_bands):
    band_count, _, _, local_x, size, _ = trial_bands.shape
    kept = locked_bands.shape[0]
    tables = dft_tables(size, 1.0)
    smem = pl.BlockSpec(memory_space=pltpu.SMEM)
    table_spec = pl.BlockSpec((size, size), lambda b, x: (0, 0))
    width = len(comps)
    return pl.pallas_call(
        functools.partial(front_kernel, comps),
        grid=(band_count, local_x),
        in_specs=[
            smem,
            smem,
            pl.BlockSpec((1, 2, 3, 1, size, size), lambda b, x: (b, 0, 0, x, 0, 0)),
            pl.BlockSpec((kept, 2, 3, 1, size, size), lambda b, x: (0, 0, 0, x, 0, 0)),
            table_spec,
            table_spec,
            table_spec,
            table_spec,
        ],
        out_specs=pl.BlockSpec((2, 1, width, 1, size, size), lambda b, x: (0, b, 0, x, 0, 0)),
        out_shape=jax.ShapeDtypeStruct((2, band_count, width, local_x, size, size), jnp.float32),
    )(coef_rows, wave_x, trial_bands, locked_bands, *tables)


def radix_sum(values, axis, count):
    if count & (count - 1):
        return lax.psum(values, axis)
    me = lax.axis_index(axis)
    stride = 1
    while stride < count:
        radix = 4 if count // stride >= 4 else 2
        digit = (me // stride) % radix
        slots = [None] * radix
        for offset in range(radix):
            if offset == 0:
                got = values
            else:
                pairs = []
                for dst in range(count):
                    dst_digit = (dst // stride) % radix
                    base = dst - dst_digit * stride
                    pairs.append((base + ((dst_digit + offset) % radix) * stride, dst))
                got = lax.ppermute(values, axis, pairs)
            slots[offset] = got
        ordered = []
        for member in range(radix):
            pick = slots[0]
            for offset in range(1, radix):
                pick = jnp.where((digit + offset) % radix == member, slots[offset], pick)
            ordered.append(pick)
        total = ordered[0]
        for member in range(1, radix):
            total = total + ordered[member]
        values = total
        stride *= radix
    return values


def butterfly_sum(values, axis, count):
    if count & (count - 1):
        return lax.psum(values, axis)
    step = 1
    while step < count:
        pairs = [(index, index ^ step) for index in range(count)]
        values = values + lax.ppermute(values, axis, pairs)
        step *= 2
    return values


def inner_sum(left_rows, right_rows):
    return jnp.einsum("an,bn->ab", left_rows, right_rows, preferred_element_type=jnp.float32)


def remove_locked(gram_sums, trial_re, trial_im, locked_re, locked_im):
    gram_a, gram_q, proj_re, proj_im = gram_sums
    kept_count = gram_a.shape[0]
    gram = jnp.concatenate(
        [jnp.concatenate([gram_a, gram_q], axis=1), jnp.concatenate([gram_q.T, gram_a], axis=1)],
        axis=0,
    )
    rhs_both = jnp.concatenate([proj_re, proj_im], axis=0)
    lower = jnp.linalg.cholesky(gram)
    middle = lax.linalg.triangular_solve(lower, rhs_both, left_side=True, lower=True)
    coef = lax.linalg.triangular_solve(lower, middle, left_side=True, lower=True, transpose_a=True)
    coef_one = coef[:kept_count]
    coef_two = coef[kept_count:]
    locked_re32 = locked_re.astype(jnp.float32)
    locked_im32 = locked_im.astype(jnp.float32)
    out_re = (
        trial_re.astype(jnp.float32)
        - jnp.einsum("ab,an->bn", coef_one, locked_re32, precision=highest)
        + jnp.einsum("ab,an->bn", coef_two, locked_im32, precision=highest)
    )
    out_im = (
        trial_im.astype(jnp.float32)
        - jnp.einsum("ab,an->bn", coef_one, locked_im32, precision=highest)
        - jnp.einsum("ab,an->bn", coef_two, locked_re32, precision=highest)
    )
    return (out_re, out_im)


def solve_coef(gram_sums):
    gram_a, gram_q, proj_re, proj_im = gram_sums
    gram = jnp.concatenate(
        [jnp.concatenate([gram_a, gram_q], axis=1), jnp.concatenate([gram_q.T, gram_a], axis=1)],
        axis=0,
    )
    rhs_both = jnp.concatenate([proj_re, proj_im], axis=0)
    lower = jnp.linalg.cholesky(gram)
    middle = lax.linalg.triangular_solve(lower, rhs_both, left_side=True, lower=True)
    return lax.linalg.triangular_solve(lower, middle, left_side=True, lower=True, transpose_a=True)


def maxwell_pass(chunks, waves, inv_diag, inv_corr, to_space_fn, to_spectrum_fn):
    space = jnp.concatenate([transform(to_space_fn(chunk), 2, 1.0) for chunk in chunks], axis=2)
    weighted = apply_tensor(space, inv_diag, inv_corr)
    homes = []
    for comp in range(weighted.shape[2]):
        source = transform(weighted[:, :, comp : comp + 1], 2, -1.0)
        if comp >= 2:
            source, _ = lax.optimization_barrier((source, homes[comp - 2]))
        home = to_spectrum_fn(source)
        home = transform(home, 3, -1.0)
        homes.append(transform(home, 4, -1.0))
    home = jnp.concatenate(homes, axis=2)
    return (curl_times_i(waves, home), space, weighted)


def per_device(wide_count, trial_bands, locked_bands, inv_diag, inv_corr):
    band_count = trial_bands.shape[0]
    kept_count = locked_bands.shape[0]
    local_x = trial_bands.shape[3]
    grid_len = trial_bands.shape[4]
    rows = jnp.concatenate(
        [locked_bands.reshape((2 * kept_count,) + locked_bands.shape[2:]),
         trial_bands.reshape((2 * band_count,) + trial_bands.shape[2:])],
        axis=0,
    )
    pairs = jnp.einsum("icxyz,jcxyz->ij", rows, rows, preferred_element_type=jnp.float32)
    pairs = radix_sum(pairs, "wide", wide_count)
    lk = pairs[: 2 * kept_count, : 2 * kept_count].reshape(kept_count, 2, kept_count, 2)
    lt = pairs[: 2 * kept_count, 2 * kept_count :].reshape(kept_count, 2, band_count, 2)
    gram_a = lk[:, 0, :, 0] + lk[:, 1, :, 1]
    gram_q = lk[:, 1, :, 0] - lk[:, 0, :, 1]
    proj_re = lt[:, 0, :, 0] + lt[:, 1, :, 1]
    proj_im = lt[:, 0, :, 1] - lt[:, 1, :, 0]
    gram_sums = (gram_a, gram_q, proj_re, proj_im)
    coef = solve_coef(gram_sums)
    start_x = lax.axis_index("wide") * local_x
    full_axis = jnp.arange(grid_len, dtype=jnp.int32)
    wave_x = signed_wave(start_x + jnp.arange(local_x, dtype=jnp.int32), grid_len)
    wave_full = signed_wave(full_axis, grid_len)
    waves = (wave_x, wave_full, wave_full)

    def exchange_rows(field, split_dim, keep_dim):
        parts, bands, comps = field.shape[0], field.shape[1], field.shape[2]
        order = (split_dim, 1, 2, keep_dim, 0, 5)
        moved = jnp.transpose(field, order).reshape(wide_count, -1, 128)
        moved = lax.all_to_all(moved, "wide", split_axis=0, concat_axis=0, tiled=True)
        local_split = field.shape[split_dim] // wide_count
        moved = moved.reshape(
            wide_count, local_split, bands, comps, field.shape[keep_dim], parts, field.shape[5]
        )
        return moved

    def send_out_one(field):
        moved = exchange_rows(field, 4, 3)
        moved = jnp.transpose(moved, (5, 2, 3, 0, 4, 1, 6))
        shape = moved.shape
        return moved.reshape(shape[0], shape[1], shape[2], shape[3] * shape[4], shape[5], shape[6])

    def send_home_one(field):
        moved = exchange_rows(field, 3, 4)
        moved = jnp.transpose(moved, (5, 2, 3, 1, 0, 4, 6))
        shape = moved.shape
        return moved.reshape(shape[0], shape[1], shape[2], shape[3], shape[4] * shape[5], shape[6])

    chunks = [front_pass((comp,), coef.T, wave_x, trial_bands, locked_bands) for comp in range(3)]
    results = [maxwell_pass(chunks, waves, inv_diag, inv_corr, send_out_one, send_home_one)]
    applied_st, space, weighted = [
        jnp.concatenate([entry[slot] for entry in results], axis=1) for slot in range(3)
    ]
    applied = jnp.stack([applied_st[0], applied_st[1]], axis=1).astype(jnp.bfloat16)
    scale_all = 1.0 / float(grid_len * grid_len * grid_len)
    left_re = space[0].reshape(band_count, -1)
    left_im = space[1].reshape(band_count, -1)
    right_re = weighted[0].reshape(band_count, -1)
    right_im = weighted[1].reshape(band_count, -1)
    part_re = jnp.einsum("an,bn->ab", left_re, right_re, precision=highest) + jnp.einsum(
        "an,bn->ab", left_im, right_im, precision=highest
    )
    part_im = jnp.einsum("an,bn->ab", left_re, right_im, precision=highest) - jnp.einsum(
        "an,bn->ab", left_im, right_re, precision=highest
    )
    total_re, total_im = butterfly_sum(jnp.stack([part_re, part_im], axis=0), "wide", wide_count)
    rayleigh = jnp.stack([total_re * scale_all, total_im * scale_all], axis=0)
    return (applied, rayleigh)


def solution(mesh):
    in_specs = (
        P("groups", None, None, "wide", None, None),
        P("groups", None, None, "wide", None, None),
        P("groups", None, "wide", None),
        P("groups", None, "wide", None),
    )
    out_specs = (P("groups", None, None, "wide", None, None), P("groups", None, None))
    wide_count = mesh.shape["wide"]
    return jax.shard_map(
        functools.partial(per_device, wide_count), mesh=mesh, in_specs=in_specs, out_specs=out_specs, check_vma=False
    )
```

```python
import functools
import math

import ml_dtypes
import numpy as np

import jax
import jax.numpy as jnp
from jax import lax
from jax.sharding import PartitionSpec as P
from jax.experimental import pallas as pl
from jax.experimental.pallas import tpu as pltpu

highest = lax.Precision.HIGHEST
three_pass = lax.Precision.HIGH


def signed_wave(indices, length):
    shifted = jnp.where(indices < length // 2, indices, indices - length)
    return shifted.astype(jnp.float32) / (length / 2.0)


def cross_wave(wave_x, wave_y, wave_z, vectors):
    comp_x = vectors[..., 0, :, :, :]
    comp_y = vectors[..., 1, :, :, :]
    comp_z = vectors[..., 2, :, :, :]
    along_x = wave_x[:, None, None]
    along_y = wave_y[None, :, None]
    along_z = wave_z[None, None, :]
    return jnp.stack(
        [
            along_y * comp_z - along_z * comp_y,
            along_z * comp_x - along_x * comp_z,
            along_x * comp_y - along_y * comp_x,
        ],
        axis=-4,
    )


def curl_times_i(waves, stacked):
    wave_x, wave_y, wave_z = waves
    return jnp.stack(
        [
            -cross_wave(wave_x, wave_y, wave_z, stacked[1]),
            cross_wave(wave_x, wave_y, wave_z, stacked[0]),
        ],
        axis=0,
    )


def apply_tensor(vectors, inv_diag, inv_corr):
    coupling_xy = inv_corr[0] * jnp.sqrt(inv_diag[0] * inv_diag[1])
    coupling_xz = inv_corr[1] * jnp.sqrt(inv_diag[0] * inv_diag[2])
    coupling_yz = inv_corr[2] * jnp.sqrt(inv_diag[1] * inv_diag[2])
    comp_x = vectors[..., 0, :, :, :]
    comp_y = vectors[..., 1, :, :, :]
    comp_z = vectors[..., 2, :, :, :]
    out_x = inv_diag[0] * comp_x + coupling_xy * comp_y + coupling_xz * comp_z
    out_y = coupling_xy * comp_x + inv_diag[1] * comp_y + coupling_yz * comp_z
    out_z = coupling_xz * comp_x + coupling_yz * comp_y + inv_diag[2] * comp_z
    return jnp.stack([out_x, out_y, out_z], axis=-4)


def complex_table(length, orient):
    indices = jnp.arange(length, dtype=jnp.int32)
    phases = indices[:, None] * indices[None, :] % length
    angles = phases.astype(jnp.float32) * (2.0 * math.pi / length)
    norm_factor = 1.0 / math.sqrt(length)
    cos_table = jnp.cos(angles) * norm_factor
    sin_table = jnp.sin(angles) * norm_factor * orient
    return jnp.stack(
        [jnp.stack([cos_table, sin_table], axis=0), jnp.stack([-sin_table, cos_table], axis=0)],
        axis=0,
    )


def transform(stacked, axis_dim, orient):
    table = complex_table(stacked.shape[axis_dim + 1], orient)
    if axis_dim == 2:
        return jnp.einsum("pbckyz,pqkn->qbcnyz", stacked, table, precision=three_pass)
    if axis_dim == 3:
        return jnp.einsum("pbcxkz,pqkn->qbcxnz", stacked, table, precision=three_pass)
    return jnp.einsum("pbcxyk,pqkn->qbcxyn", stacked, table, precision=three_pass)


def split_hi_lo(values):
    scaled = values * 65537.0
    top = scaled - (scaled - values)
    return top.astype(jnp.bfloat16), (values - top).astype(jnp.bfloat16)


def dot_right(values, table_hi, table_lo):
    high, low = split_hi_lo(values)
    f32 = jnp.float32
    return (
        jnp.dot(high, table_hi, preferred_element_type=f32)
        + jnp.dot(low, table_hi, preferred_element_type=f32)
        + jnp.dot(high, table_lo, preferred_element_type=f32)
    )


def dot_left(table_hi, table_lo, values):
    high, low = split_hi_lo(values)
    f32 = jnp.float32
    return (
        jnp.dot(table_hi, high, preferred_element_type=f32)
        + jnp.dot(table_hi, low, preferred_element_type=f32)
        + jnp.dot(table_lo, high, preferred_element_type=f32)
    )


def front_kernel(comps, coef_ref, qx_ref, trial_ref, locked_ref, chi_ref, clo_ref, shi_ref, slo_ref, out_ref):
    band = pl.program_id(0)
    plane = pl.program_id(1)
    kept = locked_ref.shape[0]
    size = trial_ref.shape[-1]
    f32 = jnp.float32
    first = [coef_ref[band, k] for k in range(kept)]
    second = [coef_ref[band, kept + k] for k in range(kept)]
    needed = sorted({(c + 1) % 3 for c in comps} | {(c + 2) % 3 for c in comps})
    part_re = {}
    part_im = {}
    for comp in needed:
        acc_re = trial_ref[0, 0, comp, 0].astype(f32)
        acc_im = trial_ref[0, 1, comp, 0].astype(f32)
        for k in range(kept):
            l_re = locked_ref[k, 0, comp, 0].astype(f32)
            l_im = locked_ref[k, 1, comp, 0].astype(f32)
            acc_re = acc_re - first[k] * l_re + second[k] * l_im
            acc_im = acc_im - first[k] * l_im - second[k] * l_re
        part_re[comp] = acc_re
        part_im[comp] = acc_im
    rows = lax.broadcasted_iota(jnp.int32, (size, 1), 0)
    cols = lax.broadcasted_iota(jnp.int32, (1, size), 1)
    half = size // 2
    wave_y = jnp.where(rows < half, rows, rows - size).astype(f32) / (size / 2.0)
    wave_z = jnp.where(cols < half, cols, cols - size).astype(f32) / (size / 2.0)
    waves = (qx_ref[plane], wave_y, wave_z)
    c_hi = chi_ref[...]
    c_lo = clo_ref[...]
    s_hi = shi_ref[...]
    s_lo = slo_ref[...]
    for slot, comp in enumerate(comps):
        a = (comp + 1) % 3
        b = (comp + 2) % 3
        cur_re = -(waves[a] * part_im[b] - waves[b] * part_im[a])
        cur_im = waves[a] * part_re[b] - waves[b] * part_re[a]
        z_re = dot_right(cur_re, c_hi, c_lo) - dot_right(cur_im, s_hi, s_lo)
        z_im = dot_right(cur_re, s_hi, s_lo) + dot_right(cur_im, c_hi, c_lo)
        y_re = dot_left(c_hi, c_lo, z_re) - dot_left(s_hi, s_lo, z_im)
        y_im = dot_left(s_hi, s_lo, z_re) + dot_left(c_hi, c_lo, z_im)
        out_ref[0, 0, slot, 0] = y_re
        out_ref[1, 0, slot, 0] = y_im


def numpy_split(table):
    full = table.astype(np.float32)
    high = full.astype(ml_dtypes.bfloat16)
    low = (full - high.astype(np.float32)).astype(ml_dtypes.bfloat16)
    return jnp.asarray(high), jnp.asarray(low)


def dft_tables(length, orient):
    indices = np.arange(length, dtype=np.int64)
    phases = indices[:, None] * indices[None, :] % length
    angles = phases.astype(np.float64) * (2.0 * math.pi / length)
    norm_factor = 1.0 / math.sqrt(length)
    c_hi, c_lo = numpy_split(np.cos(angles) * norm_factor)
    s_hi, s_lo = numpy_split(np.sin(angles) * norm_factor * orient)
    return c_hi, c_lo, s_hi, s_lo


def front_pass(comps, coef_rows, wave_x, trial_bands, locked_bands):
    band_count, _, _, local_x, size, _ = trial_bands.shape
    kept = locked_bands.shape[0]
    tables = dft_tables(size, 1.0)
    smem = pl.BlockSpec(memory_space=pltpu.SMEM)
    table_spec = pl.BlockSpec((size, size), lambda b, x: (0, 0))
    width = len(comps)
    return pl.pallas_call(
        functools.partial(front_kernel, comps),
        grid=(band_count, local_x),
        in_specs=[
            smem,
            smem,
            pl.BlockSpec((1, 2, 3, 1, size, size), lambda b, x: (b, 0, 0, x, 0, 0)),
            pl.BlockSpec((kept, 2, 3, 1, size, size), lambda b, x: (0, 0, 0, x, 0, 0)),
            table_spec,
            table_spec,
            table_spec,
            table_spec,
        ],
        out_specs=pl.BlockSpec((2, 1, width, 1, size, size), lambda b, x: (0, b, 0, x, 0, 0)),
        out_shape=jax.ShapeDtypeStruct((2, band_count, width, local_x, size, size), jnp.float32),
    )(coef_rows, wave_x, trial_bands, locked_bands, *tables)


def radix_sum(values, axis, count):
    if count & (count - 1):
        return lax.psum(values, axis)
    me = lax.axis_index(axis)
    stride = 1
    while stride < count:
        radix = 4 if count // stride >= 4 else 2
        digit = (me // stride) % radix
        slots = [None] * radix
        for offset in range(radix):
            if offset == 0:
                got = values
            else:
                pairs = []
                for dst in range(count):
                    dst_digit = (dst // stride) % radix
                    base = dst - dst_digit * stride
                    pairs.append((base + ((dst_digit + offset) % radix) * stride, dst))
                got = lax.ppermute(values, axis, pairs)
            slots[offset] = got
        ordered = []
        for member in range(radix):
            pick = slots[0]
            for offset in range(1, radix):
                pick = jnp.where((digit + offset) % radix == member, slots[offset], pick)
            ordered.append(pick)
        total = ordered[0]
        for member in range(1, radix):
            total = total + ordered[member]
        values = total
        stride *= radix
    return values


def butterfly_sum(values, axis, count):
    if count & (count - 1):
        return lax.psum(values, axis)
    step = 1
    while step < count:
        pairs = [(index, index ^ step) for index in range(count)]
        values = values + lax.ppermute(values, axis, pairs)
        step *= 2
    return values


def inner_sum(left_rows, right_rows):
    return jnp.einsum("an,bn->ab", left_rows, right_rows, preferred_element_type=jnp.float32)


def remove_locked(gram_sums, trial_re, trial_im, locked_re, locked_im):
    gram_a, gram_q, proj_re, proj_im = gram_sums
    kept_count = gram_a.shape[0]
    gram = jnp.concatenate(
        [jnp.concatenate([gram_a, gram_q], axis=1), jnp.concatenate([gram_q.T, gram_a], axis=1)],
        axis=0,
    )
    rhs_both = jnp.concatenate([proj_re, proj_im], axis=0)
    lower = jnp.linalg.cholesky(gram)
    middle = lax.linalg.triangular_solve(lower, rhs_both, left_side=True, lower=True)
    coef = lax.linalg.triangular_solve(lower, middle, left_side=True, lower=True, transpose_a=True)
    coef_one = coef[:kept_count]
    coef_two = coef[kept_count:]
    locked_re32 = locked_re.astype(jnp.float32)
    locked_im32 = locked_im.astype(jnp.float32)
    out_re = (
        trial_re.astype(jnp.float32)
        - jnp.einsum("ab,an->bn", coef_one, locked_re32, precision=highest)
        + jnp.einsum("ab,an->bn", coef_two, locked_im32, precision=highest)
    )
    out_im = (
        trial_im.astype(jnp.float32)
        - jnp.einsum("ab,an->bn", coef_one, locked_im32, precision=highest)
        - jnp.einsum("ab,an->bn", coef_two, locked_re32, precision=highest)
    )
    return (out_re, out_im)


def solve_coef(gram_sums):
    gram_a, gram_q, proj_re, proj_im = gram_sums
    gram = jnp.concatenate(
        [jnp.concatenate([gram_a, gram_q], axis=1), jnp.concatenate([gram_q.T, gram_a], axis=1)],
        axis=0,
    )
    rhs_both = jnp.concatenate([proj_re, proj_im], axis=0)
    lower = jnp.linalg.cholesky(gram)
    middle = lax.linalg.triangular_solve(lower, rhs_both, left_side=True, lower=True)
    return lax.linalg.triangular_solve(lower, middle, left_side=True, lower=True, transpose_a=True)


def maxwell_pass(chunks, waves, inv_diag, inv_corr, to_space_fn, to_spectrum_fn):
    space = jnp.concatenate([transform(to_space_fn(chunk), 2, 1.0) for chunk in chunks], axis=2)
    weighted = apply_tensor(space, inv_diag, inv_corr)
    homes = []
    for comp in range(weighted.shape[2]):
        source = transform(weighted[:, :, comp : comp + 1], 2, -1.0)
        if comp >= 2:
            source, _ = lax.optimization_barrier((source, homes[comp - 2]))
        home = to_spectrum_fn(source)
        home = transform(home, 3, -1.0)
        homes.append(transform(home, 4, -1.0))
    home = jnp.concatenate(homes, axis=2)
    return (curl_times_i(waves, home), space, weighted)


def per_device(wide_count, trial_bands, locked_bands, inv_diag, inv_corr):
    band_count = trial_bands.shape[0]
    kept_count = locked_bands.shape[0]
    local_x = trial_bands.shape[3]
    grid_len = trial_bands.shape[4]
    rows = jnp.concatenate(
        [locked_bands.reshape((2 * kept_count,) + locked_bands.shape[2:]),
         trial_bands.reshape((2 * band_count,) + trial_bands.shape[2:])],
        axis=0,
    )
    pairs = jnp.einsum("icxyz,jcxyz->ij", rows, rows, preferred_element_type=jnp.float32)
    pairs = radix_sum(pairs, "wide", wide_count)
    lk = pairs[: 2 * kept_count, : 2 * kept_count].reshape(kept_count, 2, kept_count, 2)
    lt = pairs[: 2 * kept_count, 2 * kept_count :].reshape(kept_count, 2, band_count, 2)
    gram_a = lk[:, 0, :, 0] + lk[:, 1, :, 1]
    gram_q = lk[:, 1, :, 0] - lk[:, 0, :, 1]
    proj_re = lt[:, 0, :, 0] + lt[:, 1, :, 1]
    proj_im = lt[:, 0, :, 1] - lt[:, 1, :, 0]
    gram_sums = (gram_a, gram_q, proj_re, proj_im)
    coef = solve_coef(gram_sums)
    start_x = lax.axis_index("wide") * local_x
    full_axis = jnp.arange(grid_len, dtype=jnp.int32)
    wave_x = signed_wave(start_x + jnp.arange(local_x, dtype=jnp.int32), grid_len)
    wave_full = signed_wave(full_axis, grid_len)
    waves = (wave_x, wave_full, wave_full)

    def exchange_rows(field, split_dim, keep_dim):
        parts, bands, comps = field.shape[0], field.shape[1], field.shape[2]
        order = (split_dim, 1, 2, keep_dim, 0, 5)
        moved = jnp.transpose(field, order).reshape(wide_count, -1, 128)
        moved = lax.all_to_all(moved, "wide", split_axis=0, concat_axis=0, tiled=True)
        local_split = field.shape[split_dim] // wide_count
        moved = moved.reshape(
            wide_count, local_split, bands, comps, field.shape[keep_dim], parts, field.shape[5]
        )
        return moved

    def send_out_one(field):
        moved = exchange_rows(field, 4, 3)
        moved = jnp.transpose(moved, (5, 2, 3, 0, 4, 1, 6))
        shape = moved.shape
        return moved.reshape(shape[0], shape[1], shape[2], shape[3] * shape[4], shape[5], shape[6])

    def send_home_one(field):
        moved = exchange_rows(field, 3, 4)
        moved = jnp.transpose(moved, (5, 2, 3, 1, 0, 4, 6))
        shape = moved.shape
        return moved.reshape(shape[0], shape[1], shape[2], shape[3], shape[4] * shape[5], shape[6])

    chunks = [front_pass((comp,), coef.T, wave_x, trial_bands, locked_bands) for comp in range(3)]
    results = [maxwell_pass(chunks, waves, inv_diag, inv_corr, send_out_one, send_home_one)]
    applied_st, space, weighted = [
        jnp.concatenate([entry[slot] for entry in results], axis=1) for slot in range(3)
    ]
    applied = jnp.stack([applied_st[0], applied_st[1]], axis=1).astype(jnp.bfloat16)
    scale_all = 1.0 / float(grid_len * grid_len * grid_len)
    left_re = space[0].reshape(band_count, -1)
    left_im = space[1].reshape(band_count, -1)
    right_re = weighted[0].reshape(band_count, -1)
    right_im = weighted[1].reshape(band_count, -1)
    part_re = jnp.einsum("an,bn->ab", left_re, right_re, precision=highest) + jnp.einsum(
        "an,bn->ab", left_im, right_im, precision=highest
    )
    part_im = jnp.einsum("an,bn->ab", left_re, right_im, precision=highest) - jnp.einsum(
        "an,bn->ab", left_im, right_re, precision=highest
    )
    total_re, total_im = radix_sum(jnp.stack([part_re, part_im], axis=0), "wide", wide_count)
    rayleigh = jnp.stack([total_re * scale_all, total_im * scale_all], axis=0)
    return (applied, rayleigh)


def solution(mesh):
    in_specs = (
        P("groups", None, None, "wide", None, None),
        P("groups", None, None, "wide", None, None),
        P("groups", None, "wide", None),
        P("groups", None, "wide", None),
    )
    out_specs = (P("groups", None, None, "wide", None, None), P("groups", None, None))
    wide_count = mesh.shape["wide"]
    return jax.shard_map(
        functools.partial(per_device, wide_count), mesh=mesh, in_specs=in_specs, out_specs=out_specs, check_vma=False
    )
```

```python
import functools
import math

import ml_dtypes
import numpy as np

import jax
import jax.numpy as jnp
from jax import lax
from jax.sharding import PartitionSpec as P
from jax.experimental import pallas as pl
from jax.experimental.pallas import tpu as pltpu

highest = lax.Precision.HIGHEST
three_pass = lax.Precision.HIGH


def signed_wave(indices, length):
    shifted = jnp.where(indices < length // 2, indices, indices - length)
    return shifted.astype(jnp.float32) / (length / 2.0)


def cross_wave(wave_x, wave_y, wave_z, vectors):
    comp_x = vectors[..., 0, :, :, :]
    comp_y = vectors[..., 1, :, :, :]
    comp_z = vectors[..., 2, :, :, :]
    along_x = wave_x[:, None, None]
    along_y = wave_y[None, :, None]
    along_z = wave_z[None, None, :]
    return jnp.stack(
        [
            along_y * comp_z - along_z * comp_y,
            along_z * comp_x - along_x * comp_z,
            along_x * comp_y - along_y * comp_x,
        ],
        axis=-4,
    )


def curl_times_i(waves, stacked):
    wave_x, wave_y, wave_z = waves
    return jnp.stack(
        [
            -cross_wave(wave_x, wave_y, wave_z, stacked[1]),
            cross_wave(wave_x, wave_y, wave_z, stacked[0]),
        ],
        axis=0,
    )


def apply_tensor(vectors, inv_diag, inv_corr):
    coupling_xy = inv_corr[0] * jnp.sqrt(inv_diag[0] * inv_diag[1])
    coupling_xz = inv_corr[1] * jnp.sqrt(inv_diag[0] * inv_diag[2])
    coupling_yz = inv_corr[2] * jnp.sqrt(inv_diag[1] * inv_diag[2])
    comp_x = vectors[..., 0, :, :, :]
    comp_y = vectors[..., 1, :, :, :]
    comp_z = vectors[..., 2, :, :, :]
    out_x = inv_diag[0] * comp_x + coupling_xy * comp_y + coupling_xz * comp_z
    out_y = coupling_xy * comp_x + inv_diag[1] * comp_y + coupling_yz * comp_z
    out_z = coupling_xz * comp_x + coupling_yz * comp_y + inv_diag[2] * comp_z
    return jnp.stack([out_x, out_y, out_z], axis=-4)


def complex_table(length, orient, order=None):
    indices = jnp.arange(length, dtype=jnp.int32)
    sources = indices if order is None else jnp.asarray(order, dtype=jnp.int32)
    phases = sources[:, None] * indices[None, :] % length
    angles = phases.astype(jnp.float32) * (2.0 * math.pi / length)
    norm_factor = 1.0 / math.sqrt(length)
    cos_table = jnp.cos(angles) * norm_factor
    sin_table = jnp.sin(angles) * norm_factor * orient
    return jnp.stack(
        [jnp.stack([cos_table, sin_table], axis=0), jnp.stack([-sin_table, cos_table], axis=0)],
        axis=0,
    )


def transform(stacked, axis_dim, orient, order=None):
    table = complex_table(stacked.shape[axis_dim + 1], orient, order)
    if axis_dim == 2:
        return jnp.einsum("pbckyz,pqkn->qbcnyz", stacked, table, precision=three_pass)
    if axis_dim == 3:
        return jnp.einsum("pbcxkz,pqkn->qbcxnz", stacked, table, precision=three_pass)
    return jnp.einsum("pbcxyk,pqkn->qbcxyn", stacked, table, precision=three_pass)


def split_hi_lo(values):
    scaled = values * 65537.0
    top = scaled - (scaled - values)
    return top.astype(jnp.bfloat16), (values - top).astype(jnp.bfloat16)


def dot_right(values, table_hi, table_lo):
    high, low = split_hi_lo(values)
    f32 = jnp.float32
    return (
        jnp.dot(high, table_hi, preferred_element_type=f32)
        + jnp.dot(low, table_hi, preferred_element_type=f32)
        + jnp.dot(high, table_lo, preferred_element_type=f32)
    )


def dot_left(table_hi, table_lo, values):
    high, low = split_hi_lo(values)
    f32 = jnp.float32
    return (
        jnp.dot(table_hi, high, preferred_element_type=f32)
        + jnp.dot(table_hi, low, preferred_element_type=f32)
        + jnp.dot(table_lo, high, preferred_element_type=f32)
    )


def front_kernel(comps, coef_ref, qx_ref, trial_ref, locked_ref, chi_ref, clo_ref, shi_ref, slo_ref, out_ref):
    band = pl.program_id(0)
    plane = pl.program_id(1)
    kept = locked_ref.shape[0]
    size = trial_ref.shape[-1]
    f32 = jnp.float32
    first = [coef_ref[band, k] for k in range(kept)]
    second = [coef_ref[band, kept + k] for k in range(kept)]
    needed = sorted({(c + 1) % 3 for c in comps} | {(c + 2) % 3 for c in comps})
    part_re = {}
    part_im = {}
    for comp in needed:
        acc_re = trial_ref[0, 0, comp, 0].astype(f32)
        acc_im = trial_ref[0, 1, comp, 0].astype(f32)
        for k in range(kept):
            l_re = locked_ref[k, 0, comp, 0].astype(f32)
            l_im = locked_ref[k, 1, comp, 0].astype(f32)
            acc_re = acc_re - first[k] * l_re + second[k] * l_im
            acc_im = acc_im - first[k] * l_im - second[k] * l_re
        part_re[comp] = acc_re
        part_im[comp] = acc_im
    rows = lax.broadcasted_iota(jnp.int32, (size, 1), 0)
    cols = lax.broadcasted_iota(jnp.int32, (1, size), 1)
    half = size // 2
    wave_y = jnp.where(rows < half, rows, rows - size).astype(f32) / (size / 2.0)
    wave_z = jnp.where(cols < half, cols, cols - size).astype(f32) / (size / 2.0)
    waves = (qx_ref[plane], wave_y, wave_z)
    c_hi = chi_ref[...]
    c_lo = clo_ref[...]
    s_hi = shi_ref[...]
    s_lo = slo_ref[...]
    for slot, comp in enumerate(comps):
        a = (comp + 1) % 3
        b = (comp + 2) % 3
        cur_re = -(waves[a] * part_im[b] - waves[b] * part_im[a])
        cur_im = waves[a] * part_re[b] - waves[b] * part_re[a]
        z_re = dot_right(cur_re, c_hi, c_lo) - dot_right(cur_im, s_hi, s_lo)
        z_im = dot_right(cur_re, s_hi, s_lo) + dot_right(cur_im, c_hi, c_lo)
        y_re = dot_left(c_hi, c_lo, z_re) - dot_left(s_hi, s_lo, z_im)
        y_im = dot_left(s_hi, s_lo, z_re) + dot_left(c_hi, c_lo, z_im)
        out_ref[0, 0, slot, 0] = y_re
        out_ref[1, 0, slot, 0] = y_im


def numpy_split(table):
    full = table.astype(np.float32)
    high = full.astype(ml_dtypes.bfloat16)
    low = (full - high.astype(np.float32)).astype(ml_dtypes.bfloat16)
    return jnp.asarray(high), jnp.asarray(low)


def dft_tables(length, orient):
    indices = np.arange(length, dtype=np.int64)
    phases = indices[:, None] * indices[None, :] % length
    angles = phases.astype(np.float64) * (2.0 * math.pi / length)
    norm_factor = 1.0 / math.sqrt(length)
    c_hi, c_lo = numpy_split(np.cos(angles) * norm_factor)
    s_hi, s_lo = numpy_split(np.sin(angles) * norm_factor * orient)
    return c_hi, c_lo, s_hi, s_lo


def front_pass(comps, coef_rows, wave_x, trial_bands, locked_bands, start, count):
    band_count, _, _, _, size, _ = trial_bands.shape
    kept = locked_bands.shape[0]
    tables = dft_tables(size, 1.0)
    smem = pl.BlockSpec(memory_space=pltpu.SMEM)
    table_spec = pl.BlockSpec((size, size), lambda b, x: (0, 0))
    width = len(comps)
    return pl.pallas_call(
        functools.partial(front_kernel, comps),
        grid=(band_count, count),
        in_specs=[
            smem,
            smem,
            pl.BlockSpec((1, 2, 3, 1, size, size), lambda b, x: (b, 0, 0, x + start, 0, 0)),
            pl.BlockSpec((kept, 2, 3, 1, size, size), lambda b, x: (0, 0, 0, x + start, 0, 0)),
            table_spec,
            table_spec,
            table_spec,
            table_spec,
        ],
        out_specs=pl.BlockSpec((2, 1, width, 1, size, size), lambda b, x: (0, b, 0, x, 0, 0)),
        out_shape=jax.ShapeDtypeStruct((2, band_count, width, count, size, size), jnp.float32),
    )(coef_rows, wave_x[start : start + count], trial_bands, locked_bands, *tables)


def radix_sum(values, axis, count):
    if count & (count - 1):
        return lax.psum(values, axis)
    me = lax.axis_index(axis)
    stride = 1
    while stride < count:
        radix = 4 if count // stride >= 4 else 2
        digit = (me // stride) % radix
        slots = [None] * radix
        for offset in range(radix):
            if offset == 0:
                got = values
            else:
                pairs = []
                for dst in range(count):
                    dst_digit = (dst // stride) % radix
                    base = dst - dst_digit * stride
                    pairs.append((base + ((dst_digit + offset) % radix) * stride, dst))
                got = lax.ppermute(values, axis, pairs)
            slots[offset] = got
        ordered = []
        for member in range(radix):
            pick = slots[0]
            for offset in range(1, radix):
                pick = jnp.where((digit + offset) % radix == member, slots[offset], pick)
            ordered.append(pick)
        total = ordered[0]
        for member in range(1, radix):
            total = total + ordered[member]
        values = total
        stride *= radix
    return values


def butterfly_sum(values, axis, count):
    if count & (count - 1):
        return lax.psum(values, axis)
    step = 1
    while step < count:
        pairs = [(index, index ^ step) for index in range(count)]
        values = values + lax.ppermute(values, axis, pairs)
        step *= 2
    return values


def inner_sum(left_rows, right_rows):
    return jnp.einsum("an,bn->ab", left_rows, right_rows, preferred_element_type=jnp.float32)


def remove_locked(gram_sums, trial_re, trial_im, locked_re, locked_im):
    gram_a, gram_q, proj_re, proj_im = gram_sums
    kept_count = gram_a.shape[0]
    gram = jnp.concatenate(
        [jnp.concatenate([gram_a, gram_q], axis=1), jnp.concatenate([gram_q.T, gram_a], axis=1)],
        axis=0,
    )
    rhs_both = jnp.concatenate([proj_re, proj_im], axis=0)
    lower = jnp.linalg.cholesky(gram)
    middle = lax.linalg.triangular_solve(lower, rhs_both, left_side=True, lower=True)
    coef = lax.linalg.triangular_solve(lower, middle, left_side=True, lower=True, transpose_a=True)
    coef_one = coef[:kept_count]
    coef_two = coef[kept_count:]
    locked_re32 = locked_re.astype(jnp.float32)
    locked_im32 = locked_im.astype(jnp.float32)
    out_re = (
        trial_re.astype(jnp.float32)
        - jnp.einsum("ab,an->bn", coef_one, locked_re32, precision=highest)
        + jnp.einsum("ab,an->bn", coef_two, locked_im32, precision=highest)
    )
    out_im = (
        trial_im.astype(jnp.float32)
        - jnp.einsum("ab,an->bn", coef_one, locked_im32, precision=highest)
        - jnp.einsum("ab,an->bn", coef_two, locked_re32, precision=highest)
    )
    return (out_re, out_im)


def solve_coef(gram_sums):
    gram_a, gram_q, proj_re, proj_im = gram_sums
    gram = jnp.concatenate(
        [jnp.concatenate([gram_a, gram_q], axis=1), jnp.concatenate([gram_q.T, gram_a], axis=1)],
        axis=0,
    )
    rhs_both = jnp.concatenate([proj_re, proj_im], axis=0)
    lower = jnp.linalg.cholesky(gram)
    middle = lax.linalg.triangular_solve(lower, rhs_both, left_side=True, lower=True)
    return lax.linalg.triangular_solve(lower, middle, left_side=True, lower=True, transpose_a=True)


def maxwell_pass(chunks, order, waves, inv_diag, inv_corr, to_space_fn, to_spectrum_fn):
    moved = jnp.concatenate([to_space_fn(chunk) for chunk in chunks], axis=3)
    space = transform(moved, 2, 1.0, order)
    weighted = apply_tensor(space, inv_diag, inv_corr)
    homes = []
    for comp in range(weighted.shape[2]):
        source = transform(weighted[:, :, comp : comp + 1], 2, -1.0)
        if comp >= 2:
            source, _ = lax.optimization_barrier((source, homes[comp - 2]))
        home = to_spectrum_fn(source)
        home = transform(home, 3, -1.0)
        homes.append(transform(home, 4, -1.0))
    home = jnp.concatenate(homes, axis=2)
    return (curl_times_i(waves, home), space, weighted)


def per_device(wide_count, trial_bands, locked_bands, inv_diag, inv_corr):
    band_count = trial_bands.shape[0]
    kept_count = locked_bands.shape[0]
    local_x = trial_bands.shape[3]
    grid_len = trial_bands.shape[4]
    rows = jnp.concatenate(
        [locked_bands.reshape((2 * kept_count,) + locked_bands.shape[2:]),
         trial_bands.reshape((2 * band_count,) + trial_bands.shape[2:])],
        axis=0,
    )
    pairs = jnp.einsum("icxyz,jcxyz->ij", rows, rows, preferred_element_type=jnp.float32)
    pairs = radix_sum(pairs, "wide", wide_count)
    lk = pairs[: 2 * kept_count, : 2 * kept_count].reshape(kept_count, 2, kept_count, 2)
    lt = pairs[: 2 * kept_count, 2 * kept_count :].reshape(kept_count, 2, band_count, 2)
    gram_a = lk[:, 0, :, 0] + lk[:, 1, :, 1]
    gram_q = lk[:, 1, :, 0] - lk[:, 0, :, 1]
    proj_re = lt[:, 0, :, 0] + lt[:, 1, :, 1]
    proj_im = lt[:, 0, :, 1] - lt[:, 1, :, 0]
    gram_sums = (gram_a, gram_q, proj_re, proj_im)
    coef = solve_coef(gram_sums)
    start_x = lax.axis_index("wide") * local_x
    full_axis = jnp.arange(grid_len, dtype=jnp.int32)
    wave_x = signed_wave(start_x + jnp.arange(local_x, dtype=jnp.int32), grid_len)
    wave_full = signed_wave(full_axis, grid_len)
    waves = (wave_x, wave_full, wave_full)

    def exchange_rows(field, split_dim, keep_dim):
        parts, bands, comps = field.shape[0], field.shape[1], field.shape[2]
        order = (split_dim, 1, 2, keep_dim, 0, 5)
        moved = jnp.transpose(field, order).reshape(wide_count, -1, 128)
        moved = lax.all_to_all(moved, "wide", split_axis=0, concat_axis=0, tiled=True)
        local_split = field.shape[split_dim] // wide_count
        moved = moved.reshape(
            wide_count, local_split, bands, comps, field.shape[keep_dim], parts, field.shape[5]
        )
        return moved

    def send_out_one(field):
        moved = exchange_rows(field, 4, 3)
        moved = jnp.transpose(moved, (5, 2, 3, 0, 4, 1, 6))
        shape = moved.shape
        return moved.reshape(shape[0], shape[1], shape[2], shape[3] * shape[4], shape[5], shape[6])

    def send_home_one(field):
        moved = exchange_rows(field, 3, 4)
        moved = jnp.transpose(moved, (5, 2, 3, 1, 0, 4, 6))
        shape = moved.shape
        return moved.reshape(shape[0], shape[1], shape[2], shape[3], shape[4] * shape[5], shape[6])

    first = (local_x + 1) // 2
    spans = [(0, first), (first, local_x - first)] if local_x > 1 else [(0, local_x)]
    chunks = [
        front_pass((0, 1, 2), coef.T, wave_x, trial_bands, locked_bands, start, count)
        for start, count in spans
    ]
    order = np.concatenate(
        [
            (np.arange(wide_count)[:, None] * local_x + start + np.arange(count)[None, :]).reshape(-1)
            for start, count in spans
        ]
    )
    results = [maxwell_pass(chunks, order, waves, inv_diag, inv_corr, send_out_one, send_home_one)]
    applied_st, space, weighted = [
        jnp.concatenate([entry[slot] for entry in results], axis=1) for slot in range(3)
    ]
    applied = jnp.stack([applied_st[0], applied_st[1]], axis=1).astype(jnp.bfloat16)
    scale_all = 1.0 / float(grid_len * grid_len * grid_len)
    left_re = space[0].reshape(band_count, -1)
    left_im = space[1].reshape(band_count, -1)
    right_re = weighted[0].reshape(band_count, -1)
    right_im = weighted[1].reshape(band_count, -1)
    part_re = jnp.einsum("an,bn->ab", left_re, right_re, precision=highest) + jnp.einsum(
        "an,bn->ab", left_im, right_im, precision=highest
    )
    part_im = jnp.einsum("an,bn->ab", left_re, right_im, precision=highest) - jnp.einsum(
        "an,bn->ab", left_im, right_re, precision=highest
    )
    total_re, total_im = radix_sum(jnp.stack([part_re, part_im], axis=0), "wide", wide_count)
    rayleigh = jnp.stack([total_re * scale_all, total_im * scale_all], axis=0)
    return (applied, rayleigh)


def solution(mesh):
    in_specs = (
        P("groups", None, None, "wide", None, None),
        P("groups", None, None, "wide", None, None),
        P("groups", None, "wide", None),
        P("groups", None, "wide", None),
    )
    out_specs = (P("groups", None, None, "wide", None, None), P("groups", None, None))
    wide_count = mesh.shape["wide"]
    return jax.shard_map(
        functools.partial(per_device, wide_count), mesh=mesh, in_specs=in_specs, out_specs=out_specs, check_vma=False
    )
```

```python
import functools
import math

import ml_dtypes
import numpy as np

import jax
import jax.numpy as jnp
from jax import lax
from jax.sharding import PartitionSpec as P
from jax.experimental import pallas as pl
from jax.experimental.pallas import tpu as pltpu

highest = lax.Precision.HIGHEST
three_pass = lax.Precision.HIGH


def signed_wave(indices, length):
    shifted = jnp.where(indices < length // 2, indices, indices - length)
    return shifted.astype(jnp.float32) / (length / 2.0)


def cross_wave(wave_x, wave_y, wave_z, vectors):
    comp_x = vectors[..., 0, :, :, :]
    comp_y = vectors[..., 1, :, :, :]
    comp_z = vectors[..., 2, :, :, :]
    along_x = wave_x[:, None, None]
    along_y = wave_y[None, :, None]
    along_z = wave_z[None, None, :]
    return jnp.stack(
        [
            along_y * comp_z - along_z * comp_y,
            along_z * comp_x - along_x * comp_z,
            along_x * comp_y - along_y * comp_x,
        ],
        axis=-4,
    )


def curl_times_i(waves, stacked):
    wave_x, wave_y, wave_z = waves
    return jnp.stack(
        [
            -cross_wave(wave_x, wave_y, wave_z, stacked[1]),
            cross_wave(wave_x, wave_y, wave_z, stacked[0]),
        ],
        axis=0,
    )


def apply_tensor(vectors, inv_diag, inv_corr):
    coupling_xy = inv_corr[0] * jnp.sqrt(inv_diag[0] * inv_diag[1])
    coupling_xz = inv_corr[1] * jnp.sqrt(inv_diag[0] * inv_diag[2])
    coupling_yz = inv_corr[2] * jnp.sqrt(inv_diag[1] * inv_diag[2])
    comp_x = vectors[..., 0, :, :, :]
    comp_y = vectors[..., 1, :, :, :]
    comp_z = vectors[..., 2, :, :, :]
    out_x = inv_diag[0] * comp_x + coupling_xy * comp_y + coupling_xz * comp_z
    out_y = coupling_xy * comp_x + inv_diag[1] * comp_y + coupling_yz * comp_z
    out_z = coupling_xz * comp_x + coupling_yz * comp_y + inv_diag[2] * comp_z
    return jnp.stack([out_x, out_y, out_z], axis=-4)


def complex_table(length, orient):
    indices = jnp.arange(length, dtype=jnp.int32)
    phases = indices[:, None] * indices[None, :] % length
    angles = phases.astype(jnp.float32) * (2.0 * math.pi / length)
    norm_factor = 1.0 / math.sqrt(length)
    cos_table = jnp.cos(angles) * norm_factor
    sin_table = jnp.sin(angles) * norm_factor * orient
    return jnp.stack(
        [jnp.stack([cos_table, sin_table], axis=0), jnp.stack([-sin_table, cos_table], axis=0)],
        axis=0,
    )


def transform(stacked, axis_dim, orient):
    table = complex_table(stacked.shape[axis_dim + 1], orient)
    if axis_dim == 2:
        return jnp.einsum("pbckyz,pqkn->qbcnyz", stacked, table, precision=three_pass)
    if axis_dim == 3:
        return jnp.einsum("pbcxkz,pqkn->qbcxnz", stacked, table, precision=three_pass)
    return jnp.einsum("pbcxyk,pqkn->qbcxyn", stacked, table, precision=three_pass)


def split_hi_lo(values):
    scaled = values * 65537.0
    top = scaled - (scaled - values)
    return top.astype(jnp.bfloat16), (values - top).astype(jnp.bfloat16)


def dot_right(values, table_hi, table_lo):
    high, low = split_hi_lo(values)
    f32 = jnp.float32
    return (
        jnp.dot(high, table_hi, preferred_element_type=f32)
        + jnp.dot(low, table_hi, preferred_element_type=f32)
        + jnp.dot(high, table_lo, preferred_element_type=f32)
    )


def dot_left(table_hi, table_lo, values):
    high, low = split_hi_lo(values)
    f32 = jnp.float32
    return (
        jnp.dot(table_hi, high, preferred_element_type=f32)
        + jnp.dot(table_hi, low, preferred_element_type=f32)
        + jnp.dot(table_lo, high, preferred_element_type=f32)
    )


def front_kernel(comps, coef_ref, qx_ref, trial_ref, locked_ref, chi_ref, clo_ref, shi_ref, slo_ref, out_ref):
    band = pl.program_id(0)
    plane = pl.program_id(1)
    kept = locked_ref.shape[0]
    size = trial_ref.shape[-1]
    f32 = jnp.float32
    first = [coef_ref[band, k] for k in range(kept)]
    second = [coef_ref[band, kept + k] for k in range(kept)]
    needed = sorted({(c + 1) % 3 for c in comps} | {(c + 2) % 3 for c in comps})
    part_re = {}
    part_im = {}
    for comp in needed:
        acc_re = trial_ref[0, 0, comp, 0].astype(f32)
        acc_im = trial_ref[0, 1, comp, 0].astype(f32)
        for k in range(kept):
            l_re = locked_ref[k, 0, comp, 0].astype(f32)
            l_im = locked_ref[k, 1, comp, 0].astype(f32)
            acc_re = acc_re - first[k] * l_re + second[k] * l_im
            acc_im = acc_im - first[k] * l_im - second[k] * l_re
        part_re[comp] = acc_re
        part_im[comp] = acc_im
    rows = lax.broadcasted_iota(jnp.int32, (size, 1), 0)
    cols = lax.broadcasted_iota(jnp.int32, (1, size), 1)
    half = size // 2
    wave_y = jnp.where(rows < half, rows, rows - size).astype(f32) / (size / 2.0)
    wave_z = jnp.where(cols < half, cols, cols - size).astype(f32) / (size / 2.0)
    waves = (qx_ref[plane], wave_y, wave_z)
    c_hi = chi_ref[...]
    c_lo = clo_ref[...]
    s_hi = shi_ref[...]
    s_lo = slo_ref[...]
    for slot, comp in enumerate(comps):
        a = (comp + 1) % 3
        b = (comp + 2) % 3
        cur_re = -(waves[a] * part_im[b] - waves[b] * part_im[a])
        cur_im = waves[a] * part_re[b] - waves[b] * part_re[a]
        z_re = dot_right(cur_re, c_hi, c_lo) - dot_right(cur_im, s_hi, s_lo)
        z_im = dot_right(cur_re, s_hi, s_lo) + dot_right(cur_im, c_hi, c_lo)
        y_re = dot_left(c_hi, c_lo, z_re) - dot_left(s_hi, s_lo, z_im)
        y_im = dot_left(s_hi, s_lo, z_re) + dot_left(c_hi, c_lo, z_im)
        out_ref[0, 0, slot, 0] = y_re
        out_ref[1, 0, slot, 0] = y_im


def numpy_split(table):
    full = table.astype(np.float32)
    high = full.astype(ml_dtypes.bfloat16)
    low = (full - high.astype(np.float32)).astype(ml_dtypes.bfloat16)
    return jnp.asarray(high), jnp.asarray(low)


def dft_tables(length, orient):
    indices = np.arange(length, dtype=np.int64)
    phases = indices[:, None] * indices[None, :] % length
    angles = phases.astype(np.float64) * (2.0 * math.pi / length)
    norm_factor = 1.0 / math.sqrt(length)
    c_hi, c_lo = numpy_split(np.cos(angles) * norm_factor)
    s_hi, s_lo = numpy_split(np.sin(angles) * norm_factor * orient)
    return c_hi, c_lo, s_hi, s_lo


def front_pass(comps, coef_rows, wave_x, trial_bands, locked_bands):
    band_count, _, _, local_x, size, _ = trial_bands.shape
    kept = locked_bands.shape[0]
    tables = dft_tables(size, 1.0)
    smem = pl.BlockSpec(memory_space=pltpu.SMEM)
    table_spec = pl.BlockSpec((size, size), lambda b, x: (0, 0))
    width = len(comps)
    return pl.pallas_call(
        functools.partial(front_kernel, comps),
        grid=(band_count, local_x),
        in_specs=[
            smem,
            smem,
            pl.BlockSpec((1, 2, 3, 1, size, size), lambda b, x: (b, 0, 0, x, 0, 0)),
            pl.BlockSpec((kept, 2, 3, 1, size, size), lambda b, x: (0, 0, 0, x, 0, 0)),
            table_spec,
            table_spec,
            table_spec,
            table_spec,
        ],
        out_specs=pl.BlockSpec((2, 1, width, 1, size, size), lambda b, x: (0, b, 0, x, 0, 0)),
        out_shape=jax.ShapeDtypeStruct((2, band_count, width, local_x, size, size), jnp.float32),
    )(coef_rows, wave_x, trial_bands, locked_bands, *tables)


def radix_sum(values, axis, count):
    if count & (count - 1):
        return lax.psum(values, axis)
    me = lax.axis_index(axis)
    stride = 1
    while stride < count:
        radix = min(8, count // stride)
        digit = (me // stride) % radix
        slots = [None] * radix
        for offset in range(radix):
            if offset == 0:
                got = values
            else:
                pairs = []
                for dst in range(count):
                    dst_digit = (dst // stride) % radix
                    base = dst - dst_digit * stride
                    pairs.append((base + ((dst_digit + offset) % radix) * stride, dst))
                got = lax.ppermute(values, axis, pairs)
            slots[offset] = got
        ordered = []
        for member in range(radix):
            pick = slots[0]
            for offset in range(1, radix):
                pick = jnp.where((digit + offset) % radix == member, slots[offset], pick)
            ordered.append(pick)
        total = ordered[0]
        for member in range(1, radix):
            total = total + ordered[member]
        values = total
        stride *= radix
    return values


def butterfly_sum(values, axis, count):
    if count & (count - 1):
        return lax.psum(values, axis)
    step = 1
    while step < count:
        pairs = [(index, index ^ step) for index in range(count)]
        values = values + lax.ppermute(values, axis, pairs)
        step *= 2
    return values


def inner_sum(left_rows, right_rows):
    return jnp.einsum("an,bn->ab", left_rows, right_rows, preferred_element_type=jnp.float32)


def remove_locked(gram_sums, trial_re, trial_im, locked_re, locked_im):
    gram_a, gram_q, proj_re, proj_im = gram_sums
    kept_count = gram_a.shape[0]
    gram = jnp.concatenate(
        [jnp.concatenate([gram_a, gram_q], axis=1), jnp.concatenate([gram_q.T, gram_a], axis=1)],
        axis=0,
    )
    rhs_both = jnp.concatenate([proj_re, proj_im], axis=0)
    lower = jnp.linalg.cholesky(gram)
    middle = lax.linalg.triangular_solve(lower, rhs_both, left_side=True, lower=True)
    coef = lax.linalg.triangular_solve(lower, middle, left_side=True, lower=True, transpose_a=True)
    coef_one = coef[:kept_count]
    coef_two = coef[kept_count:]
    locked_re32 = locked_re.astype(jnp.float32)
    locked_im32 = locked_im.astype(jnp.float32)
    out_re = (
        trial_re.astype(jnp.float32)
        - jnp.einsum("ab,an->bn", coef_one, locked_re32, precision=highest)
        + jnp.einsum("ab,an->bn", coef_two, locked_im32, precision=highest)
    )
    out_im = (
        trial_im.astype(jnp.float32)
        - jnp.einsum("ab,an->bn", coef_one, locked_im32, precision=highest)
        - jnp.einsum("ab,an->bn", coef_two, locked_re32, precision=highest)
    )
    return (out_re, out_im)


def solve_coef(gram_sums):
    gram_a, gram_q, proj_re, proj_im = gram_sums
    gram = jnp.concatenate(
        [jnp.concatenate([gram_a, gram_q], axis=1), jnp.concatenate([gram_q.T, gram_a], axis=1)],
        axis=0,
    )
    rhs_both = jnp.concatenate([proj_re, proj_im], axis=0)
    lower = jnp.linalg.cholesky(gram)
    middle = lax.linalg.triangular_solve(lower, rhs_both, left_side=True, lower=True)
    return lax.linalg.triangular_solve(lower, middle, left_side=True, lower=True, transpose_a=True)


def maxwell_pass(chunks, waves, inv_diag, inv_corr, to_space_fn, to_spectrum_fn):
    space = jnp.concatenate([transform(to_space_fn(chunk), 2, 1.0) for chunk in chunks], axis=2)
    weighted = apply_tensor(space, inv_diag, inv_corr)
    homes = []
    for comp in range(weighted.shape[2]):
        source = transform(weighted[:, :, comp : comp + 1], 2, -1.0)
        if comp >= 2:
            source, _ = lax.optimization_barrier((source, homes[comp - 2]))
        home = to_spectrum_fn(source)
        home = transform(home, 3, -1.0)
        homes.append(transform(home, 4, -1.0))
    home = jnp.concatenate(homes, axis=2)
    return (curl_times_i(waves, home), space, weighted)


def per_device(wide_count, trial_bands, locked_bands, inv_diag, inv_corr):
    band_count = trial_bands.shape[0]
    kept_count = locked_bands.shape[0]
    local_x = trial_bands.shape[3]
    grid_len = trial_bands.shape[4]
    rows = jnp.concatenate(
        [locked_bands.reshape((2 * kept_count,) + locked_bands.shape[2:]),
         trial_bands.reshape((2 * band_count,) + trial_bands.shape[2:])],
        axis=0,
    )
    pairs = jnp.einsum("icxyz,jcxyz->ij", rows, rows, preferred_element_type=jnp.float32)
    pairs = radix_sum(pairs, "wide", wide_count)
    lk = pairs[: 2 * kept_count, : 2 * kept_count].reshape(kept_count, 2, kept_count, 2)
    lt = pairs[: 2 * kept_count, 2 * kept_count :].reshape(kept_count, 2, band_count, 2)
    gram_a = lk[:, 0, :, 0] + lk[:, 1, :, 1]
    gram_q = lk[:, 1, :, 0] - lk[:, 0, :, 1]
    proj_re = lt[:, 0, :, 0] + lt[:, 1, :, 1]
    proj_im = lt[:, 0, :, 1] - lt[:, 1, :, 0]
    gram_sums = (gram_a, gram_q, proj_re, proj_im)
    coef = solve_coef(gram_sums)
    start_x = lax.axis_index("wide") * local_x
    full_axis = jnp.arange(grid_len, dtype=jnp.int32)
    wave_x = signed_wave(start_x + jnp.arange(local_x, dtype=jnp.int32), grid_len)
    wave_full = signed_wave(full_axis, grid_len)
    waves = (wave_x, wave_full, wave_full)

    def exchange_rows(field, split_dim, keep_dim):
        parts, bands, comps = field.shape[0], field.shape[1], field.shape[2]
        order = (split_dim, 1, 2, keep_dim, 0, 5)
        moved = jnp.transpose(field, order).reshape(wide_count, -1, 128)
        moved = lax.all_to_all(moved, "wide", split_axis=0, concat_axis=0, tiled=True)
        local_split = field.shape[split_dim] // wide_count
        moved = moved.reshape(
            wide_count, local_split, bands, comps, field.shape[keep_dim], parts, field.shape[5]
        )
        return moved

    def send_out_one(field):
        moved = exchange_rows(field, 4, 3)
        moved = jnp.transpose(moved, (5, 2, 3, 0, 4, 1, 6))
        shape = moved.shape
        return moved.reshape(shape[0], shape[1], shape[2], shape[3] * shape[4], shape[5], shape[6])

    def send_home_one(field):
        moved = exchange_rows(field, 3, 4)
        moved = jnp.transpose(moved, (5, 2, 3, 1, 0, 4, 6))
        shape = moved.shape
        return moved.reshape(shape[0], shape[1], shape[2], shape[3], shape[4] * shape[5], shape[6])

    chunks = [front_pass((comp,), coef.T, wave_x, trial_bands, locked_bands) for comp in range(3)]
    results = [maxwell_pass(chunks, waves, inv_diag, inv_corr, send_out_one, send_home_one)]
    applied_st, space, weighted = [
        jnp.concatenate([entry[slot] for entry in results], axis=1) for slot in range(3)
    ]
    applied = jnp.stack([applied_st[0], applied_st[1]], axis=1).astype(jnp.bfloat16)
    scale_all = 1.0 / float(grid_len * grid_len * grid_len)
    left_re = space[0].reshape(band_count, -1)
    left_im = space[1].reshape(band_count, -1)
    right_re = weighted[0].reshape(band_count, -1)
    right_im = weighted[1].reshape(band_count, -1)
    part_re = jnp.einsum("an,bn->ab", left_re, right_re, precision=highest) + jnp.einsum(
        "an,bn->ab", left_im, right_im, precision=highest
    )
    part_im = jnp.einsum("an,bn->ab", left_re, right_im, precision=highest) - jnp.einsum(
        "an,bn->ab", left_im, right_re, precision=highest
    )
    total_re, total_im = radix_sum(jnp.stack([part_re, part_im], axis=0), "wide", wide_count)
    rayleigh = jnp.stack([total_re * scale_all, total_im * scale_all], axis=0)
    return (applied, rayleigh)


def solution(mesh):
    in_specs = (
        P("groups", None, None, "wide", None, None),
        P("groups", None, None, "wide", None, None),
        P("groups", None, "wide", None),
        P("groups", None, "wide", None),
    )
    out_specs = (P("groups", None, None, "wide", None, None), P("groups", None, None))
    wide_count = mesh.shape["wide"]
    return jax.shard_map(
        functools.partial(per_device, wide_count), mesh=mesh, in_specs=in_specs, out_specs=out_specs, check_vma=False
    )
```
